256 devices in a mesh: seq: 32 (over x, z), exp: 8 (over y, core).
Axes of the slice: x: 4, y: 4, z: 8, core: 2. Of those that a mesh axis runs over, the one named last changes fastest.
Arguments:
- queries: bfloat16 [32768, 4096], P(('seq', 'exp')), may hold values from -1.75 to 1.75
- keys: bfloat16 [32768, 4096], P(('seq', 'exp')), may hold values from -1.75 to 1.75
- values: bfloat16 [32768, 4096], P(('seq', 'exp')), may hold values from -6 to 6
- out_grad: bfloat16 [32768, 4096], P(('seq', 'exp')), may hold values from -0.0625 to 0.0625
- log_decay: bfloat16 [32768, 32], P(('seq', 'exp')), may hold values from -0.7 to 0
Outputs:
- query_grad: bfloat16 [32768, 4096], P(('seq', 'exp'))
- key_grad: bfloat16 [32768, 4096], P(('seq', 'exp'))
- value_grad: bfloat16 [32768, 4096], P(('seq', 'exp'))
The draws below stay inside these ranges and needn't reach their ends.
All inputs are finite; a program needn't handle non-finite values.
Results may differ from the reference program's by a relative error of at most 0.0095.
Values may be sent and summed in bfloat16 or wider, within the bound.
No kernel may reach another device: no remote copies, remote signals or barrier semaphores. Data moves between devices by JAX's collectives and lax.ppermute only.
A program may use at most 64 MiB of HBM per device.

```python
import math
import jax
import jax.numpy as jnp
from jax import lax

ATTENTION_HEADS = 32
HEAD_DIM = 128
BLOCK = 128
TOK_DEV = 128
SEQUENCE_LENGTH = 32768


def draw_log_decay(key, part):
    full_keys = jax.random.split(key, 7)
    fast_share = 0.5
    fast = jax.random.uniform(full_keys[0], (ATTENTION_HEADS,)) < fast_share
    slow_rate = jnp.exp(jax.random.uniform(full_keys[1], (ATTENTION_HEADS,), jnp.float32, math.log(0.2 / SEQUENCE_LENGTH), math.log(1.0 / SEQUENCE_LENGTH)))
    fast_rate = jnp.exp(jax.random.uniform(full_keys[2], (ATTENTION_HEADS,), jnp.float32, math.log(0.02), math.log(0.05)))
    decay_rate = jnp.where(fast, fast_rate, slow_rate)
    segment_range = jnp.exp(jax.random.uniform(full_keys[3], (SEQUENCE_LENGTH // TOK_DEV, ATTENTION_HEADS), jnp.float32, math.log(0.5), math.log(2.0)))
    segment_range = jnp.repeat(segment_range, TOK_DEV, axis=0)
    coarse_estimate = jax.random.uniform(full_keys[4], (SEQUENCE_LENGTH, ATTENTION_HEADS), jnp.float32, 0.5, 1.5)
    spike_flags = jax.random.randint(full_keys[5], (SEQUENCE_LENGTH, 1), 0, max(SEQUENCE_LENGTH // 2, 1)) == 0
    spike_value = jax.random.uniform(full_keys[6], (SEQUENCE_LENGTH, ATTENTION_HEADS), jnp.float32, math.log(0.5), math.log(0.8))
    return jnp.where(spike_flags, spike_value, -decay_rate[None, :] * segment_range * coarse_estimate).astype(jnp.bfloat16)


def levels(rng, dims, cuts, smallest, top_value):
    def one(axis_at, blocks):
        steps = jax.random.uniform(jax.random.fold_in(jax.random.fold_in(rng, 6), axis_at), (blocks,), jnp.float32, smallest / len(cuts), top_value / len(cuts))
        return jnp.repeat(jnp.exp(steps), dims[axis_at] // blocks).reshape((-1,) + (1,) * (len(dims) - axis_at - 1))

    loudness = one(*cuts[0])
    for cut in cuts[1:]:
        loudness = loudness * one(*cut)
    return loudness


def bell_draw(key, shape, scale, bound, cuts=(), kind=jnp.bfloat16):
    factor_of = levels(key, shape, cuts, -0.22, 0.18) if cuts else 1.0
    drawn = jax.random.normal(key, shape, jnp.float32) * scale * factor_of
    return jnp.minimum(jnp.maximum(drawn, -bound), bound).astype(kind)


def setup_inputs(seed: int = 0) -> dict:
    key_list = jax.random.split(jax.random.key(seed), 6)
    queries = bell_draw(key_list[0], (SEQUENCE_LENGTH, ATTENTION_HEADS * HEAD_DIM), 0.3, 1.75, ((0, 256),))
    keys = bell_draw(key_list[1], (SEQUENCE_LENGTH, ATTENTION_HEADS * HEAD_DIM), 0.3, 1.75, ((0, 256),))
    values = bell_draw(key_list[2], (SEQUENCE_LENGTH, ATTENTION_HEADS * HEAD_DIM), 1.0, 6.0, ((0, 256),))
    out_grad = bell_draw(key_list[3], (SEQUENCE_LENGTH, ATTENTION_HEADS * HEAD_DIM), (2.0 / SEQUENCE_LENGTH ** 0.5), 0.0625, ((0, 256),))
    log_decay = draw_log_decay(jax.random.fold_in(key_list[5], 71), 0)
    return {"queries": queries, "keys": keys, "values": values, "out_grad": out_grad, "log_decay": log_decay}


highest = lax.Precision.HIGHEST


def widen(array):
    return array.astype(jnp.float32)


def block_weights(cumul):
    heads_first = cumul.T
    spread = heads_first[:, :, None] - heads_first[:, None, :]
    length = cumul.shape[0]
    causal = lax.broadcasted_iota(jnp.int32, (length, length), 1) <= lax.broadcasted_iota(jnp.int32, (length, length), 0)
    return jnp.where(causal[None], jnp.exp(jnp.where(causal[None], spread, 0.0)), 0.0)


def inner_query(query_blk, key_blk, value_blk, grad_blk, cumul):
    weights = block_weights(cumul)
    grad_scores = jnp.einsum('thd,shd->hts', widen(grad_blk), widen(value_blk), precision=highest)
    first = (weights * grad_scores).astype(jnp.bfloat16)
    return jnp.einsum('hts,shd->thd', widen(first), widen(key_blk), precision=highest)


def inner_keys(query_blk, key_blk, value_blk, grad_blk, cumul):
    weights = block_weights(cumul)
    grad_scores = jnp.einsum('thd,shd->hts', widen(grad_blk), widen(value_blk), precision=highest)
    key_scores = jnp.einsum('thd,shd->hts', widen(query_blk), widen(key_blk), precision=highest)
    first = (weights * grad_scores).astype(jnp.bfloat16)
    second = (weights * key_scores).astype(jnp.bfloat16)
    key_part = jnp.einsum('hts,thd->shd', widen(first), widen(query_blk), precision=highest)
    value_part = jnp.einsum('hts,thd->shd', widen(second), widen(grad_blk), precision=highest)
    return key_part, value_part


def reference(queries, keys, values, out_grad, log_decay):
    blocks = SEQUENCE_LENGTH // BLOCK

    def split(array):
        return array.reshape(blocks, BLOCK, ATTENTION_HEADS, HEAD_DIM)

    cumul = jnp.cumsum(widen(log_decay).reshape(blocks, BLOCK, ATTENTION_HEADS), axis=1)
    data = (split(queries), split(keys), split(values), split(out_grad), cumul)

    def forward(state, item):
        query_blk, key_blk, value_blk, grad_blk, cumul_blk = item
        query_part = inner_query(query_blk, key_blk, value_blk, grad_blk, cumul_blk)
        total = cumul_blk[-1]
        before = jnp.exp(cumul_blk)
        after = jnp.exp(total[None, :] - cumul_blk)
        grad_query = query_part + before[:, :, None] * jnp.einsum('thb,hab->tha', widen(grad_blk), state, precision=highest)
        state = jnp.exp(total)[:, None, None] * state + jnp.einsum('sha,shb->hab', after[:, :, None] * widen(key_blk), widen(value_blk), precision=highest)
        return state, grad_query.astype(jnp.bfloat16)

    def backward(adjoint, item):
        query_blk, key_blk, value_blk, grad_blk, cumul_blk = item
        key_part, value_part = inner_keys(query_blk, key_blk, value_blk, grad_blk, cumul_blk)
        total = cumul_blk[-1]
        before = jnp.exp(cumul_blk)
        after = jnp.exp(total[None, :] - cumul_blk)
        grad_key = key_part + after[:, :, None] * jnp.einsum('shb,hab->sha', widen(value_blk), adjoint, precision=highest)
        grad_value = value_part + after[:, :, None] * jnp.einsum('sha,hab->shb', widen(key_blk), adjoint, precision=highest)
        adjoint = jnp.exp(total)[:, None, None] * adjoint + jnp.einsum('tha,thb->hab', before[:, :, None] * widen(query_blk), widen(grad_blk), precision=highest)
        return adjoint, (grad_key.astype(jnp.bfloat16), grad_value.astype(jnp.bfloat16))

    zero_state = jnp.zeros((ATTENTION_HEADS, HEAD_DIM, HEAD_DIM), jnp.float32)
    unused, grad_query = lax.scan(forward, zero_state, data)
    unused_too, (grad_key, grad_value) = lax.scan(backward, zero_state, data, reverse=True)
    width = ATTENTION_HEADS * HEAD_DIM
    return (grad_query.reshape(SEQUENCE_LENGTH, width), grad_key.reshape(SEQUENCE_LENGTH, width), grad_value.reshape(SEQUENCE_LENGTH, width))
```

```python
import jax
import jax.numpy as jnp
from jax import lax
from jax.sharding import PartitionSpec as P

BLOCK = 128
SEQ_EXP = ("seq", "exp")


def widen(array):
    return array.astype(jnp.float32)


def halves(array):
    high = array.astype(jnp.bfloat16)
    low = (array - widen(high)).astype(jnp.bfloat16)
    return (high, low)


def product(form, first_op, second_op):
    return jnp.einsum(form, first_op, second_op, preferred_element_type=jnp.float32)


def split_left(form, wide_op, narrow_op):
    high, low = halves(wide_op)
    return product(form, high, narrow_op) + product(form, low, narrow_op)


def split_right(form, narrow_op, wide_op):
    high, low = halves(wide_op)
    return product(form, narrow_op, high) + product(form, narrow_op, low)


def link(earlier, later):
    return (earlier[0] + later[0], jnp.exp(later[0])[:, None, None] * earlier[1] + later[1])


def carried_in(elem, axis, reverse):
    peers = lax.axis_size(axis)
    inclusive = elem
    exclusive = jax.tree.map(jnp.zeros_like, elem)
    shift = 1
    while shift < peers:
        if reverse:
            pairs = [(i, i - shift) for i in range(shift, peers)]
        else:
            pairs = [(i, i + shift) for i in range(peers - shift)]
        got = jax.tree.map(lambda part: lax.ppermute(part, axis, pairs), inclusive)
        exclusive = link(got, exclusive)
        shift *= 2
        if shift < peers:
            inclusive = link(got, inclusive)
    return exclusive


def running_sum(decay_blk):
    length = decay_blk.shape[1]
    lower = (
        lax.broadcasted_iota(jnp.int32, (length, length), 1)
        <= lax.broadcasted_iota(jnp.int32, (length, length), 0)
    ).astype(decay_blk.dtype)
    return jnp.einsum("ts,nsh->nth", lower, decay_blk, preferred_element_type=jnp.float32)


def unrolled(totals, pieces, reverse):
    blocks = totals.shape[0]
    heads, width = pieces.shape[1], pieces.shape[2]
    carry = jnp.zeros((heads, width, width), jnp.float32)
    logsum = jnp.zeros((heads,), jnp.float32)
    seen = [None] * blocks
    seen_log = [None] * blocks
    order = reversed(range(blocks)) if reverse else range(blocks)
    for i in order:
        seen[i] = carry
        seen_log[i] = logsum
        carry = jnp.exp(totals[i])[:, None, None] * carry + pieces[i]
        logsum = logsum + totals[i]
    return jnp.stack(seen), jnp.stack(seen_log), carry, logsum


def key_side(key_loc, value_loc, decay_loc):
    rows = key_loc.shape[0]
    heads = decay_loc.shape[1]
    width = key_loc.shape[1] // heads
    blocks = rows // BLOCK
    key_blk = key_loc.reshape(blocks, BLOCK, heads, width)
    value_blk = value_loc.reshape(blocks, BLOCK, heads, width)
    cumul = running_sum(decay_loc.reshape(blocks, BLOCK, heads))
    totals = cumul[:, -1, :]
    after = jnp.exp(totals[:, None, :] - cumul)
    contrib = split_left("nsha,nshb->nhab", after[..., None] * widen(key_blk), value_blk)
    prefix, prefix_log, dev_state, dev_log = unrolled(totals, contrib, False)
    return (key_blk, value_blk, cumul, totals, after, prefix, prefix_log, dev_state, dev_log)


def query_side(query_loc, grad_loc, cumul, totals):
    blocks, length, heads = cumul.shape
    width = query_loc.shape[1] // heads
    query_blk = query_loc.reshape(blocks, length, heads, width)
    grad_blk = grad_loc.reshape(blocks, length, heads, width)
    before = jnp.exp(cumul)
    updates = split_left("ntha,nthb->nhab", before[..., None] * widen(query_blk), grad_blk)
    suffix, suffix_log, dev_adjoint, unused = unrolled(totals, updates, True)
    return (query_blk, grad_blk, before, suffix, suffix_log, dev_adjoint)


def finish(
    query_blk,
    key_blk,
    value_blk,
    grad_blk,
    cumul,
    after,
    before,
    prefix,
    prefix_log,
    suffix,
    suffix_log,
    start_state,
    start_adjoint,
):
    state_prev = jnp.exp(prefix_log)[:, :, None, None] * start_state[None] + prefix
    adjoint = jnp.exp(suffix_log)[:, :, None, None] * start_adjoint[None] + suffix
    blocks, length, heads = cumul.shape
    width = key_blk.shape[3]
    heads_first = jnp.transpose(cumul, (0, 2, 1))
    spread = heads_first[:, :, :, None] - heads_first[:, :, None, :]
    causal = lax.broadcasted_iota(jnp.int32, (length, length), 1) <= lax.broadcasted_iota(
        jnp.int32, (length, length), 0
    )
    weights = jnp.where(
        causal[None, None], jnp.exp(jnp.where(causal[None, None], spread, 0.0)), 0.0
    )
    grad_scores = product("nthd,nshd->nhts", grad_blk, value_blk)
    key_scores = product("nthd,nshd->nhts", query_blk, key_blk)
    first = (weights * grad_scores).astype(jnp.bfloat16)
    second = (weights * key_scores).astype(jnp.bfloat16)
    query_part = product("nhts,nshd->nthd", first, key_blk)
    key_part = product("nhts,nthd->nshd", first, query_blk)
    value_part = product("nhts,nthd->nshd", second, grad_blk)
    grad_query = query_part + before[..., None] * split_right(
        "nthb,nhab->ntha", grad_blk, state_prev
    )
    adj_high, adj_low = halves(adjoint)
    grad_key = key_part + after[..., None] * (
        product("nshb,nhab->nsha", value_blk, adj_high)
        + product("nshb,nhab->nsha", value_blk, adj_low)
    )
    grad_value = value_part + after[..., None] * (
        product("nsha,nhab->nshb", key_blk, adj_high) + product("nsha,nhab->nshb", key_blk, adj_low)
    )
    rows = blocks * length
    flat_query = grad_query.astype(jnp.bfloat16).reshape(rows, heads * width)
    flat_key = grad_key.astype(jnp.bfloat16).reshape(rows, heads * width)
    flat_value = grad_value.astype(jnp.bfloat16).reshape(rows, heads * width)
    return (flat_query, flat_key, flat_value)


def by_target(array, peers):
    rows = array.shape[0]
    return jnp.transpose(array.reshape(rows, peers, -1), (1, 0, 2))


def body(queries, keys, values, out_grad, log_decay):
    peers = lax.axis_size("exp")
    rows = queries.shape[0]
    width = queries.shape[1] // peers
    lanes = 128
    decay_part = by_target(log_decay, peers)
    narrow = decay_part.shape[2]
    decay_part = jnp.pad(decay_part, ((0, 0), (0, 0), (0, lanes - narrow)))
    packed = jnp.concatenate(
        [by_target(x, peers) for x in (queries, keys, values, out_grad)] + [decay_part], axis=2
    )
    arrived = lax.all_to_all(packed, "exp", 0, 0, tiled=True)
    group_rows = peers * rows

    def column(i, size):
        return arrived[:, :, i * width : i * width + size].reshape(group_rows, size)

    query_loc, key_loc, value_loc, grad_loc = (column(i, width) for i in range(4))
    decay_loc = column(4, narrow)
    key_blk, value_blk, cumul, totals, after, prefix, prefix_log, dev_state, dev_log = key_side(
        key_loc, value_loc, decay_loc
    )
    start_state = carried_in((dev_log, dev_state), "seq", False)[1]
    query_blk, grad_blk, before, suffix, suffix_log, dev_adjoint = query_side(
        query_loc, grad_loc, cumul, totals
    )
    start_adjoint = carried_in((dev_log, dev_adjoint), "seq", True)[1]
    flat_query, flat_key, flat_value = finish(
        query_blk,
        key_blk,
        value_blk,
        grad_blk,
        cumul,
        after,
        before,
        prefix,
        prefix_log,
        suffix,
        suffix_log,
        start_state,
        start_adjoint,
    )
    out_packed = jnp.concatenate([flat_query, flat_key, flat_value], axis=1).reshape(
        peers, rows, 3 * width
    )
    back = lax.all_to_all(out_packed, "exp", 0, 0, tiled=True)

    def gathered(i):
        return jnp.transpose(back[:, :, i * width : (i + 1) * width], (1, 0, 2)).reshape(
            rows, peers * width
        )

    return tuple(gathered(i) for i in range(3))


def solution(mesh):
    placed = tuple(P(SEQ_EXP, None) for _ in range(5))
    return jax.shard_map(
        body,
        mesh=mesh,
        in_specs=placed,
        out_specs=(P(SEQ_EXP, None), P(SEQ_EXP, None), P(SEQ_EXP, None)),
        check_vma=False,
    )
```

```python
import jax
import jax.numpy as jnp
from jax import lax
from jax.sharding import PartitionSpec as P

BLOCK = 128
SEQ_EXP = ("seq", "exp")


def widen(array):
    return array.astype(jnp.float32)


def halves(array):
    high = array.astype(jnp.bfloat16)
    low = (array - widen(high)).astype(jnp.bfloat16)
    return (high, low)


def product(form, first_op, second_op):
    return jnp.einsum(form, first_op, second_op, preferred_element_type=jnp.float32)


def split_left(form, wide_op, narrow_op):
    high, low = halves(wide_op)
    return product(form, high, narrow_op) + product(form, low, narrow_op)


def split_right(form, narrow_op, wide_op):
    high, low = halves(wide_op)
    return product(form, narrow_op, high) + product(form, narrow_op, low)


def link(earlier, later):
    return (earlier[0] + later[0], jnp.exp(later[0])[:, None, None] * earlier[1] + later[1])


def carried_both(dev_log, dev_state, dev_adjoint, axis):
    peers = lax.axis_size(axis)
    here = lax.axis_index(axis)
    heads, width = dev_state.shape[0], dev_state.shape[2]
    share = heads * width // peers
    spare = 8
    logs = jnp.zeros((spare, width), jnp.float32).at[:heads, :].set(
        jnp.broadcast_to(dev_log[:, None], (heads, width))
    )
    payload = jnp.concatenate(
        [
            dev_state.reshape(peers, share, width),
            dev_adjoint.reshape(peers, share, width),
            jnp.broadcast_to(logs[None], (peers, spare, width)),
        ],
        axis=1,
    )
    got = lax.all_to_all(payload, axis, 0, 0, tiled=True)
    head = (here * share) // width
    pick = (lax.broadcasted_iota(jnp.int32, (heads,), 0) == head).astype(jnp.float32)
    totals = jnp.sum(got[:, 2 * share : 2 * share + heads, 0] * pick[None, :], axis=1)
    dst = lax.broadcasted_iota(jnp.int32, (peers, peers, peers), 0)
    src = lax.broadcasted_iota(jnp.int32, (peers, peers, peers), 1)
    mid = lax.broadcasted_iota(jnp.int32, (peers, peers, peers), 2)
    between_fwd = (src < mid) & (mid < dst)
    between_bwd = (dst < mid) & (mid < src)
    log_fwd = jnp.sum(jnp.where(between_fwd, totals[None, None, :], 0.0), axis=2)
    log_bwd = jnp.sum(jnp.where(between_bwd, totals[None, None, :], 0.0), axis=2)
    dst2 = lax.broadcasted_iota(jnp.int32, (peers, peers), 0)
    src2 = lax.broadcasted_iota(jnp.int32, (peers, peers), 1)
    w_fwd = jnp.where(src2 < dst2, jnp.exp(jnp.where(src2 < dst2, log_fwd, 0.0)), 0.0)
    w_bwd = jnp.where(src2 > dst2, jnp.exp(jnp.where(src2 > dst2, log_bwd, 0.0)), 0.0)
    highest = lax.Precision.HIGHEST
    state_rows = jnp.einsum("di,irc->drc", w_fwd, got[:, :share], precision=highest)
    adjoint_rows = jnp.einsum("di,irc->drc", w_bwd, got[:, share : 2 * share], precision=highest)
    back = lax.all_to_all(
        jnp.concatenate([state_rows, adjoint_rows], axis=1), axis, 0, 0, tiled=True
    )
    start_state = back[:, :share].reshape(heads, width, width)
    start_adjoint = back[:, share:].reshape(heads, width, width)
    return start_state, start_adjoint


def running_sum(decay_blk):
    length = decay_blk.shape[1]
    lower = (
        lax.broadcasted_iota(jnp.int32, (length, length), 1)
        <= lax.broadcasted_iota(jnp.int32, (length, length), 0)
    ).astype(decay_blk.dtype)
    return jnp.einsum("ts,nsh->nth", lower, decay_blk, preferred_element_type=jnp.float32)


def unrolled(totals, pieces, reverse):
    blocks = totals.shape[0]
    heads, width = pieces.shape[1], pieces.shape[2]
    carry = jnp.zeros((heads, width, width), jnp.float32)
    logsum = jnp.zeros((heads,), jnp.float32)
    seen = [None] * blocks
    seen_log = [None] * blocks
    order = reversed(range(blocks)) if reverse else range(blocks)
    for i in order:
        seen[i] = carry
        seen_log[i] = logsum
        carry = jnp.exp(totals[i])[:, None, None] * carry + pieces[i]
        logsum = logsum + totals[i]
    return jnp.stack(seen), jnp.stack(seen_log), carry, logsum


def key_side(key_loc, value_loc, decay_loc):
    rows = key_loc.shape[0]
    heads = decay_loc.shape[1]
    width = key_loc.shape[1] // heads
    blocks = rows // BLOCK
    key_blk = key_loc.reshape(blocks, BLOCK, heads, width)
    value_blk = value_loc.reshape(blocks, BLOCK, heads, width)
    cumul = running_sum(decay_loc.reshape(blocks, BLOCK, heads))
    totals = cumul[:, -1, :]
    after = jnp.exp(totals[:, None, :] - cumul)
    contrib = split_left("nsha,nshb->nhab", after[..., None] * widen(key_blk), value_blk)
    prefix, prefix_log, dev_state, dev_log = unrolled(totals, contrib, False)
    return (key_blk, value_blk, cumul, totals, after, prefix, prefix_log, dev_state, dev_log)


def query_side(query_loc, grad_loc, cumul, totals):
    blocks, length, heads = cumul.shape
    width = query_loc.shape[1] // heads
    query_blk = query_loc.reshape(blocks, length, heads, width)
    grad_blk = grad_loc.reshape(blocks, length, heads, width)
    before = jnp.exp(cumul)
    updates = split_left("ntha,nthb->nhab", before[..., None] * widen(query_blk), grad_blk)
    suffix, suffix_log, dev_adjoint, unused = unrolled(totals, updates, True)
    return (query_blk, grad_blk, before, suffix, suffix_log, dev_adjoint)


def finish(
    query_blk,
    key_blk,
    value_blk,
    grad_blk,
    cumul,
    after,
    before,
    prefix,
    prefix_log,
    suffix,
    suffix_log,
    start_state,
    start_adjoint,
):
    state_prev = jnp.exp(prefix_log)[:, :, None, None] * start_state[None] + prefix
    adjoint = jnp.exp(suffix_log)[:, :, None, None] * start_adjoint[None] + suffix
    blocks, length, heads = cumul.shape
    width = key_blk.shape[3]
    heads_first = jnp.transpose(cumul, (0, 2, 1))
    spread = heads_first[:, :, :, None] - heads_first[:, :, None, :]
    causal = lax.broadcasted_iota(jnp.int32, (length, length), 1) <= lax.broadcasted_iota(
        jnp.int32, (length, length), 0
    )
    weights = jnp.where(
        causal[None, None], jnp.exp(jnp.where(causal[None, None], spread, 0.0)), 0.0
    )
    grad_scores = product("nthd,nshd->nhts", grad_blk, value_blk)
    key_scores = product("nthd,nshd->nhts", query_blk, key_blk)
    first = (weights * grad_scores).astype(jnp.bfloat16)
    second = (weights * key_scores).astype(jnp.bfloat16)
    query_part = product("nhts,nshd->nthd", first, key_blk)
    key_part = product("nhts,nthd->nshd", first, query_blk)
    value_part = product("nhts,nthd->nshd", second, grad_blk)
    grad_query = query_part + before[..., None] * split_right(
        "nthb,nhab->ntha", grad_blk, state_prev
    )
    adj_high, adj_low = halves(adjoint)
    grad_key = key_part + after[..., None] * (
        product("nshb,nhab->nsha", value_blk, adj_high)
        + product("nshb,nhab->nsha", value_blk, adj_low)
    )
    grad_value = value_part + after[..., None] * (
        product("nsha,nhab->nshb", key_blk, adj_high) + product("nsha,nhab->nshb", key_blk, adj_low)
    )
    rows = blocks * length
    flat_query = grad_query.astype(jnp.bfloat16).reshape(rows, heads * width)
    flat_key = grad_key.astype(jnp.bfloat16).reshape(rows, heads * width)
    flat_value = grad_value.astype(jnp.bfloat16).reshape(rows, heads * width)
    return (flat_query, flat_key, flat_value)


def by_target(array, peers):
    rows = array.shape[0]
    return jnp.transpose(array.reshape(rows, peers, -1), (1, 0, 2))


def body(queries, keys, values, out_grad, log_decay):
    peers = lax.axis_size("exp")
    rows = queries.shape[0]
    width = queries.shape[1] // peers
    lanes = 128
    decay_part = by_target(log_decay, peers)
    narrow = decay_part.shape[2]
    decay_part = jnp.pad(decay_part, ((0, 0), (0, 0), (0, lanes - narrow)))
    packed = jnp.concatenate(
        [by_target(x, peers) for x in (queries, keys, values, out_grad)] + [decay_part], axis=2
    )
    arrived = lax.all_to_all(packed, "exp", 0, 0, tiled=True)
    group_rows = peers * rows

    def column(i, size):
        return arrived[:, :, i * width : i * width + size].reshape(group_rows, size)

    query_loc, key_loc, value_loc, grad_loc = (column(i, width) for i in range(4))
    decay_loc = column(4, narrow)
    key_blk, value_blk, cumul, totals, after, prefix, prefix_log, dev_state, dev_log = key_side(
        key_loc, value_loc, decay_loc
    )
    query_blk, grad_blk, before, suffix, suffix_log, dev_adjoint = query_side(
        query_loc, grad_loc, cumul, totals
    )
    start_state, start_adjoint = carried_both(dev_log, dev_state, dev_adjoint, "seq")
    flat_query, flat_key, flat_value = finish(
        query_blk,
        key_blk,
        value_blk,
        grad_blk,
        cumul,
        after,
        before,
        prefix,
        prefix_log,
        suffix,
        suffix_log,
        start_state,
        start_adjoint,
    )
    out_packed = jnp.concatenate([flat_query, flat_key, flat_value], axis=1).reshape(
        peers, rows, 3 * width
    )
    back = lax.all_to_all(out_packed, "exp", 0, 0, tiled=True)

    def gathered(i):
        return jnp.transpose(back[:, :, i * width : (i + 1) * width], (1, 0, 2)).reshape(
            rows, peers * width
        )

    return tuple(gathered(i) for i in range(3))


def solution(mesh):
    placed = tuple(P(SEQ_EXP, None) for _ in range(5))
    return jax.shard_map(
        body,
        mesh=mesh,
        in_specs=placed,
        out_specs=(P(SEQ_EXP, None), P(SEQ_EXP, None), P(SEQ_EXP, None)),
        check_vma=False,
    )
```

```python
import jax
import jax.numpy as jnp
from jax import lax
from jax.sharding import PartitionSpec as P

BLOCK = 128
SEQ_EXP = ("seq", "exp")


def widen(array):
    return array.astype(jnp.float32)


def halves(array):
    high = array.astype(jnp.bfloat16)
    low = (array - widen(high)).astype(jnp.bfloat16)
    return (high, low)


def product(form, first_op, second_op):
    return jnp.einsum(form, first_op, second_op, preferred_element_type=jnp.float32)


def split_left(form, wide_op, narrow_op):
    high, low = halves(wide_op)
    return product(form, high, narrow_op) + product(form, low, narrow_op)


def split_right(form, narrow_op, wide_op):
    high, low = halves(wide_op)
    return product(form, narrow_op, high) + product(form, narrow_op, low)


def link(earlier, later):
    return (earlier[0] + later[0], jnp.exp(later[0])[:, None, None] * earlier[1] + later[1])


def carried_both(dev_log, dev_state, dev_adjoint, axis):
    peers = lax.axis_size(axis)
    here = lax.axis_index(axis)
    heads, width = dev_state.shape[0], dev_state.shape[2]
    share = heads * width // peers
    spare = 8
    logs = jnp.zeros((spare, width), jnp.float32).at[:heads, :].set(
        jnp.broadcast_to(dev_log[:, None], (heads, width))
    )
    payload = jnp.concatenate(
        [
            dev_state.reshape(peers, share, width),
            dev_adjoint.reshape(peers, share, width),
            jnp.broadcast_to(logs[None], (peers, spare, width)),
        ],
        axis=1,
    )
    got = lax.all_to_all(payload, axis, 0, 0, tiled=True)
    head = (here * share) // width
    pick = (lax.broadcasted_iota(jnp.int32, (heads,), 0) == head).astype(jnp.float32)
    totals = jnp.sum(got[:, 2 * share : 2 * share + heads, 0] * pick[None, :], axis=1)
    dst = lax.broadcasted_iota(jnp.int32, (peers, peers, peers), 0)
    src = lax.broadcasted_iota(jnp.int32, (peers, peers, peers), 1)
    mid = lax.broadcasted_iota(jnp.int32, (peers, peers, peers), 2)
    between_fwd = (src < mid) & (mid < dst)
    between_bwd = (dst < mid) & (mid < src)
    log_fwd = jnp.sum(jnp.where(between_fwd, totals[None, None, :], 0.0), axis=2)
    log_bwd = jnp.sum(jnp.where(between_bwd, totals[None, None, :], 0.0), axis=2)
    dst2 = lax.broadcasted_iota(jnp.int32, (peers, peers), 0)
    src2 = lax.broadcasted_iota(jnp.int32, (peers, peers), 1)
    w_fwd = jnp.where(src2 < dst2, jnp.exp(jnp.where(src2 < dst2, log_fwd, 0.0)), 0.0)
    w_bwd = jnp.where(src2 > dst2, jnp.exp(jnp.where(src2 > dst2, log_bwd, 0.0)), 0.0)
    highest = lax.Precision.HIGHEST
    state_rows = jnp.einsum("di,irc->drc", w_fwd, got[:, :share], precision=highest)
    adjoint_rows = jnp.einsum("di,irc->drc", w_bwd, got[:, share : 2 * share], precision=highest)
    back = lax.all_to_all(
        jnp.concatenate([state_rows, adjoint_rows], axis=1), axis, 0, 0, tiled=True
    )
    start_state = back[:, :share].reshape(heads, width, width)
    start_adjoint = back[:, share:].reshape(heads, width, width)
    return start_state, start_adjoint


def running_sum(decay_blk):
    length = decay_blk.shape[1]
    lower = (
        lax.broadcasted_iota(jnp.int32, (length, length), 1)
        <= lax.broadcasted_iota(jnp.int32, (length, length), 0)
    ).astype(decay_blk.dtype)
    return jnp.einsum("ts,nsh->nth", lower, decay_blk, preferred_element_type=jnp.float32)


def unrolled(totals, pieces, reverse):
    blocks = totals.shape[0]
    heads, width = pieces.shape[1], pieces.shape[2]
    carry = jnp.zeros((heads, width, width), jnp.float32)
    logsum = jnp.zeros((heads,), jnp.float32)
    seen = [None] * blocks
    seen_log = [None] * blocks
    order = reversed(range(blocks)) if reverse else range(blocks)
    for i in order:
        seen[i] = carry
        seen_log[i] = logsum
        carry = jnp.exp(totals[i])[:, None, None] * carry + pieces[i]
        logsum = logsum + totals[i]
    return jnp.stack(seen), jnp.stack(seen_log), carry, logsum


def local_block(queries, keys, values, out_grad, log_decay):
    length = queries.shape[0]
    heads = log_decay.shape[1]
    width = queries.shape[1] // heads
    query_blk = queries.reshape(length, heads, width)
    key_blk = keys.reshape(length, heads, width)
    value_blk = values.reshape(length, heads, width)
    grad_blk = out_grad.reshape(length, heads, width)
    cumul = running_sum(log_decay[None])[0]
    total = cumul[-1]
    after = jnp.exp(total[None, :] - cumul)
    before = jnp.exp(cumul)
    contrib = split_left("sha,shb->hab", after[..., None] * widen(key_blk), value_blk)
    update = split_left("tha,thb->hab", before[..., None] * widen(query_blk), grad_blk)
    return (query_blk, key_blk, value_blk, grad_blk, cumul, after, before, contrib, update)


def intra(query_blk, key_blk, value_blk, grad_blk, cumul):
    length = cumul.shape[0]
    heads_first = cumul.T
    spread = heads_first[:, :, None] - heads_first[:, None, :]
    causal = lax.broadcasted_iota(jnp.int32, (length, length), 1) <= lax.broadcasted_iota(
        jnp.int32, (length, length), 0
    )
    weights = jnp.where(causal[None], jnp.exp(jnp.where(causal[None], spread, 0.0)), 0.0)
    grad_scores = product("thd,shd->hts", grad_blk, value_blk)
    key_scores = product("thd,shd->hts", query_blk, key_blk)
    first = (weights * grad_scores).astype(jnp.bfloat16)
    second = (weights * key_scores).astype(jnp.bfloat16)
    query_part = product("hts,shd->thd", first, key_blk)
    key_part = product("hts,thd->shd", first, query_blk)
    value_part = product("hts,thd->shd", second, grad_blk)
    return query_part, key_part, value_part


def body(queries, keys, values, out_grad, log_decay):
    peers = lax.axis_size("exp")
    length = queries.shape[0]
    heads = log_decay.shape[1]
    width = queries.shape[1] // heads
    group = heads // peers
    (query_blk, key_blk, value_blk, grad_blk, cumul, after, before, contrib, update) = local_block(
        queries, keys, values, out_grad, log_decay
    )
    share = group * width
    decay_rows = jnp.transpose(log_decay.reshape(length, peers, group), (1, 2, 0))
    pad_rows = 16
    decay_rows = jnp.pad(decay_rows, ((0, 0), (0, pad_rows - group), (0, 0)))
    packed = jnp.concatenate(
        [
            contrib.astype(jnp.bfloat16).reshape(peers, share, width),
            update.astype(jnp.bfloat16).reshape(peers, share, width),
            decay_rows.astype(jnp.bfloat16),
        ],
        axis=1,
    )
    got = lax.all_to_all(packed, "exp", 0, 0, tiled=True)
    contrib_g = widen(got[:, :share]).reshape(peers, group, width, width)
    update_g = widen(got[:, share : 2 * share]).reshape(peers, group, width, width)
    totals = jnp.sum(widen(got[:, 2 * share : 2 * share + group]), axis=2)
    prefix, prefix_log, dev_state, dev_log = unrolled(totals, contrib_g, False)
    suffix, suffix_log, dev_adjoint, unused = unrolled(totals, update_g, True)
    start_state, start_adjoint = carried_both(dev_log, dev_state, dev_adjoint, "seq")
    state_prev = jnp.exp(prefix_log)[:, :, None, None] * start_state[None] + prefix
    adjoint = jnp.exp(suffix_log)[:, :, None, None] * start_adjoint[None] + suffix
    returned = jnp.concatenate(
        [
            state_prev.astype(jnp.bfloat16).reshape(peers, share, width),
            adjoint.astype(jnp.bfloat16).reshape(peers, share, width),
        ],
        axis=1,
    )
    back = lax.all_to_all(returned, "exp", 0, 0, tiled=True)
    state_in = back[:, :share].reshape(heads, width, width)
    adjoint_in = back[:, share:].reshape(heads, width, width)
    query_part, key_part, value_part = intra(query_blk, key_blk, value_blk, grad_blk, cumul)
    grad_query = query_part + before[..., None] * product("thb,hab->tha", grad_blk, state_in)
    grad_key = key_part + after[..., None] * product("shb,hab->sha", value_blk, adjoint_in)
    grad_value = value_part + after[..., None] * product("sha,hab->shb", key_blk, adjoint_in)
    flat = lambda x: x.astype(jnp.bfloat16).reshape(length, heads * width)
    return (flat(grad_query), flat(grad_key), flat(grad_value))


def solution(mesh):
    placed = tuple(P(SEQ_EXP, None) for _ in range(5))
    return jax.shard_map(
        body,
        mesh=mesh,
        in_specs=placed,
        out_specs=(P(SEQ_EXP, None), P(SEQ_EXP, None), P(SEQ_EXP, None)),
        check_vma=False,
    )
```

```python
import jax
import jax.numpy as jnp
from jax import lax
from jax.sharding import PartitionSpec as P

BLOCK = 128
SEQ_EXP = ("seq", "exp")


def widen(array):
    return array.astype(jnp.float32)


def halves(array):
    high = array.astype(jnp.bfloat16)
    low = (array - widen(high)).astype(jnp.bfloat16)
    return (high, low)


def product(form, first_op, second_op):
    return jnp.einsum(form, first_op, second_op, preferred_element_type=jnp.float32)


def split_left(form, wide_op, narrow_op):
    high, low = halves(wide_op)
    return product(form, high, narrow_op) + product(form, low, narrow_op)


def split_right(form, narrow_op, wide_op):
    high, low = halves(wide_op)
    return product(form, narrow_op, high) + product(form, narrow_op, low)


def link(earlier, later):
    return (earlier[0] + later[0], jnp.exp(later[0])[:, None, None] * earlier[1] + later[1])


def carried_both(dev_log, dev_state, dev_adjoint, axis):
    peers = lax.axis_size(axis)
    here = lax.axis_index(axis)
    heads, width = dev_state.shape[0], dev_state.shape[2]
    share = heads * width // peers
    spare = 8
    logs = jnp.zeros((spare, width), jnp.float32).at[:heads, :].set(
        jnp.broadcast_to(dev_log[:, None], (heads, width))
    )
    payload = jnp.concatenate(
        [
            dev_state.reshape(peers, share, width),
            dev_adjoint.reshape(peers, share, width),
            jnp.broadcast_to(logs[None], (peers, spare, width)),
        ],
        axis=1,
    )
    got = lax.all_to_all(payload, axis, 0, 0, tiled=True)
    head = (here * share) // width
    pick = (lax.broadcasted_iota(jnp.int32, (heads,), 0) == head).astype(jnp.float32)
    totals = jnp.sum(got[:, 2 * share : 2 * share + heads, 0] * pick[None, :], axis=1)
    dst = lax.broadcasted_iota(jnp.int32, (peers, peers, peers), 0)
    src = lax.broadcasted_iota(jnp.int32, (peers, peers, peers), 1)
    mid = lax.broadcasted_iota(jnp.int32, (peers, peers, peers), 2)
    between_fwd = (src < mid) & (mid < dst)
    between_bwd = (dst < mid) & (mid < src)
    log_fwd = jnp.sum(jnp.where(between_fwd, totals[None, None, :], 0.0), axis=2)
    log_bwd = jnp.sum(jnp.where(between_bwd, totals[None, None, :], 0.0), axis=2)
    dst2 = lax.broadcasted_iota(jnp.int32, (peers, peers), 0)
    src2 = lax.broadcasted_iota(jnp.int32, (peers, peers), 1)
    w_fwd = jnp.where(src2 < dst2, jnp.exp(jnp.where(src2 < dst2, log_fwd, 0.0)), 0.0)
    w_bwd = jnp.where(src2 > dst2, jnp.exp(jnp.where(src2 > dst2, log_bwd, 0.0)), 0.0)
    highest = lax.Precision.HIGHEST
    state_rows = jnp.einsum("di,irc->drc", w_fwd, got[:, :share], precision=highest)
    adjoint_rows = jnp.einsum("di,irc->drc", w_bwd, got[:, share : 2 * share], precision=highest)
    back = lax.all_to_all(
        jnp.concatenate([state_rows, adjoint_rows], axis=1), axis, 0, 0, tiled=True
    )
    start_state = back[:, :share].reshape(heads, width, width)
    start_adjoint = back[:, share:].reshape(heads, width, width)
    return start_state, start_adjoint


def running_sum(decay_blk):
    length = decay_blk.shape[1]
    lower = (
        lax.broadcasted_iota(jnp.int32, (length, length), 1)
        <= lax.broadcasted_iota(jnp.int32, (length, length), 0)
    ).astype(decay_blk.dtype)
    return jnp.einsum("ts,nsh->nth", lower, decay_blk, preferred_element_type=jnp.float32)


def within_group(totals, pieces, reverse):
    blocks = totals.shape[0]
    at = lax.broadcasted_iota(jnp.int32, (blocks, blocks, blocks), 0)
    src = lax.broadcasted_iota(jnp.int32, (blocks, blocks, blocks), 1)
    mid = lax.broadcasted_iota(jnp.int32, (blocks, blocks, blocks), 2)
    between = ((at < mid) & (mid < src)) if reverse else ((src < mid) & (mid < at))
    logs = jnp.sum(jnp.where(between[..., None], totals[None, None], 0.0), axis=2)
    pos = lax.broadcasted_iota(jnp.int32, (blocks, blocks), 0)
    other = lax.broadcasted_iota(jnp.int32, (blocks, blocks), 1)
    earlier = (other > pos) if reverse else (other < pos)
    later = (other < pos) if reverse else (other > pos)
    weights = jnp.where(earlier[..., None], jnp.exp(jnp.where(earlier[..., None], logs, 0.0)), 0.0)
    seen_log = jnp.sum(jnp.where(earlier[..., None], totals[None], 0.0), axis=1)
    tail_log = jnp.sum(jnp.where(later[..., None], totals[None], 0.0), axis=1)
    highest = lax.Precision.HIGHEST
    seen = jnp.einsum("ijh,jhab->ihab", weights, pieces, precision=highest)
    whole = jnp.einsum("jh,jhab->hab", jnp.exp(tail_log), pieces, precision=highest)
    return seen, seen_log, whole, jnp.sum(totals, axis=0)


def local_block(queries, keys, values, out_grad, log_decay):
    length = queries.shape[0]
    heads = log_decay.shape[1]
    width = queries.shape[1] // heads
    query_blk = queries.reshape(length, heads, width)
    key_blk = keys.reshape(length, heads, width)
    value_blk = values.reshape(length, heads, width)
    grad_blk = out_grad.reshape(length, heads, width)
    cumul = running_sum(log_decay[None])[0]
    total = cumul[-1]
    after = jnp.exp(total[None, :] - cumul)
    before = jnp.exp(cumul)
    contrib = split_left("sha,shb->hab", after[..., None] * widen(key_blk), value_blk)
    update = split_left("tha,thb->hab", before[..., None] * widen(query_blk), grad_blk)
    return (query_blk, key_blk, value_blk, grad_blk, cumul, after, before, contrib, update)


def intra(query_blk, key_blk, value_blk, grad_blk, cumul):
    length = cumul.shape[0]
    heads_first = cumul.T
    spread = heads_first[:, :, None] - heads_first[:, None, :]
    causal = lax.broadcasted_iota(jnp.int32, (length, length), 1) <= lax.broadcasted_iota(
        jnp.int32, (length, length), 0
    )
    weights = jnp.where(causal[None], jnp.exp(jnp.where(causal[None], spread, 0.0)), 0.0)
    grad_scores = product("thd,shd->hts", grad_blk, value_blk)
    key_scores = product("thd,shd->hts", query_blk, key_blk)
    first = (weights * grad_scores).astype(jnp.bfloat16)
    second = (weights * key_scores).astype(jnp.bfloat16)
    query_part = product("hts,shd->thd", first, key_blk)
    key_part = product("hts,thd->shd", first, query_blk)
    value_part = product("hts,thd->shd", second, grad_blk)
    return query_part, key_part, value_part


def body(queries, keys, values, out_grad, log_decay):
    peers = lax.axis_size("exp")
    length = queries.shape[0]
    heads = log_decay.shape[1]
    width = queries.shape[1] // heads
    group = heads // peers
    (query_blk, key_blk, value_blk, grad_blk, cumul, after, before, contrib, update) = local_block(
        queries, keys, values, out_grad, log_decay
    )
    share = group * width
    decay_rows = jnp.transpose(log_decay.reshape(length, peers, group), (1, 2, 0))
    pad_rows = 16
    decay_rows = jnp.pad(decay_rows, ((0, 0), (0, pad_rows - group), (0, 0)))
    packed = jnp.concatenate(
        [
            contrib.astype(jnp.bfloat16).reshape(peers, share, width),
            update.astype(jnp.bfloat16).reshape(peers, share, width),
            decay_rows.astype(jnp.bfloat16),
        ],
        axis=1,
    )
    got = lax.all_to_all(packed, "exp", 0, 0, tiled=True)
    contrib_g = widen(got[:, :share]).reshape(peers, group, width, width)
    update_g = widen(got[:, share : 2 * share]).reshape(peers, group, width, width)
    totals = jnp.sum(widen(got[:, 2 * share : 2 * share + group]), axis=2)
    query_part, key_part, value_part = intra(query_blk, key_blk, value_blk, grad_blk, cumul)
    totals, contrib_g, update_g, query_part, key_part, value_part = lax.optimization_barrier(
        (totals, contrib_g, update_g, query_part, key_part, value_part)
    )
    prefix, prefix_log, dev_state, dev_log = within_group(totals, contrib_g, False)
    suffix, suffix_log, dev_adjoint, unused = within_group(totals, update_g, True)
    start_state, start_adjoint = carried_both(dev_log, dev_state, dev_adjoint, "seq")
    state_prev = jnp.exp(prefix_log)[:, :, None, None] * start_state[None] + prefix
    adjoint = jnp.exp(suffix_log)[:, :, None, None] * start_adjoint[None] + suffix
    returned = jnp.concatenate(
        [
            state_prev.astype(jnp.bfloat16).reshape(peers, share, width),
            adjoint.astype(jnp.bfloat16).reshape(peers, share, width),
        ],
        axis=1,
    )
    back = lax.all_to_all(returned, "exp", 0, 0, tiled=True)
    state_in = back[:, :share].reshape(heads, width, width)
    adjoint_in = back[:, share:].reshape(heads, width, width)
    grad_query = query_part + before[..., None] * product("thb,hab->tha", grad_blk, state_in)
    grad_key = key_part + after[..., None] * product("shb,hab->sha", value_blk, adjoint_in)
    grad_value = value_part + after[..., None] * product("sha,hab->shb", key_blk, adjoint_in)
    flat = lambda x: x.astype(jnp.bfloat16).reshape(length, heads * width)
    return (flat(grad_query), flat(grad_key), flat(grad_value))


def solution(mesh):
    placed = tuple(P(SEQ_EXP, None) for _ in range(5))
    return jax.shard_map(
        body,
        mesh=mesh,
        in_specs=placed,
        out_specs=(P(SEQ_EXP, None), P(SEQ_EXP, None), P(SEQ_EXP, None)),
        check_vma=False,
    )
```

```python
import jax
import jax.numpy as jnp
from jax import lax
from jax.sharding import PartitionSpec as P

BLOCK = 128
SEQ_EXP = ("seq", "exp")


def widen(array):
    return array.astype(jnp.float32)


def halves(array):
    high = array.astype(jnp.bfloat16)
    low = (array - widen(high)).astype(jnp.bfloat16)
    return (high, low)


def product(form, first_op, second_op):
    return jnp.einsum(form, first_op, second_op, preferred_element_type=jnp.float32)


def split_left(form, wide_op, narrow_op):
    high, low = halves(wide_op)
    return product(form, high, narrow_op) + product(form, low, narrow_op)


def split_right(form, narrow_op, wide_op):
    high, low = halves(wide_op)
    return product(form, narrow_op, high) + product(form, narrow_op, low)


def link(earlier, later):
    return (earlier[0] + later[0], jnp.exp(later[0])[:, None, None] * earlier[1] + later[1])


def pieces_of(array):
    high = array.astype(jnp.bfloat16)
    rest = array - widen(high)
    mid = rest.astype(jnp.bfloat16)
    low = (rest - widen(mid)).astype(jnp.bfloat16)
    return high, mid, low


def carried_both(dev_log, dev_state, dev_adjoint, axis):
    peers = lax.axis_size(axis)
    here = lax.axis_index(axis)
    heads, width = dev_state.shape[0], dev_state.shape[2]
    share = heads * width // peers
    spare = 16
    logs = jnp.zeros((spare, width), jnp.bfloat16)
    for i, part in enumerate(pieces_of(dev_log)):
        logs = logs.at[i * heads : (i + 1) * heads, :].set(
            jnp.broadcast_to(part[:, None], (heads, width))
        )
    payload = jnp.concatenate(
        [
            dev_state.astype(jnp.bfloat16).reshape(peers, share, width),
            dev_adjoint.astype(jnp.bfloat16).reshape(peers, share, width),
            jnp.broadcast_to(logs[None], (peers, spare, width)),
        ],
        axis=1,
    )
    got = lax.all_to_all(payload, axis, 0, 0, tiled=True)
    head = (here * share) // width
    pick = (lax.broadcasted_iota(jnp.int32, (heads,), 0) == head).astype(jnp.float32)
    log_rows = widen(got[:, 2 * share : 2 * share + 3 * heads, 0]).reshape(peers, 3, heads)
    totals = jnp.sum(log_rows[:, 0] * pick[None, :], axis=1)
    totals = totals + jnp.sum(log_rows[:, 1] * pick[None, :], axis=1)
    totals = totals + jnp.sum(log_rows[:, 2] * pick[None, :], axis=1)
    dst = lax.broadcasted_iota(jnp.int32, (peers, peers, peers), 0)
    src = lax.broadcasted_iota(jnp.int32, (peers, peers, peers), 1)
    mid = lax.broadcasted_iota(jnp.int32, (peers, peers, peers), 2)
    between_fwd = (src < mid) & (mid < dst)
    between_bwd = (dst < mid) & (mid < src)
    log_fwd = jnp.sum(jnp.where(between_fwd, totals[None, None, :], 0.0), axis=2)
    log_bwd = jnp.sum(jnp.where(between_bwd, totals[None, None, :], 0.0), axis=2)
    dst2 = lax.broadcasted_iota(jnp.int32, (peers, peers), 0)
    src2 = lax.broadcasted_iota(jnp.int32, (peers, peers), 1)
    w_fwd = jnp.where(src2 < dst2, jnp.exp(jnp.where(src2 < dst2, log_fwd, 0.0)), 0.0)
    w_bwd = jnp.where(src2 > dst2, jnp.exp(jnp.where(src2 > dst2, log_bwd, 0.0)), 0.0)
    highest = lax.Precision.HIGHEST
    state_rows = jnp.einsum("di,irc->drc", w_fwd, widen(got[:, :share]), precision=highest)
    adjoint_rows = jnp.einsum(
        "di,irc->drc", w_bwd, widen(got[:, share : 2 * share]), precision=highest
    )
    back = lax.all_to_all(
        jnp.concatenate([state_rows, adjoint_rows], axis=1).astype(jnp.bfloat16),
        axis,
        0,
        0,
        tiled=True,
    )
    start_state = widen(back[:, :share]).reshape(heads, width, width)
    start_adjoint = widen(back[:, share:]).reshape(heads, width, width)
    return start_state, start_adjoint


def running_sum(decay_blk):
    length = decay_blk.shape[1]
    lower = (
        lax.broadcasted_iota(jnp.int32, (length, length), 1)
        <= lax.broadcasted_iota(jnp.int32, (length, length), 0)
    ).astype(decay_blk.dtype)
    return jnp.einsum("ts,nsh->nth", lower, decay_blk, preferred_element_type=jnp.float32)


def within_group(totals, pieces, reverse):
    blocks = totals.shape[0]
    at = lax.broadcasted_iota(jnp.int32, (blocks, blocks, blocks), 0)
    src = lax.broadcasted_iota(jnp.int32, (blocks, blocks, blocks), 1)
    mid = lax.broadcasted_iota(jnp.int32, (blocks, blocks, blocks), 2)
    between = ((at < mid) & (mid < src)) if reverse else ((src < mid) & (mid < at))
    logs = jnp.sum(jnp.where(between[..., None], totals[None, None], 0.0), axis=2)
    pos = lax.broadcasted_iota(jnp.int32, (blocks, blocks), 0)
    other = lax.broadcasted_iota(jnp.int32, (blocks, blocks), 1)
    earlier = (other > pos) if reverse else (other < pos)
    later = (other < pos) if reverse else (other > pos)
    weights = jnp.where(earlier[..., None], jnp.exp(jnp.where(earlier[..., None], logs, 0.0)), 0.0)
    seen_log = jnp.sum(jnp.where(earlier[..., None], totals[None], 0.0), axis=1)
    tail_log = jnp.sum(jnp.where(later[..., None], totals[None], 0.0), axis=1)
    highest = lax.Precision.HIGHEST
    seen = jnp.einsum("ijh,jhab->ihab", weights, pieces, precision=highest)
    whole = jnp.einsum("jh,jhab->hab", jnp.exp(tail_log), pieces, precision=highest)
    return seen, seen_log, whole, jnp.sum(totals, axis=0)


def local_block(queries, keys, values, out_grad, log_decay):
    length = queries.shape[0]
    heads = log_decay.shape[1]
    width = queries.shape[1] // heads
    query_blk = queries.reshape(length, heads, width)
    key_blk = keys.reshape(length, heads, width)
    value_blk = values.reshape(length, heads, width)
    grad_blk = out_grad.reshape(length, heads, width)
    cumul = running_sum(log_decay[None])[0]
    total = cumul[-1]
    after = jnp.exp(total[None, :] - cumul)
    before = jnp.exp(cumul)
    contrib = split_left("sha,shb->hab", after[..., None] * widen(key_blk), value_blk)
    update = split_left("tha,thb->hab", before[..., None] * widen(query_blk), grad_blk)
    return (query_blk, key_blk, value_blk, grad_blk, cumul, after, before, contrib, update)


def intra(query_blk, key_blk, value_blk, grad_blk, cumul):
    length = cumul.shape[0]
    heads_first = cumul.T
    spread = heads_first[:, :, None] - heads_first[:, None, :]
    causal = lax.broadcasted_iota(jnp.int32, (length, length), 1) <= lax.broadcasted_iota(
        jnp.int32, (length, length), 0
    )
    weights = jnp.where(causal[None], jnp.exp(jnp.where(causal[None], spread, 0.0)), 0.0)
    grad_scores = product("thd,shd->hts", grad_blk, value_blk)
    key_scores = product("thd,shd->hts", query_blk, key_blk)
    first = (weights * grad_scores).astype(jnp.bfloat16)
    second = (weights * key_scores).astype(jnp.bfloat16)
    query_part = product("hts,shd->thd", first, key_blk)
    key_part = product("hts,thd->shd", first, query_blk)
    value_part = product("hts,thd->shd", second, grad_blk)
    return query_part, key_part, value_part


def body(queries, keys, values, out_grad, log_decay):
    peers = lax.axis_size("exp")
    length = queries.shape[0]
    heads = log_decay.shape[1]
    width = queries.shape[1] // heads
    group = heads // peers
    (query_blk, key_blk, value_blk, grad_blk, cumul, after, before, contrib, update) = local_block(
        queries, keys, values, out_grad, log_decay
    )
    share = group * width
    decay_rows = jnp.transpose(log_decay.reshape(length, peers, group), (1, 2, 0))
    pad_rows = 16
    decay_rows = jnp.pad(decay_rows, ((0, 0), (0, pad_rows - group), (0, 0)))
    packed = jnp.concatenate(
        [
            contrib.astype(jnp.bfloat16).reshape(peers, share, width),
            update.astype(jnp.bfloat16).reshape(peers, share, width),
            decay_rows.astype(jnp.bfloat16),
        ],
        axis=1,
    )
    got = lax.all_to_all(packed, "exp", 0, 0, tiled=True)
    contrib_g = widen(got[:, :share]).reshape(peers, group, width, width)
    update_g = widen(got[:, share : 2 * share]).reshape(peers, group, width, width)
    totals = jnp.sum(widen(got[:, 2 * share : 2 * share + group]), axis=2)
    query_part, key_part, value_part = intra(query_blk, key_blk, value_blk, grad_blk, cumul)
    totals, contrib_g, update_g, query_part, key_part, value_part = lax.optimization_barrier(
        (totals, contrib_g, update_g, query_part, key_part, value_part)
    )
    prefix, prefix_log, dev_state, dev_log = within_group(totals, contrib_g, False)
    suffix, suffix_log, dev_adjoint, unused = within_group(totals, update_g, True)
    start_state, start_adjoint = carried_both(dev_log, dev_state, dev_adjoint, "seq")
    state_prev = jnp.exp(prefix_log)[:, :, None, None] * start_state[None] + prefix
    adjoint = jnp.exp(suffix_log)[:, :, None, None] * start_adjoint[None] + suffix
    returned = jnp.concatenate(
        [
            state_prev.astype(jnp.bfloat16).reshape(peers, share, width),
            adjoint.astype(jnp.bfloat16).reshape(peers, share, width),
        ],
        axis=1,
    )
    back = lax.all_to_all(returned, "exp", 0, 0, tiled=True)
    state_in = back[:, :share].reshape(heads, width, width)
    adjoint_in = back[:, share:].reshape(heads, width, width)
    grad_query = query_part + before[..., None] * product("thb,hab->tha", grad_blk, state_in)
    grad_key = key_part + after[..., None] * product("shb,hab->sha", value_blk, adjoint_in)
    grad_value = value_part + after[..., None] * product("sha,hab->shb", key_blk, adjoint_in)
    flat = lambda x: x.astype(jnp.bfloat16).reshape(length, heads * width)
    return (flat(grad_query), flat(grad_key), flat(grad_value))


def solution(mesh):
    placed = tuple(P(SEQ_EXP, None) for _ in range(5))
    return jax.shard_map(
        body,
        mesh=mesh,
        in_specs=placed,
        out_specs=(P(SEQ_EXP, None), P(SEQ_EXP, None), P(SEQ_EXP, None)),
        check_vma=False,
    )
```

```python
import jax
import jax.numpy as jnp
from jax import lax
from jax.sharding import PartitionSpec as P

BLOCK = 128
SEQ_EXP = ("seq", "exp")


def widen(array):
    return array.astype(jnp.float32)


def halves(array):
    high = array.astype(jnp.bfloat16)
    low = (array - widen(high)).astype(jnp.bfloat16)
    return (high, low)


def product(form, first_op, second_op):
    return jnp.einsum(form, first_op, second_op, preferred_element_type=jnp.float32)


def split_left(form, wide_op, narrow_op):
    high, low = halves(wide_op)
    return product(form, high, narrow_op) + product(form, low, narrow_op)


def split_right(form, narrow_op, wide_op):
    high, low = halves(wide_op)
    return product(form, narrow_op, high) + product(form, narrow_op, low)


def link(earlier, later):
    return (earlier[0] + later[0], jnp.exp(later[0])[:, None, None] * earlier[1] + later[1])


def pieces_of(array):
    high = array.astype(jnp.bfloat16)
    rest = array - widen(high)
    mid = rest.astype(jnp.bfloat16)
    low = (rest - widen(mid)).astype(jnp.bfloat16)
    return high, mid, low


def carried_both(dev_log, dev_state, dev_adjoint, axis, riders):
    peers = lax.axis_size(axis)
    here = lax.axis_index(axis)
    heads, width = dev_state.shape[0], dev_state.shape[2]
    share = heads * width // peers
    spare = 16
    logs = jnp.zeros((spare, width), jnp.bfloat16)
    for i, part in enumerate(pieces_of(dev_log)):
        logs = logs.at[i * heads : (i + 1) * heads, :].set(
            jnp.broadcast_to(part[:, None], (heads, width))
        )
    payload = jnp.concatenate(
        [
            dev_state.astype(jnp.bfloat16).reshape(peers, share, width),
            dev_adjoint.astype(jnp.bfloat16).reshape(peers, share, width),
            jnp.broadcast_to(logs[None], (peers, spare, width)),
        ],
        axis=1,
    )
    got = lax.all_to_all(payload, axis, 0, 0, tiled=True)
    got, riders = lax.optimization_barrier((got, riders))
    head = (here * share) // width
    pick = (lax.broadcasted_iota(jnp.int32, (heads,), 0) == head).astype(jnp.float32)
    log_rows = widen(got[:, 2 * share : 2 * share + 3 * heads, 0]).reshape(peers, 3, heads)
    totals = jnp.sum(log_rows[:, 0] * pick[None, :], axis=1)
    totals = totals + jnp.sum(log_rows[:, 1] * pick[None, :], axis=1)
    totals = totals + jnp.sum(log_rows[:, 2] * pick[None, :], axis=1)
    dst = lax.broadcasted_iota(jnp.int32, (peers, peers, peers), 0)
    src = lax.broadcasted_iota(jnp.int32, (peers, peers, peers), 1)
    mid = lax.broadcasted_iota(jnp.int32, (peers, peers, peers), 2)
    between_fwd = (src < mid) & (mid < dst)
    between_bwd = (dst < mid) & (mid < src)
    log_fwd = jnp.sum(jnp.where(between_fwd, totals[None, None, :], 0.0), axis=2)
    log_bwd = jnp.sum(jnp.where(between_bwd, totals[None, None, :], 0.0), axis=2)
    dst2 = lax.broadcasted_iota(jnp.int32, (peers, peers), 0)
    src2 = lax.broadcasted_iota(jnp.int32, (peers, peers), 1)
    w_fwd = jnp.where(src2 < dst2, jnp.exp(jnp.where(src2 < dst2, log_fwd, 0.0)), 0.0)
    w_bwd = jnp.where(src2 > dst2, jnp.exp(jnp.where(src2 > dst2, log_bwd, 0.0)), 0.0)
    highest = lax.Precision.HIGHEST
    state_rows = jnp.einsum("di,irc->drc", w_fwd, widen(got[:, :share]), precision=highest)
    adjoint_rows = jnp.einsum(
        "di,irc->drc", w_bwd, widen(got[:, share : 2 * share]), precision=highest
    )
    back = lax.all_to_all(
        jnp.concatenate([state_rows, adjoint_rows], axis=1).astype(jnp.bfloat16),
        axis,
        0,
        0,
        tiled=True,
    )
    start_state = widen(back[:, :share]).reshape(heads, width, width)
    start_adjoint = widen(back[:, share:]).reshape(heads, width, width)
    return start_state, start_adjoint, riders


def running_sum(decay_blk):
    length = decay_blk.shape[1]
    lower = (
        lax.broadcasted_iota(jnp.int32, (length, length), 1)
        <= lax.broadcasted_iota(jnp.int32, (length, length), 0)
    ).astype(decay_blk.dtype)
    return jnp.einsum("ts,nsh->nth", lower, decay_blk, preferred_element_type=jnp.float32)


def within_group(totals, pieces, reverse):
    blocks = totals.shape[0]
    at = lax.broadcasted_iota(jnp.int32, (blocks, blocks, blocks), 0)
    src = lax.broadcasted_iota(jnp.int32, (blocks, blocks, blocks), 1)
    mid = lax.broadcasted_iota(jnp.int32, (blocks, blocks, blocks), 2)
    between = ((at < mid) & (mid < src)) if reverse else ((src < mid) & (mid < at))
    logs = jnp.sum(jnp.where(between[..., None], totals[None, None], 0.0), axis=2)
    pos = lax.broadcasted_iota(jnp.int32, (blocks, blocks), 0)
    other = lax.broadcasted_iota(jnp.int32, (blocks, blocks), 1)
    earlier = (other > pos) if reverse else (other < pos)
    later = (other < pos) if reverse else (other > pos)
    weights = jnp.where(earlier[..., None], jnp.exp(jnp.where(earlier[..., None], logs, 0.0)), 0.0)
    seen_log = jnp.sum(jnp.where(earlier[..., None], totals[None], 0.0), axis=1)
    tail_log = jnp.sum(jnp.where(later[..., None], totals[None], 0.0), axis=1)
    highest = lax.Precision.HIGHEST
    seen = jnp.einsum("ijh,jhab->ihab", weights, pieces, precision=highest)
    whole = jnp.einsum("jh,jhab->hab", jnp.exp(tail_log), pieces, precision=highest)
    return seen, seen_log, whole, jnp.sum(totals, axis=0)


def local_block(queries, keys, values, out_grad, log_decay):
    length = queries.shape[0]
    heads = log_decay.shape[1]
    width = queries.shape[1] // heads
    query_blk = queries.reshape(length, heads, width)
    key_blk = keys.reshape(length, heads, width)
    value_blk = values.reshape(length, heads, width)
    grad_blk = out_grad.reshape(length, heads, width)
    cumul = running_sum(log_decay[None])[0]
    total = cumul[-1]
    after = jnp.exp(total[None, :] - cumul)
    before = jnp.exp(cumul)
    contrib = split_left("sha,shb->hab", after[..., None] * widen(key_blk), value_blk)
    update = split_left("tha,thb->hab", before[..., None] * widen(query_blk), grad_blk)
    return (query_blk, key_blk, value_blk, grad_blk, cumul, after, before, contrib, update)


def intra(query_blk, key_blk, value_blk, grad_blk, cumul):
    length = cumul.shape[0]
    heads_first = cumul.T
    spread = heads_first[:, :, None] - heads_first[:, None, :]
    causal = lax.broadcasted_iota(jnp.int32, (length, length), 1) <= lax.broadcasted_iota(
        jnp.int32, (length, length), 0
    )
    weights = jnp.where(causal[None], jnp.exp(jnp.where(causal[None], spread, 0.0)), 0.0)
    grad_scores = product("thd,shd->hts", grad_blk, value_blk)
    key_scores = product("thd,shd->hts", query_blk, key_blk)
    first = (weights * grad_scores).astype(jnp.bfloat16)
    second = (weights * key_scores).astype(jnp.bfloat16)
    query_part = product("hts,shd->thd", first, key_blk)
    key_part = product("hts,thd->shd", first, query_blk)
    value_part = product("hts,thd->shd", second, grad_blk)
    return query_part, key_part, value_part


def body(queries, keys, values, out_grad, log_decay):
    peers = lax.axis_size("exp")
    length = queries.shape[0]
    heads = log_decay.shape[1]
    width = queries.shape[1] // heads
    group = heads // peers
    (query_blk, key_blk, value_blk, grad_blk, cumul, after, before, contrib, update) = local_block(
        queries, keys, values, out_grad, log_decay
    )
    share = group * width
    decay_rows = jnp.transpose(log_decay.reshape(length, peers, group), (1, 2, 0))
    pad_rows = 16
    decay_rows = jnp.pad(decay_rows, ((0, 0), (0, pad_rows - group), (0, 0)))
    packed = jnp.concatenate(
        [
            contrib.astype(jnp.bfloat16).reshape(peers, share, width),
            update.astype(jnp.bfloat16).reshape(peers, share, width),
            decay_rows.astype(jnp.bfloat16),
        ],
        axis=1,
    )
    got = lax.all_to_all(packed, "exp", 0, 0, tiled=True)
    contrib_g = widen(got[:, :share]).reshape(peers, group, width, width)
    update_g = widen(got[:, share : 2 * share]).reshape(peers, group, width, width)
    totals = jnp.sum(widen(got[:, 2 * share : 2 * share + group]), axis=2)
    query_part, key_part, value_part = intra(query_blk, key_blk, value_blk, grad_blk, cumul)
    totals, contrib_g, update_g, query_part, key_part, value_part = lax.optimization_barrier(
        (totals, contrib_g, update_g, query_part, key_part, value_part)
    )
    prefix, prefix_log, dev_state, dev_log = within_group(totals, contrib_g, False)
    suffix, suffix_log, dev_adjoint, unused = within_group(totals, update_g, True)
    start_state, start_adjoint, (prefix, suffix) = carried_both(
        dev_log, dev_state, dev_adjoint, "seq", (prefix, suffix)
    )
    state_prev = jnp.exp(prefix_log)[:, :, None, None] * start_state[None] + prefix
    adjoint = jnp.exp(suffix_log)[:, :, None, None] * start_adjoint[None] + suffix
    returned = jnp.concatenate(
        [
            state_prev.astype(jnp.bfloat16).reshape(peers, share, width),
            adjoint.astype(jnp.bfloat16).reshape(peers, share, width),
        ],
        axis=1,
    )
    back = lax.all_to_all(returned, "exp", 0, 0, tiled=True)
    state_in = back[:, :share].reshape(heads, width, width)
    adjoint_in = back[:, share:].reshape(heads, width, width)
    grad_query = query_part + before[..., None] * product("thb,hab->tha", grad_blk, state_in)
    grad_key = key_part + after[..., None] * product("shb,hab->sha", value_blk, adjoint_in)
    grad_value = value_part + after[..., None] * product("sha,hab->shb", key_blk, adjoint_in)
    flat = lambda x: x.astype(jnp.bfloat16).reshape(length, heads * width)
    return (flat(grad_query), flat(grad_key), flat(grad_value))


def solution(mesh):
    placed = tuple(P(SEQ_EXP, None) for _ in range(5))
    return jax.shard_map(
        body,
        mesh=mesh,
        in_specs=placed,
        out_specs=(P(SEQ_EXP, None), P(SEQ_EXP, None), P(SEQ_EXP, None)),
        check_vma=False,
    )
```

```python
import jax
import jax.numpy as jnp
from jax import lax
from jax.sharding import PartitionSpec as P
from jax.experimental import pallas as pl

BLOCK = 128
SEQ_EXP = ("seq", "exp")


def widen(array):
    return array.astype(jnp.float32)


def halves(array):
    high = array.astype(jnp.bfloat16)
    low = (array - widen(high)).astype(jnp.bfloat16)
    return (high, low)


def product(form, first_op, second_op):
    return jnp.einsum(form, first_op, second_op, preferred_element_type=jnp.float32)


def split_left(form, wide_op, narrow_op):
    high, low = halves(wide_op)
    return product(form, high, narrow_op) + product(form, low, narrow_op)


def split_right(form, narrow_op, wide_op):
    high, low = halves(wide_op)
    return product(form, narrow_op, high) + product(form, narrow_op, low)


def link(earlier, later):
    return (earlier[0] + later[0], jnp.exp(later[0])[:, None, None] * earlier[1] + later[1])


def pieces_of(array):
    high = array.astype(jnp.bfloat16)
    rest = array - widen(high)
    mid = rest.astype(jnp.bfloat16)
    low = (rest - widen(mid)).astype(jnp.bfloat16)
    return high, mid, low


def carried_both(dev_log, dev_state, dev_adjoint, axis, riders):
    peers = lax.axis_size(axis)
    here = lax.axis_index(axis)
    heads, width = dev_state.shape[0], dev_state.shape[2]
    share = heads * width // peers
    spare = 16
    logs = jnp.zeros((spare, width), jnp.bfloat16)
    for i, part in enumerate(pieces_of(dev_log)):
        logs = logs.at[i * heads : (i + 1) * heads, :].set(
            jnp.broadcast_to(part[:, None], (heads, width))
        )
    payload = jnp.concatenate(
        [
            dev_state.astype(jnp.bfloat16).reshape(peers, share, width),
            dev_adjoint.astype(jnp.bfloat16).reshape(peers, share, width),
            jnp.broadcast_to(logs[None], (peers, spare, width)),
        ],
        axis=1,
    )
    got = lax.all_to_all(payload, axis, 0, 0, tiled=True)
    got, riders = lax.optimization_barrier((got, riders))
    head = (here * share) // width
    pick = (lax.broadcasted_iota(jnp.int32, (heads,), 0) == head).astype(jnp.float32)
    log_rows = widen(got[:, 2 * share : 2 * share + 3 * heads, 0]).reshape(peers, 3, heads)
    totals = jnp.sum(log_rows[:, 0] * pick[None, :], axis=1)
    totals = totals + jnp.sum(log_rows[:, 1] * pick[None, :], axis=1)
    totals = totals + jnp.sum(log_rows[:, 2] * pick[None, :], axis=1)
    dst = lax.broadcasted_iota(jnp.int32, (peers, peers, peers), 0)
    src = lax.broadcasted_iota(jnp.int32, (peers, peers, peers), 1)
    mid = lax.broadcasted_iota(jnp.int32, (peers, peers, peers), 2)
    between_fwd = (src < mid) & (mid < dst)
    between_bwd = (dst < mid) & (mid < src)
    log_fwd = jnp.sum(jnp.where(between_fwd, totals[None, None, :], 0.0), axis=2)
    log_bwd = jnp.sum(jnp.where(between_bwd, totals[None, None, :], 0.0), axis=2)
    dst2 = lax.broadcasted_iota(jnp.int32, (peers, peers), 0)
    src2 = lax.broadcasted_iota(jnp.int32, (peers, peers), 1)
    w_fwd = jnp.where(src2 < dst2, jnp.exp(jnp.where(src2 < dst2, log_fwd, 0.0)), 0.0)
    w_bwd = jnp.where(src2 > dst2, jnp.exp(jnp.where(src2 > dst2, log_bwd, 0.0)), 0.0)
    highest = lax.Precision.HIGHEST
    state_rows = jnp.einsum("di,irc->drc", w_fwd, widen(got[:, :share]), precision=highest)
    adjoint_rows = jnp.einsum(
        "di,irc->drc", w_bwd, widen(got[:, share : 2 * share]), precision=highest
    )
    back = lax.all_to_all(
        jnp.concatenate([state_rows, adjoint_rows], axis=1).astype(jnp.bfloat16),
        axis,
        0,
        0,
        tiled=True,
    )
    start_state = widen(back[:, :share]).reshape(heads, width, width)
    start_adjoint = widen(back[:, share:]).reshape(heads, width, width)
    return start_state, start_adjoint, riders


def running_sum(decay_blk):
    length = decay_blk.shape[1]
    lower = (
        lax.broadcasted_iota(jnp.int32, (length, length), 1)
        <= lax.broadcasted_iota(jnp.int32, (length, length), 0)
    ).astype(decay_blk.dtype)
    return jnp.einsum("ts,nsh->nth", lower, decay_blk, preferred_element_type=jnp.float32)


def within_group(totals, pieces, reverse):
    blocks = totals.shape[0]
    at = lax.broadcasted_iota(jnp.int32, (blocks, blocks, blocks), 0)
    src = lax.broadcasted_iota(jnp.int32, (blocks, blocks, blocks), 1)
    mid = lax.broadcasted_iota(jnp.int32, (blocks, blocks, blocks), 2)
    between = ((at < mid) & (mid < src)) if reverse else ((src < mid) & (mid < at))
    logs = jnp.sum(jnp.where(between[..., None], totals[None, None], 0.0), axis=2)
    pos = lax.broadcasted_iota(jnp.int32, (blocks, blocks), 0)
    other = lax.broadcasted_iota(jnp.int32, (blocks, blocks), 1)
    earlier = (other > pos) if reverse else (other < pos)
    later = (other < pos) if reverse else (other > pos)
    weights = jnp.where(earlier[..., None], jnp.exp(jnp.where(earlier[..., None], logs, 0.0)), 0.0)
    seen_log = jnp.sum(jnp.where(earlier[..., None], totals[None], 0.0), axis=1)
    tail_log = jnp.sum(jnp.where(later[..., None], totals[None], 0.0), axis=1)
    highest = lax.Precision.HIGHEST
    seen = jnp.einsum("ijh,jhab->ihab", weights, pieces, precision=highest)
    whole = jnp.einsum("jh,jhab->hab", jnp.exp(tail_log), pieces, precision=highest)
    return seen, seen_log, whole, jnp.sum(totals, axis=0)


def local_block(queries, keys, values, out_grad, log_decay):
    length = queries.shape[0]
    heads = log_decay.shape[1]
    width = queries.shape[1] // heads
    query_blk = queries.reshape(length, heads, width)
    key_blk = keys.reshape(length, heads, width)
    value_blk = values.reshape(length, heads, width)
    grad_blk = out_grad.reshape(length, heads, width)
    cumul = running_sum(log_decay[None])[0]
    total = cumul[-1]
    after = jnp.exp(total[None, :] - cumul)
    before = jnp.exp(cumul)
    contrib = split_left("sha,shb->hab", after[..., None] * widen(key_blk), value_blk)
    update = split_left("tha,thb->hab", before[..., None] * widen(query_blk), grad_blk)
    return (query_blk, key_blk, value_blk, grad_blk, cumul, after, before, contrib, update)


def intra(query_blk, key_blk, value_blk, grad_blk, cumul):
    length = cumul.shape[0]
    heads_first = cumul.T
    spread = heads_first[:, :, None] - heads_first[:, None, :]
    causal = lax.broadcasted_iota(jnp.int32, (length, length), 1) <= lax.broadcasted_iota(
        jnp.int32, (length, length), 0
    )
    weights = jnp.where(causal[None], jnp.exp(jnp.where(causal[None], spread, 0.0)), 0.0)
    grad_scores = product("thd,shd->hts", grad_blk, value_blk)
    key_scores = product("thd,shd->hts", query_blk, key_blk)
    first = (weights * grad_scores).astype(jnp.bfloat16)
    second = (weights * key_scores).astype(jnp.bfloat16)
    query_part = product("hts,shd->htd", first, key_blk)
    key_part = product("hts,thd->hsd", first, query_blk)
    value_part = product("hts,thd->hsd", second, grad_blk)
    return query_part, key_part, value_part


def finish_kernel(
    grad_ref, value_ref, key_ref, state_ref, adjoint_ref, qp_ref, kp_ref, vp_ref, before_ref,
    after_ref, gq_ref, gk_ref, gv_ref,
):
    group, width = state_ref.shape[0], state_ref.shape[2]
    back = (((1,), (1,)), ((), ()))
    for i in range(group):
        cols = slice(i * width, (i + 1) * width)
        grad = grad_ref[:, cols]
        value = value_ref[:, cols]
        key = key_ref[:, cols]
        state = state_ref[i]
        adjoint = adjoint_ref[i]
        with_state = lax.dot_general(grad, state, back, preferred_element_type=jnp.float32)
        with_adjoint_v = lax.dot_general(value, adjoint, back, preferred_element_type=jnp.float32)
        with_adjoint_k = jnp.dot(key, adjoint, preferred_element_type=jnp.float32)
        gq_ref[:, cols] = (qp_ref[i] + before_ref[i] * with_state).astype(gq_ref.dtype)
        gk_ref[:, cols] = (kp_ref[i] + after_ref[i] * with_adjoint_v).astype(gk_ref.dtype)
        gv_ref[:, cols] = (vp_ref[i] + after_ref[i] * with_adjoint_k).astype(gv_ref.dtype)


def finish_call(out_grad, values, keys, state_in, adjoint_in, qp, kp, vp, before_t, after_t):
    length, columns = out_grad.shape
    heads, width = state_in.shape[0], state_in.shape[2]
    group = 4
    steps = heads // group
    flat_spec = pl.BlockSpec((length, group * width), lambda h: (0, h))
    head_spec = pl.BlockSpec((group, width, width), lambda h: (h, 0, 0))
    part_spec = pl.BlockSpec((group, length, width), lambda h: (h, 0, 0))
    scale_spec = pl.BlockSpec((group, length, 1), lambda h: (h, 0, 0))
    out = jax.ShapeDtypeStruct((length, columns), jnp.bfloat16)
    return pl.pallas_call(
        finish_kernel,
        grid=(steps,),
        in_specs=[flat_spec, flat_spec, flat_spec, head_spec, head_spec, part_spec, part_spec,
                  part_spec, scale_spec, scale_spec],
        out_specs=[flat_spec, flat_spec, flat_spec],
        out_shape=[out, out, out],
    )(out_grad, values, keys, state_in, adjoint_in, qp, kp, vp, before_t, after_t)


def body(queries, keys, values, out_grad, log_decay):
    peers = lax.axis_size("exp")
    length = queries.shape[0]
    heads = log_decay.shape[1]
    width = queries.shape[1] // heads
    group = heads // peers
    (query_blk, key_blk, value_blk, grad_blk, cumul, after, before, contrib, update) = local_block(
        queries, keys, values, out_grad, log_decay
    )
    share = group * width
    decay_rows = jnp.transpose(log_decay.reshape(length, peers, group), (1, 2, 0))
    pad_rows = 16
    decay_rows = jnp.pad(decay_rows, ((0, 0), (0, pad_rows - group), (0, 0)))
    packed = jnp.concatenate(
        [
            contrib.astype(jnp.bfloat16).reshape(peers, share, width),
            update.astype(jnp.bfloat16).reshape(peers, share, width),
            decay_rows.astype(jnp.bfloat16),
        ],
        axis=1,
    )
    got = lax.all_to_all(packed, "exp", 0, 0, tiled=True)
    contrib_g = widen(got[:, :share]).reshape(peers, group, width, width)
    update_g = widen(got[:, share : 2 * share]).reshape(peers, group, width, width)
    totals = jnp.sum(widen(got[:, 2 * share : 2 * share + group]), axis=2)
    query_part, key_part, value_part = intra(query_blk, key_blk, value_blk, grad_blk, cumul)
    totals, contrib_g, update_g, query_part, key_part, value_part = lax.optimization_barrier(
        (totals, contrib_g, update_g, query_part, key_part, value_part)
    )
    prefix, prefix_log, dev_state, dev_log = within_group(totals, contrib_g, False)
    suffix, suffix_log, dev_adjoint, unused = within_group(totals, update_g, True)
    start_state, start_adjoint, (prefix, suffix) = carried_both(
        dev_log, dev_state, dev_adjoint, "seq", (prefix, suffix)
    )
    state_prev = jnp.exp(prefix_log)[:, :, None, None] * start_state[None] + prefix
    adjoint = jnp.exp(suffix_log)[:, :, None, None] * start_adjoint[None] + suffix
    returned = jnp.concatenate(
        [
            state_prev.astype(jnp.bfloat16).reshape(peers, share, width),
            adjoint.astype(jnp.bfloat16).reshape(peers, share, width),
        ],
        axis=1,
    )
    back = lax.all_to_all(returned, "exp", 0, 0, tiled=True)
    state_in = back[:, :share].reshape(heads, width, width)
    adjoint_in = back[:, share:].reshape(heads, width, width)
    grad_query, grad_key, grad_value = finish_call(
        out_grad, values, keys, state_in, adjoint_in, query_part, key_part, value_part,
        before.T[:, :, None], after.T[:, :, None],
    )
    return (grad_query, grad_key, grad_value)


def solution(mesh):
    placed = tuple(P(SEQ_EXP, None) for _ in range(5))
    return jax.shard_map(
        body,
        mesh=mesh,
        in_specs=placed,
        out_specs=(P(SEQ_EXP, None), P(SEQ_EXP, None), P(SEQ_EXP, None)),
        check_vma=False,
    )
```

```python
import jax
import jax.numpy as jnp
from jax import lax
from jax.sharding import PartitionSpec as P
from jax.experimental import pallas as pl

BLOCK = 128
SEQ_EXP = ("seq", "exp")


def widen(array):
    return array.astype(jnp.float32)


def halves(array):
    high = array.astype(jnp.bfloat16)
    low = (array - widen(high)).astype(jnp.bfloat16)
    return (high, low)


def product(form, first_op, second_op):
    return jnp.einsum(form, first_op, second_op, preferred_element_type=jnp.float32)


def split_left(form, wide_op, narrow_op):
    high, low = halves(wide_op)
    return product(form, high, narrow_op) + product(form, low, narrow_op)


def split_right(form, narrow_op, wide_op):
    high, low = halves(wide_op)
    return product(form, narrow_op, high) + product(form, narrow_op, low)


def link(earlier, later):
    return (earlier[0] + later[0], jnp.exp(later[0])[:, None, None] * earlier[1] + later[1])


def pieces_of(array):
    high = array.astype(jnp.bfloat16)
    rest = array - widen(high)
    mid = rest.astype(jnp.bfloat16)
    low = (rest - widen(mid)).astype(jnp.bfloat16)
    return high, mid, low


def carried_both(dev_log, dev_state, dev_adjoint, axis, riders):
    peers = lax.axis_size(axis)
    here = lax.axis_index(axis)
    heads, width = dev_state.shape[0], dev_state.shape[2]
    share = heads * width // peers
    spare = 16
    logs = jnp.zeros((spare, width), jnp.bfloat16)
    for i, part in enumerate(pieces_of(dev_log)):
        logs = logs.at[i * heads : (i + 1) * heads, :].set(
            jnp.broadcast_to(part[:, None], (heads, width))
        )
    payload = jnp.concatenate(
        [
            dev_state.astype(jnp.bfloat16).reshape(peers, share, width),
            dev_adjoint.astype(jnp.bfloat16).reshape(peers, share, width),
            jnp.broadcast_to(logs[None], (peers, spare, width)),
        ],
        axis=1,
    )
    got = lax.all_to_all(payload, axis, 0, 0, tiled=True)
    got, riders = lax.optimization_barrier((got, riders))
    head = (here * share) // width
    pick = (lax.broadcasted_iota(jnp.int32, (heads,), 0) == head).astype(jnp.float32)
    log_rows = widen(got[:, 2 * share : 2 * share + 3 * heads, 0]).reshape(peers, 3, heads)
    totals = jnp.sum(log_rows[:, 0] * pick[None, :], axis=1)
    totals = totals + jnp.sum(log_rows[:, 1] * pick[None, :], axis=1)
    totals = totals + jnp.sum(log_rows[:, 2] * pick[None, :], axis=1)
    dst = lax.broadcasted_iota(jnp.int32, (peers, peers, peers), 0)
    src = lax.broadcasted_iota(jnp.int32, (peers, peers, peers), 1)
    mid = lax.broadcasted_iota(jnp.int32, (peers, peers, peers), 2)
    between_fwd = (src < mid) & (mid < dst)
    between_bwd = (dst < mid) & (mid < src)
    log_fwd = jnp.sum(jnp.where(between_fwd, totals[None, None, :], 0.0), axis=2)
    log_bwd = jnp.sum(jnp.where(between_bwd, totals[None, None, :], 0.0), axis=2)
    dst2 = lax.broadcasted_iota(jnp.int32, (peers, peers), 0)
    src2 = lax.broadcasted_iota(jnp.int32, (peers, peers), 1)
    w_fwd = jnp.where(src2 < dst2, jnp.exp(jnp.where(src2 < dst2, log_fwd, 0.0)), 0.0)
    w_bwd = jnp.where(src2 > dst2, jnp.exp(jnp.where(src2 > dst2, log_bwd, 0.0)), 0.0)
    highest = lax.Precision.HIGHEST
    state_rows = jnp.einsum("di,irc->drc", w_fwd, widen(got[:, :share]), precision=highest)
    adjoint_rows = jnp.einsum(
        "di,irc->drc", w_bwd, widen(got[:, share : 2 * share]), precision=highest
    )
    back = lax.all_to_all(
        jnp.concatenate([state_rows, adjoint_rows], axis=1), axis, 0, 0, tiled=True
    )
    start_state = back[:, :share].reshape(heads, width, width)
    start_adjoint = back[:, share:].reshape(heads, width, width)
    return start_state, start_adjoint, riders


def running_sum(decay_blk):
    length = decay_blk.shape[1]
    lower = (
        lax.broadcasted_iota(jnp.int32, (length, length), 1)
        <= lax.broadcasted_iota(jnp.int32, (length, length), 0)
    ).astype(decay_blk.dtype)
    return jnp.einsum("ts,nsh->nth", lower, decay_blk, preferred_element_type=jnp.float32)


def within_group(totals, pieces, reverse):
    blocks = totals.shape[0]
    at = lax.broadcasted_iota(jnp.int32, (blocks, blocks, blocks), 0)
    src = lax.broadcasted_iota(jnp.int32, (blocks, blocks, blocks), 1)
    mid = lax.broadcasted_iota(jnp.int32, (blocks, blocks, blocks), 2)
    between = ((at < mid) & (mid < src)) if reverse else ((src < mid) & (mid < at))
    logs = jnp.sum(jnp.where(between[..., None], totals[None, None], 0.0), axis=2)
    pos = lax.broadcasted_iota(jnp.int32, (blocks, blocks), 0)
    other = lax.broadcasted_iota(jnp.int32, (blocks, blocks), 1)
    earlier = (other > pos) if reverse else (other < pos)
    later = (other < pos) if reverse else (other > pos)
    weights = jnp.where(earlier[..., None], jnp.exp(jnp.where(earlier[..., None], logs, 0.0)), 0.0)
    seen_log = jnp.sum(jnp.where(earlier[..., None], totals[None], 0.0), axis=1)
    tail_log = jnp.sum(jnp.where(later[..., None], totals[None], 0.0), axis=1)
    highest = lax.Precision.HIGHEST
    seen = jnp.einsum("ijh,jhab->ihab", weights, pieces, precision=highest)
    whole = jnp.einsum("jh,jhab->hab", jnp.exp(tail_log), pieces, precision=highest)
    return seen, seen_log, whole, jnp.sum(totals, axis=0)


def local_block(queries, keys, values, out_grad, log_decay):
    length = queries.shape[0]
    heads = log_decay.shape[1]
    width = queries.shape[1] // heads
    query_blk = queries.reshape(length, heads, width)
    key_blk = keys.reshape(length, heads, width)
    value_blk = values.reshape(length, heads, width)
    grad_blk = out_grad.reshape(length, heads, width)
    cumul = running_sum(log_decay[None])[0]
    total = cumul[-1]
    after = jnp.exp(total[None, :] - cumul)
    before = jnp.exp(cumul)
    contrib = split_left("sha,shb->hab", after[..., None] * widen(key_blk), value_blk)
    update = split_left("tha,thb->hab", before[..., None] * widen(query_blk), grad_blk)
    return (query_blk, key_blk, value_blk, grad_blk, cumul, after, before, contrib, update)


def intra(query_blk, key_blk, value_blk, grad_blk, cumul):
    length = cumul.shape[0]
    heads_first = cumul.T
    spread = heads_first[:, :, None] - heads_first[:, None, :]
    causal = lax.broadcasted_iota(jnp.int32, (length, length), 1) <= lax.broadcasted_iota(
        jnp.int32, (length, length), 0
    )
    weights = jnp.where(causal[None], jnp.exp(jnp.where(causal[None], spread, 0.0)), 0.0)
    grad_scores = product("thd,shd->hts", grad_blk, value_blk)
    key_scores = product("thd,shd->hts", query_blk, key_blk)
    first = (weights * grad_scores).astype(jnp.bfloat16)
    second = (weights * key_scores).astype(jnp.bfloat16)
    query_part = product("hts,shd->htd", first, key_blk)
    key_part = product("hts,thd->hsd", first, query_blk)
    value_part = product("hts,thd->hsd", second, grad_blk)
    return query_part, key_part, value_part


def finish_kernel(
    grad_ref, value_ref, key_ref, state_ref, adjoint_ref, qp_ref, kp_ref, vp_ref, before_ref,
    after_ref, gq_ref, gk_ref, gv_ref,
):
    group, width = state_ref.shape[0], state_ref.shape[2]
    back = (((1,), (1,)), ((), ()))
    for i in range(group):
        cols = slice(i * width, (i + 1) * width)
        grad = grad_ref[:, cols]
        value = value_ref[:, cols]
        key = key_ref[:, cols]
        state = state_ref[i]
        adjoint = adjoint_ref[i]
        with_state = lax.dot_general(grad, state, back, preferred_element_type=jnp.float32)
        with_adjoint_v = lax.dot_general(value, adjoint, back, preferred_element_type=jnp.float32)
        with_adjoint_k = jnp.dot(key, adjoint, preferred_element_type=jnp.float32)
        gq_ref[:, cols] = (qp_ref[i] + before_ref[i] * with_state).astype(gq_ref.dtype)
        gk_ref[:, cols] = (kp_ref[i] + after_ref[i] * with_adjoint_v).astype(gk_ref.dtype)
        gv_ref[:, cols] = (vp_ref[i] + after_ref[i] * with_adjoint_k).astype(gv_ref.dtype)


def finish_call(out_grad, values, keys, state_in, adjoint_in, qp, kp, vp, before_t, after_t):
    length, columns = out_grad.shape
    heads, width = state_in.shape[0], state_in.shape[2]
    group = 4
    steps = heads // group
    flat_spec = pl.BlockSpec((length, group * width), lambda h: (0, h))
    head_spec = pl.BlockSpec((group, width, width), lambda h: (h, 0, 0))
    part_spec = pl.BlockSpec((group, length, width), lambda h: (h, 0, 0))
    scale_spec = pl.BlockSpec((group, length, 1), lambda h: (h, 0, 0))
    out = jax.ShapeDtypeStruct((length, columns), jnp.bfloat16)
    return pl.pallas_call(
        finish_kernel,
        grid=(steps,),
        in_specs=[flat_spec, flat_spec, flat_spec, head_spec, head_spec, part_spec, part_spec,
                  part_spec, scale_spec, scale_spec],
        out_specs=[flat_spec, flat_spec, flat_spec],
        out_shape=[out, out, out],
    )(out_grad, values, keys, state_in, adjoint_in, qp, kp, vp, before_t, after_t)


def body(queries, keys, values, out_grad, log_decay):
    peers = lax.axis_size("exp")
    length = queries.shape[0]
    heads = log_decay.shape[1]
    width = queries.shape[1] // heads
    group = heads // peers
    (query_blk, key_blk, value_blk, grad_blk, cumul, after, before, contrib, update) = local_block(
        queries, keys, values, out_grad, log_decay
    )
    share = group * width
    decay_rows = jnp.transpose(log_decay.reshape(length, peers, group), (1, 2, 0))
    pad_rows = 16
    decay_rows = jnp.pad(decay_rows, ((0, 0), (0, pad_rows - group), (0, 0)))
    packed = jnp.concatenate(
        [
            contrib.astype(jnp.bfloat16).reshape(peers, share, width),
            update.astype(jnp.bfloat16).reshape(peers, share, width),
            decay_rows.astype(jnp.bfloat16),
        ],
        axis=1,
    )
    got = lax.all_to_all(packed, "exp", 0, 0, tiled=True)
    contrib_g = widen(got[:, :share]).reshape(peers, group, width, width)
    update_g = widen(got[:, share : 2 * share]).reshape(peers, group, width, width)
    totals = jnp.sum(widen(got[:, 2 * share : 2 * share + group]), axis=2)
    query_part, key_part, value_part = intra(query_blk, key_blk, value_blk, grad_blk, cumul)
    totals, contrib_g, update_g, query_part, key_part, value_part = lax.optimization_barrier(
        (totals, contrib_g, update_g, query_part, key_part, value_part)
    )
    prefix, prefix_log, dev_state, dev_log = within_group(totals, contrib_g, False)
    suffix, suffix_log, dev_adjoint, unused = within_group(totals, update_g, True)
    start_state, start_adjoint, (prefix, suffix) = carried_both(
        dev_log, dev_state, dev_adjoint, "seq", (prefix, suffix)
    )
    state_prev = jnp.exp(prefix_log)[:, :, None, None] * start_state[None] + prefix
    adjoint = jnp.exp(suffix_log)[:, :, None, None] * start_adjoint[None] + suffix
    returned = jnp.concatenate(
        [
            state_prev.astype(jnp.bfloat16).reshape(peers, share, width),
            adjoint.astype(jnp.bfloat16).reshape(peers, share, width),
        ],
        axis=1,
    )
    back = lax.all_to_all(returned, "exp", 0, 0, tiled=True)
    state_in = back[:, :share].reshape(heads, width, width)
    adjoint_in = back[:, share:].reshape(heads, width, width)
    grad_query, grad_key, grad_value = finish_call(
        out_grad, values, keys, state_in, adjoint_in, query_part, key_part, value_part,
        before.T[:, :, None], after.T[:, :, None],
    )
    return (grad_query, grad_key, grad_value)


def solution(mesh):
    placed = tuple(P(SEQ_EXP, None) for _ in range(5))
    return jax.shard_map(
        body,
        mesh=mesh,
        in_specs=placed,
        out_specs=(P(SEQ_EXP, None), P(SEQ_EXP, None), P(SEQ_EXP, None)),
        check_vma=False,
    )
```

```python
import jax
import jax.numpy as jnp
from jax import lax
from jax.sharding import PartitionSpec as P
from jax.experimental import pallas as pl

BLOCK = 128
SEQ_EXP = ("seq", "exp")


def widen(array):
    return array.astype(jnp.float32)


def halves(array):
    high = array.astype(jnp.bfloat16)
    low = (array - widen(high)).astype(jnp.bfloat16)
    return (high, low)


def product(form, first_op, second_op):
    return jnp.einsum(form, first_op, second_op, preferred_element_type=jnp.float32)


def split_left(form, wide_op, narrow_op):
    high, low = halves(wide_op)
    return product(form, high, narrow_op) + product(form, low, narrow_op)


def split_right(form, narrow_op, wide_op):
    high, low = halves(wide_op)
    return product(form, narrow_op, high) + product(form, narrow_op, low)


def link(earlier, later):
    return (earlier[0] + later[0], jnp.exp(later[0])[:, None, None] * earlier[1] + later[1])


def pieces_of(array):
    high = array.astype(jnp.bfloat16)
    rest = array - widen(high)
    mid = rest.astype(jnp.bfloat16)
    low = (rest - widen(mid)).astype(jnp.bfloat16)
    return high, mid, low


def carried_both(dev_log, dev_state, dev_adjoint, axis, riders):
    peers = lax.axis_size(axis)
    here = lax.axis_index(axis)
    heads, width = dev_state.shape[0], dev_state.shape[2]
    share = heads * width // peers
    spare = 16
    logs = jnp.zeros((spare, width), jnp.bfloat16)
    for i, part in enumerate(pieces_of(dev_log)):
        logs = logs.at[i * heads : (i + 1) * heads, :].set(
            jnp.broadcast_to(part[:, None], (heads, width))
        )
    payload = jnp.concatenate(
        [
            dev_state.astype(jnp.bfloat16).reshape(peers, share, width),
            dev_adjoint.astype(jnp.bfloat16).reshape(peers, share, width),
            jnp.broadcast_to(logs[None], (peers, spare, width)),
        ],
        axis=1,
    )
    got = lax.all_to_all(payload, axis, 0, 0, tiled=True)
    got, riders = lax.optimization_barrier((got, riders))
    head = (here * share) // width
    pick = (lax.broadcasted_iota(jnp.int32, (heads,), 0) == head).astype(jnp.float32)
    log_rows = widen(got[:, 2 * share : 2 * share + 3 * heads, 0]).reshape(peers, 3, heads)
    totals = jnp.sum(log_rows[:, 0] * pick[None, :], axis=1)
    totals = totals + jnp.sum(log_rows[:, 1] * pick[None, :], axis=1)
    totals = totals + jnp.sum(log_rows[:, 2] * pick[None, :], axis=1)
    dst = lax.broadcasted_iota(jnp.int32, (peers, peers, peers), 0)
    src = lax.broadcasted_iota(jnp.int32, (peers, peers, peers), 1)
    mid = lax.broadcasted_iota(jnp.int32, (peers, peers, peers), 2)
    between_fwd = (src < mid) & (mid < dst)
    between_bwd = (dst < mid) & (mid < src)
    log_fwd = jnp.sum(jnp.where(between_fwd, totals[None, None, :], 0.0), axis=2)
    log_bwd = jnp.sum(jnp.where(between_bwd, totals[None, None, :], 0.0), axis=2)
    dst2 = lax.broadcasted_iota(jnp.int32, (peers, peers), 0)
    src2 = lax.broadcasted_iota(jnp.int32, (peers, peers), 1)
    w_fwd = jnp.where(src2 < dst2, jnp.exp(jnp.where(src2 < dst2, log_fwd, 0.0)), 0.0)
    w_bwd = jnp.where(src2 > dst2, jnp.exp(jnp.where(src2 > dst2, log_bwd, 0.0)), 0.0)
    highest = lax.Precision.HIGHEST
    state_rows = jnp.einsum("di,irc->drc", w_fwd, widen(got[:, :share]), precision=highest)
    adjoint_rows = jnp.einsum(
        "di,irc->drc", w_bwd, widen(got[:, share : 2 * share]), precision=highest
    )
    back = lax.all_to_all(
        jnp.concatenate([state_rows, adjoint_rows], axis=1), axis, 0, 0, tiled=True
    )
    start_state = back[:, :share].reshape(heads, width, width)
    start_adjoint = back[:, share:].reshape(heads, width, width)
    return start_state, start_adjoint, riders


def running_sum(decay_blk):
    length = decay_blk.shape[1]
    lower = (
        lax.broadcasted_iota(jnp.int32, (length, length), 1)
        <= lax.broadcasted_iota(jnp.int32, (length, length), 0)
    ).astype(decay_blk.dtype)
    return jnp.einsum("ts,nsh->nth", lower, decay_blk, preferred_element_type=jnp.float32)


def within_group(totals, pieces, reverse):
    blocks = totals.shape[0]
    at = lax.broadcasted_iota(jnp.int32, (blocks, blocks, blocks), 0)
    src = lax.broadcasted_iota(jnp.int32, (blocks, blocks, blocks), 1)
    mid = lax.broadcasted_iota(jnp.int32, (blocks, blocks, blocks), 2)
    between = ((at < mid) & (mid < src)) if reverse else ((src < mid) & (mid < at))
    logs = jnp.sum(jnp.where(between[..., None], totals[None, None], 0.0), axis=2)
    pos = lax.broadcasted_iota(jnp.int32, (blocks, blocks), 0)
    other = lax.broadcasted_iota(jnp.int32, (blocks, blocks), 1)
    earlier = (other > pos) if reverse else (other < pos)
    later = (other < pos) if reverse else (other > pos)
    weights = jnp.where(earlier[..., None], jnp.exp(jnp.where(earlier[..., None], logs, 0.0)), 0.0)
    seen_log = jnp.sum(jnp.where(earlier[..., None], totals[None], 0.0), axis=1)
    tail_log = jnp.sum(jnp.where(later[..., None], totals[None], 0.0), axis=1)
    highest = lax.Precision.HIGHEST
    seen = jnp.einsum("ijh,jhab->ihab", weights, pieces, precision=highest)
    whole = jnp.einsum("jh,jhab->hab", jnp.exp(tail_log), pieces, precision=highest)
    return seen, seen_log, whole, jnp.sum(totals, axis=0)


def local_block(queries, keys, values, out_grad, log_decay):
    length = queries.shape[0]
    heads = log_decay.shape[1]
    width = queries.shape[1] // heads
    query_blk = queries.reshape(length, heads, width)
    key_blk = keys.reshape(length, heads, width)
    value_blk = values.reshape(length, heads, width)
    grad_blk = out_grad.reshape(length, heads, width)
    cumul = running_sum(log_decay[None])[0]
    total = cumul[-1]
    after = jnp.exp(total[None, :] - cumul)
    before = jnp.exp(cumul)
    return (query_blk, key_blk, value_blk, grad_blk, cumul, after, before)


def intra(query_blk, key_blk, value_blk, grad_blk, cumul):
    length = cumul.shape[0]
    heads_first = cumul.T
    spread = heads_first[:, :, None] - heads_first[:, None, :]
    causal = lax.broadcasted_iota(jnp.int32, (length, length), 1) <= lax.broadcasted_iota(
        jnp.int32, (length, length), 0
    )
    weights = jnp.where(causal[None], jnp.exp(jnp.where(causal[None], spread, 0.0)), 0.0)
    grad_scores = product("thd,shd->hts", grad_blk, value_blk)
    key_scores = product("thd,shd->hts", query_blk, key_blk)
    first = (weights * grad_scores).astype(jnp.bfloat16)
    second = (weights * key_scores).astype(jnp.bfloat16)
    query_part = product("hts,shd->htd", first, key_blk)
    key_part = product("hts,thd->hsd", first, query_blk)
    value_part = product("hts,thd->hsd", second, grad_blk)
    return query_part, key_part, value_part


def contrib_kernel(key_ref, value_ref, query_ref, grad_ref, after_ref, before_ref, out_ref):
    width = out_ref.shape[2]
    group = out_ref.shape[1] // (2 * width)
    step = pl.program_id(0)
    lanes = lax.broadcasted_iota(jnp.int32, after_ref.shape, 1)
    after_all = after_ref[...]
    before_all = before_ref[...]
    for i in range(group):
        head = step * group + i
        cols = slice(i * width, (i + 1) * width)
        after = jnp.sum(jnp.where(lanes == head, after_all, 0.0), axis=1, keepdims=True)
        before = jnp.sum(jnp.where(lanes == head, before_all, 0.0), axis=1, keepdims=True)
        for slot, scale, left_ref, right_ref in (
            (i, after, key_ref, value_ref),
            (group + i, before, query_ref, grad_ref),
        ):
            scaled = (scale * left_ref[:, cols].astype(jnp.float32)).T
            high = scaled.astype(jnp.bfloat16)
            low = (scaled - high.astype(jnp.float32)).astype(jnp.bfloat16)
            right = right_ref[:, cols]
            total = jnp.dot(high, right, preferred_element_type=jnp.float32) + jnp.dot(
                low, right, preferred_element_type=jnp.float32
            )
            out_ref[0, slot * width : (slot + 1) * width, :] = total.astype(out_ref.dtype)


def contrib_call(keys, values, queries, out_grad, after, before, peers):
    length, columns = keys.shape
    heads = after.shape[1]
    width = columns // heads
    group = heads // peers
    flat_spec = pl.BlockSpec((length, group * width), lambda t: (0, t))
    scale_spec = pl.BlockSpec((length, heads), lambda t: (0, 0))
    return pl.pallas_call(
        contrib_kernel,
        grid=(peers,),
        in_specs=[flat_spec, flat_spec, flat_spec, flat_spec, scale_spec, scale_spec],
        out_specs=pl.BlockSpec((1, 2 * group * width, width), lambda t: (t, 0, 0)),
        out_shape=jax.ShapeDtypeStruct((peers, 2 * group * width, width), jnp.bfloat16),
    )(keys, values, queries, out_grad, after, before)


def finish_kernel(
    grad_ref, value_ref, key_ref, state_ref, adjoint_ref, qp_ref, kp_ref, vp_ref, before_ref,
    after_ref, gq_ref, gk_ref, gv_ref,
):
    group, width = state_ref.shape[0], state_ref.shape[2]
    back = (((1,), (1,)), ((), ()))
    for i in range(group):
        cols = slice(i * width, (i + 1) * width)
        grad = grad_ref[:, cols]
        value = value_ref[:, cols]
        key = key_ref[:, cols]
        state = state_ref[i]
        adjoint = adjoint_ref[i]
        with_state = lax.dot_general(grad, state, back, preferred_element_type=jnp.float32)
        with_adjoint_v = lax.dot_general(value, adjoint, back, preferred_element_type=jnp.float32)
        with_adjoint_k = jnp.dot(key, adjoint, preferred_element_type=jnp.float32)
        gq_ref[:, cols] = (qp_ref[i] + before_ref[i] * with_state).astype(gq_ref.dtype)
        gk_ref[:, cols] = (kp_ref[i] + after_ref[i] * with_adjoint_v).astype(gk_ref.dtype)
        gv_ref[:, cols] = (vp_ref[i] + after_ref[i] * with_adjoint_k).astype(gv_ref.dtype)


def finish_call(out_grad, values, keys, state_in, adjoint_in, qp, kp, vp, before_t, after_t):
    length, columns = out_grad.shape
    heads, width = state_in.shape[0], state_in.shape[2]
    group = 4
    steps = heads // group
    flat_spec = pl.BlockSpec((length, group * width), lambda h: (0, h))
    head_spec = pl.BlockSpec((group, width, width), lambda h: (h, 0, 0))
    part_spec = pl.BlockSpec((group, length, width), lambda h: (h, 0, 0))
    scale_spec = pl.BlockSpec((group, length, 1), lambda h: (h, 0, 0))
    out = jax.ShapeDtypeStruct((length, columns), jnp.bfloat16)
    return pl.pallas_call(
        finish_kernel,
        grid=(steps,),
        in_specs=[flat_spec, flat_spec, flat_spec, head_spec, head_spec, part_spec, part_spec,
                  part_spec, scale_spec, scale_spec],
        out_specs=[flat_spec, flat_spec, flat_spec],
        out_shape=[out, out, out],
    )(out_grad, values, keys, state_in, adjoint_in, qp, kp, vp, before_t, after_t)


def body(queries, keys, values, out_grad, log_decay):
    peers = lax.axis_size("exp")
    length = queries.shape[0]
    heads = log_decay.shape[1]
    width = queries.shape[1] // heads
    group = heads // peers
    (query_blk, key_blk, value_blk, grad_blk, cumul, after, before) = local_block(
        queries, keys, values, out_grad, log_decay
    )
    share = group * width
    decay_rows = jnp.transpose(log_decay.reshape(length, peers, group), (1, 2, 0))
    pad_rows = 16
    decay_rows = jnp.pad(decay_rows, ((0, 0), (0, pad_rows - group), (0, 0)))
    both = contrib_call(keys, values, queries, out_grad, after, before, peers)
    packed = jnp.concatenate([both, decay_rows.astype(jnp.bfloat16)], axis=1)
    got = lax.all_to_all(packed, "exp", 0, 0, tiled=True)
    contrib_g = widen(got[:, :share]).reshape(peers, group, width, width)
    update_g = widen(got[:, share : 2 * share]).reshape(peers, group, width, width)
    totals = jnp.sum(widen(got[:, 2 * share : 2 * share + group]), axis=2)
    query_part, key_part, value_part = intra(query_blk, key_blk, value_blk, grad_blk, cumul)
    totals, contrib_g, update_g, query_part, key_part, value_part = lax.optimization_barrier(
        (totals, contrib_g, update_g, query_part, key_part, value_part)
    )
    prefix, prefix_log, dev_state, dev_log = within_group(totals, contrib_g, False)
    suffix, suffix_log, dev_adjoint, unused = within_group(totals, update_g, True)
    start_state, start_adjoint, (prefix, suffix) = carried_both(
        dev_log, dev_state, dev_adjoint, "seq", (prefix, suffix)
    )
    state_prev = jnp.exp(prefix_log)[:, :, None, None] * start_state[None] + prefix
    adjoint = jnp.exp(suffix_log)[:, :, None, None] * start_adjoint[None] + suffix
    returned = jnp.concatenate(
        [
            state_prev.astype(jnp.bfloat16).reshape(peers, share, width),
            adjoint.astype(jnp.bfloat16).reshape(peers, share, width),
        ],
        axis=1,
    )
    back = lax.all_to_all(returned, "exp", 0, 0, tiled=True)
    state_in = back[:, :share].reshape(heads, width, width)
    adjoint_in = back[:, share:].reshape(heads, width, width)
    grad_query, grad_key, grad_value = finish_call(
        out_grad, values, keys, state_in, adjoint_in, query_part, key_part, value_part,
        before.T[:, :, None], after.T[:, :, None],
    )
    return (grad_query, grad_key, grad_value)


def solution(mesh):
    placed = tuple(P(SEQ_EXP, None) for _ in range(5))
    return jax.shard_map(
        body,
        mesh=mesh,
        in_specs=placed,
        out_specs=(P(SEQ_EXP, None), P(SEQ_EXP, None), P(SEQ_EXP, None)),
        check_vma=False,
    )
```

```python
import jax
import jax.numpy as jnp
from jax import lax
from jax.sharding import PartitionSpec as P
from jax.experimental import pallas as pl

BLOCK = 128
SEQ_EXP = ("seq", "exp")


def widen(array):
    return array.astype(jnp.float32)


def halves(array):
    high = array.astype(jnp.bfloat16)
    low = (array - widen(high)).astype(jnp.bfloat16)
    return (high, low)


def product(form, first_op, second_op):
    return jnp.einsum(form, first_op, second_op, preferred_element_type=jnp.float32)


def split_left(form, wide_op, narrow_op):
    high, low = halves(wide_op)
    return product(form, high, narrow_op) + product(form, low, narrow_op)


def split_right(form, narrow_op, wide_op):
    high, low = halves(wide_op)
    return product(form, narrow_op, high) + product(form, narrow_op, low)


def link(earlier, later):
    return (earlier[0] + later[0], jnp.exp(later[0])[:, None, None] * earlier[1] + later[1])


def pieces_of(array):
    high = array.astype(jnp.bfloat16)
    rest = array - widen(high)
    mid = rest.astype(jnp.bfloat16)
    low = (rest - widen(mid)).astype(jnp.bfloat16)
    return high, mid, low


def carried_both(dev_log, dev_state, dev_adjoint, axis, riders):
    peers = lax.axis_size(axis)
    here = lax.axis_index(axis)
    heads, width = dev_state.shape[0], dev_state.shape[2]
    share = heads * width // peers
    spare = 16
    logs = jnp.zeros((spare, width), jnp.bfloat16)
    for i, part in enumerate(pieces_of(dev_log)):
        logs = logs.at[i * heads : (i + 1) * heads, :].set(
            jnp.broadcast_to(part[:, None], (heads, width))
        )
    payload = jnp.concatenate(
        [
            dev_state.astype(jnp.bfloat16).reshape(peers, share, width),
            dev_adjoint.astype(jnp.bfloat16).reshape(peers, share, width),
            jnp.broadcast_to(logs[None], (peers, spare, width)),
        ],
        axis=1,
    )
    got = lax.all_to_all(payload, axis, 0, 0, tiled=True)
    got, riders = lax.optimization_barrier((got, riders))
    head = (here * share) // width
    pick = (lax.broadcasted_iota(jnp.int32, (heads,), 0) == head).astype(jnp.float32)
    log_rows = widen(got[:, 2 * share : 2 * share + 3 * heads, 0]).reshape(peers, 3, heads)
    totals = jnp.sum(log_rows[:, 0] * pick[None, :], axis=1)
    totals = totals + jnp.sum(log_rows[:, 1] * pick[None, :], axis=1)
    totals = totals + jnp.sum(log_rows[:, 2] * pick[None, :], axis=1)
    dst = lax.broadcasted_iota(jnp.int32, (peers, peers, peers), 0)
    src = lax.broadcasted_iota(jnp.int32, (peers, peers, peers), 1)
    mid = lax.broadcasted_iota(jnp.int32, (peers, peers, peers), 2)
    between_fwd = (src < mid) & (mid < dst)
    between_bwd = (dst < mid) & (mid < src)
    log_fwd = jnp.sum(jnp.where(between_fwd, totals[None, None, :], 0.0), axis=2)
    log_bwd = jnp.sum(jnp.where(between_bwd, totals[None, None, :], 0.0), axis=2)
    dst2 = lax.broadcasted_iota(jnp.int32, (peers, peers), 0)
    src2 = lax.broadcasted_iota(jnp.int32, (peers, peers), 1)
    w_fwd = jnp.where(src2 < dst2, jnp.exp(jnp.where(src2 < dst2, log_fwd, 0.0)), 0.0)
    w_bwd = jnp.where(src2 > dst2, jnp.exp(jnp.where(src2 > dst2, log_bwd, 0.0)), 0.0)
    state_rows = split_left("di,irc->drc", w_fwd, got[:, :share])
    adjoint_rows = split_left("di,irc->drc", w_bwd, got[:, share : 2 * share])
    back = lax.all_to_all(
        jnp.concatenate([state_rows, adjoint_rows], axis=1), axis, 0, 0, tiled=True
    )
    start_state = back[:, :share].reshape(heads, width, width)
    start_adjoint = back[:, share:].reshape(heads, width, width)
    return start_state, start_adjoint, riders


def running_sum(decay_blk):
    length = decay_blk.shape[1]
    lower = (
        lax.broadcasted_iota(jnp.int32, (length, length), 1)
        <= lax.broadcasted_iota(jnp.int32, (length, length), 0)
    ).astype(decay_blk.dtype)
    return jnp.einsum("ts,nsh->nth", lower, decay_blk, preferred_element_type=jnp.float32)


def within_group(totals, pieces, reverse):
    blocks = totals.shape[0]
    at = lax.broadcasted_iota(jnp.int32, (blocks, blocks, blocks), 0)
    src = lax.broadcasted_iota(jnp.int32, (blocks, blocks, blocks), 1)
    mid = lax.broadcasted_iota(jnp.int32, (blocks, blocks, blocks), 2)
    between = ((at < mid) & (mid < src)) if reverse else ((src < mid) & (mid < at))
    logs = jnp.sum(jnp.where(between[..., None], totals[None, None], 0.0), axis=2)
    pos = lax.broadcasted_iota(jnp.int32, (blocks, blocks), 0)
    other = lax.broadcasted_iota(jnp.int32, (blocks, blocks), 1)
    earlier = (other > pos) if reverse else (other < pos)
    later = (other < pos) if reverse else (other > pos)
    weights = jnp.where(earlier[..., None], jnp.exp(jnp.where(earlier[..., None], logs, 0.0)), 0.0)
    seen_log = jnp.sum(jnp.where(earlier[..., None], totals[None], 0.0), axis=1)
    tail_log = jnp.sum(jnp.where(later[..., None], totals[None], 0.0), axis=1)
    seen = split_left("ijh,jhab->ihab", weights, pieces)
    whole = split_left("jh,jhab->hab", jnp.exp(tail_log), pieces)
    return seen, seen_log, whole, jnp.sum(totals, axis=0)


def local_block(queries, keys, values, out_grad, log_decay):
    length = queries.shape[0]
    heads = log_decay.shape[1]
    width = queries.shape[1] // heads
    query_blk = queries.reshape(length, heads, width)
    key_blk = keys.reshape(length, heads, width)
    value_blk = values.reshape(length, heads, width)
    grad_blk = out_grad.reshape(length, heads, width)
    cumul = running_sum(log_decay[None])[0]
    total = cumul[-1]
    after = jnp.exp(total[None, :] - cumul)
    before = jnp.exp(cumul)
    contrib = split_left("sha,shb->hab", after[..., None] * widen(key_blk), value_blk)
    update = split_left("tha,thb->hab", before[..., None] * widen(query_blk), grad_blk)
    return (query_blk, key_blk, value_blk, grad_blk, cumul, after, before, contrib, update)


def intra(query_blk, key_blk, value_blk, grad_blk, cumul):
    length = cumul.shape[0]
    heads_first = cumul.T
    spread = heads_first[:, :, None] - heads_first[:, None, :]
    causal = lax.broadcasted_iota(jnp.int32, (length, length), 1) <= lax.broadcasted_iota(
        jnp.int32, (length, length), 0
    )
    weights = jnp.where(causal[None], jnp.exp(jnp.where(causal[None], spread, 0.0)), 0.0)
    grad_scores = product("thd,shd->hts", grad_blk, value_blk)
    key_scores = product("thd,shd->hts", query_blk, key_blk)
    first = (weights * grad_scores).astype(jnp.bfloat16)
    second = (weights * key_scores).astype(jnp.bfloat16)
    query_part = product("hts,shd->htd", first, key_blk)
    key_part = product("hts,thd->hsd", first, query_blk)
    value_part = product("hts,thd->hsd", second, grad_blk)
    return query_part, key_part, value_part


def finish_kernel(
    grad_ref, value_ref, key_ref, state_ref, adjoint_ref, qp_ref, kp_ref, vp_ref, before_ref,
    after_ref, gq_ref, gk_ref, gv_ref,
):
    group, width = state_ref.shape[0], state_ref.shape[2]
    back = (((1,), (1,)), ((), ()))
    for i in range(group):
        cols = slice(i * width, (i + 1) * width)
        grad = grad_ref[:, cols]
        value = value_ref[:, cols]
        key = key_ref[:, cols]
        state = state_ref[i]
        adjoint = adjoint_ref[i]
        with_state = lax.dot_general(grad, state, back, preferred_element_type=jnp.float32)
        with_adjoint_v = lax.dot_general(value, adjoint, back, preferred_element_type=jnp.float32)
        with_adjoint_k = jnp.dot(key, adjoint, preferred_element_type=jnp.float32)
        gq_ref[:, cols] = (qp_ref[i] + before_ref[i] * with_state).astype(gq_ref.dtype)
        gk_ref[:, cols] = (kp_ref[i] + after_ref[i] * with_adjoint_v).astype(gk_ref.dtype)
        gv_ref[:, cols] = (vp_ref[i] + after_ref[i] * with_adjoint_k).astype(gv_ref.dtype)


def finish_call(out_grad, values, keys, state_in, adjoint_in, qp, kp, vp, before_t, after_t):
    length, columns = out_grad.shape
    heads, width = state_in.shape[0], state_in.shape[2]
    group = 4
    steps = heads // group
    flat_spec = pl.BlockSpec((length, group * width), lambda h: (0, h))
    head_spec = pl.BlockSpec((group, width, width), lambda h: (h, 0, 0))
    part_spec = pl.BlockSpec((group, length, width), lambda h: (h, 0, 0))
    scale_spec = pl.BlockSpec((group, length, 1), lambda h: (h, 0, 0))
    out = jax.ShapeDtypeStruct((length, columns), jnp.bfloat16)
    return pl.pallas_call(
        finish_kernel,
        grid=(steps,),
        in_specs=[flat_spec, flat_spec, flat_spec, head_spec, head_spec, part_spec, part_spec,
                  part_spec, scale_spec, scale_spec],
        out_specs=[flat_spec, flat_spec, flat_spec],
        out_shape=[out, out, out],
    )(out_grad, values, keys, state_in, adjoint_in, qp, kp, vp, before_t, after_t)


def body(queries, keys, values, out_grad, log_decay):
    peers = lax.axis_size("exp")
    length = queries.shape[0]
    heads = log_decay.shape[1]
    width = queries.shape[1] // heads
    group = heads // peers
    (query_blk, key_blk, value_blk, grad_blk, cumul, after, before, contrib, update) = local_block(
        queries, keys, values, out_grad, log_decay
    )
    share = group * width
    decay_rows = jnp.transpose(log_decay.reshape(length, peers, group), (1, 2, 0))
    pad_rows = 16
    decay_rows = jnp.pad(decay_rows, ((0, 0), (0, pad_rows - group), (0, 0)))
    packed = jnp.concatenate(
        [
            contrib.astype(jnp.bfloat16).reshape(peers, share, width),
            update.astype(jnp.bfloat16).reshape(peers, share, width),
            decay_rows.astype(jnp.bfloat16),
        ],
        axis=1,
    )
    got = lax.all_to_all(packed, "exp", 0, 0, tiled=True)
    contrib_g = got[:, :share].reshape(peers, group, width, width)
    update_g = got[:, share : 2 * share].reshape(peers, group, width, width)
    totals = jnp.sum(widen(got[:, 2 * share : 2 * share + group]), axis=2)
    query_part, key_part, value_part = intra(query_blk, key_blk, value_blk, grad_blk, cumul)
    totals, contrib_g, update_g, query_part, key_part, value_part = lax.optimization_barrier(
        (totals, contrib_g, update_g, query_part, key_part, value_part)
    )
    prefix, prefix_log, dev_state, dev_log = within_group(totals, contrib_g, False)
    suffix, suffix_log, dev_adjoint, unused = within_group(totals, update_g, True)
    start_state, start_adjoint, (prefix, suffix) = carried_both(
        dev_log, dev_state, dev_adjoint, "seq", (prefix, suffix)
    )
    state_prev = jnp.exp(prefix_log)[:, :, None, None] * start_state[None] + prefix
    adjoint = jnp.exp(suffix_log)[:, :, None, None] * start_adjoint[None] + suffix
    returned = jnp.concatenate(
        [
            state_prev.astype(jnp.bfloat16).reshape(peers, share, width),
            adjoint.astype(jnp.bfloat16).reshape(peers, share, width),
        ],
        axis=1,
    )
    back = lax.all_to_all(returned, "exp", 0, 0, tiled=True)
    state_in = back[:, :share].reshape(heads, width, width)
    adjoint_in = back[:, share:].reshape(heads, width, width)
    grad_query, grad_key, grad_value = finish_call(
        out_grad, values, keys, state_in, adjoint_in, query_part, key_part, value_part,
        before.T[:, :, None], after.T[:, :, None],
    )
    return (grad_query, grad_key, grad_value)


def solution(mesh):
    placed = tuple(P(SEQ_EXP, None) for _ in range(5))
    return jax.shard_map(
        body,
        mesh=mesh,
        in_specs=placed,
        out_specs=(P(SEQ_EXP, None), P(SEQ_EXP, None), P(SEQ_EXP, None)),
        check_vma=False,
    )
```

```python
import jax
import jax.numpy as jnp
from jax import lax
from jax.sharding import PartitionSpec as P
from jax.experimental import pallas as pl

BLOCK = 128
SEQ_EXP = ("seq", "exp")


def widen(array):
    return array.astype(jnp.float32)


def halves(array):
    rounded = lax.reduce_precision(array, exponent_bits=8, mantissa_bits=7)
    low = (array - rounded).astype(jnp.bfloat16)
    return (rounded.astype(jnp.bfloat16), low)


def product(form, first_op, second_op):
    return jnp.einsum(form, first_op, second_op, preferred_element_type=jnp.float32)


def split_left(form, wide_op, narrow_op):
    high, low = halves(wide_op)
    return product(form, high, narrow_op) + product(form, low, narrow_op)


def split_right(form, narrow_op, wide_op):
    high, low = halves(wide_op)
    return product(form, narrow_op, high) + product(form, narrow_op, low)


def link(earlier, later):
    return (earlier[0] + later[0], jnp.exp(later[0])[:, None, None] * earlier[1] + later[1])


def pieces_of(array):
    high = array.astype(jnp.bfloat16)
    rest = array - widen(high)
    mid = rest.astype(jnp.bfloat16)
    low = (rest - widen(mid)).astype(jnp.bfloat16)
    return high, mid, low


def carried_both(dev_log, dev_state, dev_adjoint, axis, riders):
    peers = lax.axis_size(axis)
    here = lax.axis_index(axis)
    heads, width = dev_state.shape[0], dev_state.shape[2]
    share = heads * width // peers
    spare = 16
    logs = jnp.zeros((spare, width), jnp.bfloat16)
    for i, part in enumerate(pieces_of(dev_log)):
        logs = logs.at[i * heads : (i + 1) * heads, :].set(
            jnp.broadcast_to(part[:, None], (heads, width))
        )
    payload = jnp.concatenate(
        [
            dev_state.astype(jnp.bfloat16).reshape(peers, share, width),
            dev_adjoint.astype(jnp.bfloat16).reshape(peers, share, width),
            jnp.broadcast_to(logs[None], (peers, spare, width)),
        ],
        axis=1,
    )
    got = lax.all_to_all(payload, axis, 0, 0, tiled=True)
    got, riders = lax.optimization_barrier((got, riders))
    head = (here * share) // width
    pick = (lax.broadcasted_iota(jnp.int32, (heads,), 0) == head).astype(jnp.float32)
    log_rows = widen(got[:, 2 * share : 2 * share + 3 * heads, 0]).reshape(peers, 3, heads)
    totals = jnp.sum(log_rows[:, 0] * pick[None, :], axis=1)
    totals = totals + jnp.sum(log_rows[:, 1] * pick[None, :], axis=1)
    totals = totals + jnp.sum(log_rows[:, 2] * pick[None, :], axis=1)
    dst = lax.broadcasted_iota(jnp.int32, (peers, peers, peers), 0)
    src = lax.broadcasted_iota(jnp.int32, (peers, peers, peers), 1)
    mid = lax.broadcasted_iota(jnp.int32, (peers, peers, peers), 2)
    between_fwd = (src < mid) & (mid < dst)
    between_bwd = (dst < mid) & (mid < src)
    log_fwd = jnp.sum(jnp.where(between_fwd, totals[None, None, :], 0.0), axis=2)
    log_bwd = jnp.sum(jnp.where(between_bwd, totals[None, None, :], 0.0), axis=2)
    dst2 = lax.broadcasted_iota(jnp.int32, (peers, peers), 0)
    src2 = lax.broadcasted_iota(jnp.int32, (peers, peers), 1)
    w_fwd = jnp.where(src2 < dst2, jnp.exp(jnp.where(src2 < dst2, log_fwd, 0.0)), 0.0)
    w_bwd = jnp.where(src2 > dst2, jnp.exp(jnp.where(src2 > dst2, log_bwd, 0.0)), 0.0)
    state_rows = split_left("di,irc->drc", w_fwd, got[:, :share])
    adjoint_rows = split_left("di,irc->drc", w_bwd, got[:, share : 2 * share])
    back = lax.all_to_all(
        jnp.concatenate([state_rows, adjoint_rows], axis=1), axis, 0, 0, tiled=True
    )
    start_state = back[:, :share].reshape(heads, width, width)
    start_adjoint = back[:, share:].reshape(heads, width, width)
    return start_state, start_adjoint, riders


def running_sum(decay_blk):
    length = decay_blk.shape[1]
    lower = (
        lax.broadcasted_iota(jnp.int32, (length, length), 1)
        <= lax.broadcasted_iota(jnp.int32, (length, length), 0)
    ).astype(decay_blk.dtype)
    return jnp.einsum("ts,nsh->nth", lower, decay_blk, preferred_element_type=jnp.float32)


def within_group(totals, pieces, reverse):
    blocks = totals.shape[0]
    at = lax.broadcasted_iota(jnp.int32, (blocks, blocks, blocks), 0)
    src = lax.broadcasted_iota(jnp.int32, (blocks, blocks, blocks), 1)
    mid = lax.broadcasted_iota(jnp.int32, (blocks, blocks, blocks), 2)
    between = ((at < mid) & (mid < src)) if reverse else ((src < mid) & (mid < at))
    logs = jnp.sum(jnp.where(between[..., None], totals[None, None], 0.0), axis=2)
    pos = lax.broadcasted_iota(jnp.int32, (blocks, blocks), 0)
    other = lax.broadcasted_iota(jnp.int32, (blocks, blocks), 1)
    earlier = (other > pos) if reverse else (other < pos)
    later = (other < pos) if reverse else (other > pos)
    weights = jnp.where(earlier[..., None], jnp.exp(jnp.where(earlier[..., None], logs, 0.0)), 0.0)
    seen_log = jnp.sum(jnp.where(earlier[..., None], totals[None], 0.0), axis=1)
    tail_log = jnp.sum(jnp.where(later[..., None], totals[None], 0.0), axis=1)
    seen = split_left("ijh,jhab->ihab", weights, pieces)
    whole = split_left("jh,jhab->hab", jnp.exp(tail_log), pieces)
    return seen, seen_log, whole, jnp.sum(totals, axis=0)


def local_block(queries, keys, values, out_grad, log_decay):
    length = queries.shape[0]
    heads = log_decay.shape[1]
    width = queries.shape[1] // heads
    query_blk = queries.reshape(length, heads, width)
    key_blk = keys.reshape(length, heads, width)
    value_blk = values.reshape(length, heads, width)
    grad_blk = out_grad.reshape(length, heads, width)
    cumul = running_sum(log_decay[None])[0]
    total = cumul[-1]
    after = jnp.exp(total[None, :] - cumul)
    before = jnp.exp(cumul)
    contrib = split_left("sha,shb->hab", after[..., None] * widen(key_blk), value_blk)
    update = split_left("tha,thb->hab", before[..., None] * widen(query_blk), grad_blk)
    return (query_blk, key_blk, value_blk, grad_blk, cumul, after, before, contrib, update)


def intra(query_blk, key_blk, value_blk, grad_blk, cumul):
    length = cumul.shape[0]
    heads_first = cumul.T
    spread = heads_first[:, :, None] - heads_first[:, None, :]
    causal = lax.broadcasted_iota(jnp.int32, (length, length), 1) <= lax.broadcasted_iota(
        jnp.int32, (length, length), 0
    )
    weights = jnp.where(causal[None], jnp.exp(jnp.where(causal[None], spread, 0.0)), 0.0)
    grad_scores = product("thd,shd->hts", grad_blk, value_blk)
    key_scores = product("thd,shd->hts", query_blk, key_blk)
    first = (weights * grad_scores).astype(jnp.bfloat16)
    second = (weights * key_scores).astype(jnp.bfloat16)
    query_part = product("hts,shd->htd", first, key_blk)
    key_part = product("hts,thd->hsd", first, query_blk)
    value_part = product("hts,thd->hsd", second, grad_blk)
    return query_part, key_part, value_part


def finish_kernel(
    grad_ref, value_ref, key_ref, state_ref, adjoint_ref, qp_ref, kp_ref, vp_ref, before_ref,
    after_ref, gq_ref, gk_ref, gv_ref,
):
    group, width = state_ref.shape[0], state_ref.shape[2]
    back = (((1,), (1,)), ((), ()))
    for i in range(group):
        cols = slice(i * width, (i + 1) * width)
        grad = grad_ref[:, cols]
        value = value_ref[:, cols]
        key = key_ref[:, cols]
        state = state_ref[i]
        adjoint = adjoint_ref[i]
        with_state = lax.dot_general(grad, state, back, preferred_element_type=jnp.float32)
        with_adjoint_v = lax.dot_general(value, adjoint, back, preferred_element_type=jnp.float32)
        with_adjoint_k = jnp.dot(key, adjoint, preferred_element_type=jnp.float32)
        gq_ref[:, cols] = (qp_ref[i] + before_ref[i] * with_state).astype(gq_ref.dtype)
        gk_ref[:, cols] = (kp_ref[i] + after_ref[i] * with_adjoint_v).astype(gk_ref.dtype)
        gv_ref[:, cols] = (vp_ref[i] + after_ref[i] * with_adjoint_k).astype(gv_ref.dtype)


def finish_call(out_grad, values, keys, state_in, adjoint_in, qp, kp, vp, before_t, after_t):
    length, columns = out_grad.shape
    heads, width = state_in.shape[0], state_in.shape[2]
    group = 4
    steps = heads // group
    flat_spec = pl.BlockSpec((length, group * width), lambda h: (0, h))
    head_spec = pl.BlockSpec((group, width, width), lambda h: (h, 0, 0))
    part_spec = pl.BlockSpec((group, length, width), lambda h: (h, 0, 0))
    scale_spec = pl.BlockSpec((group, length, 1), lambda h: (h, 0, 0))
    out = jax.ShapeDtypeStruct((length, columns), jnp.bfloat16)
    return pl.pallas_call(
        finish_kernel,
        grid=(steps,),
        in_specs=[flat_spec, flat_spec, flat_spec, head_spec, head_spec, part_spec, part_spec,
                  part_spec, scale_spec, scale_spec],
        out_specs=[flat_spec, flat_spec, flat_spec],
        out_shape=[out, out, out],
    )(out_grad, values, keys, state_in, adjoint_in, qp, kp, vp, before_t, after_t)


def body(queries, keys, values, out_grad, log_decay):
    peers = lax.axis_size("exp")
    length = queries.shape[0]
    heads = log_decay.shape[1]
    width = queries.shape[1] // heads
    group = heads // peers
    (query_blk, key_blk, value_blk, grad_blk, cumul, after, before, contrib, update) = local_block(
        queries, keys, values, out_grad, log_decay
    )
    share = group * width
    decay_rows = jnp.transpose(log_decay.reshape(length, peers, group), (1, 2, 0))
    pad_rows = 16
    decay_rows = jnp.pad(decay_rows, ((0, 0), (0, pad_rows - group), (0, 0)))
    packed = jnp.concatenate(
        [
            contrib.astype(jnp.bfloat16).reshape(peers, share, width),
            update.astype(jnp.bfloat16).reshape(peers, share, width),
            decay_rows.astype(jnp.bfloat16),
        ],
        axis=1,
    )
    got = lax.all_to_all(packed, "exp", 0, 0, tiled=True)
    contrib_g = got[:, :share].reshape(peers, group, width, width)
    update_g = got[:, share : 2 * share].reshape(peers, group, width, width)
    totals = jnp.sum(widen(got[:, 2 * share : 2 * share + group]), axis=2)
    query_part, key_part, value_part = intra(query_blk, key_blk, value_blk, grad_blk, cumul)
    totals, contrib_g, update_g, query_part, key_part, value_part = lax.optimization_barrier(
        (totals, contrib_g, update_g, query_part, key_part, value_part)
    )
    prefix, prefix_log, dev_state, dev_log = within_group(totals, contrib_g, False)
    suffix, suffix_log, dev_adjoint, unused = within_group(totals, update_g, True)
    start_state, start_adjoint, (prefix, suffix) = carried_both(
        dev_log, dev_state, dev_adjoint, "seq", (prefix, suffix)
    )
    state_prev = jnp.exp(prefix_log)[:, :, None, None] * start_state[None] + prefix
    adjoint = jnp.exp(suffix_log)[:, :, None, None] * start_adjoint[None] + suffix
    returned = jnp.concatenate(
        [
            state_prev.astype(jnp.bfloat16).reshape(peers, share, width),
            adjoint.astype(jnp.bfloat16).reshape(peers, share, width),
        ],
        axis=1,
    )
    back = lax.all_to_all(returned, "exp", 0, 0, tiled=True)
    state_in = back[:, :share].reshape(heads, width, width)
    adjoint_in = back[:, share:].reshape(heads, width, width)
    grad_query, grad_key, grad_value = finish_call(
        out_grad, values, keys, state_in, adjoint_in, query_part, key_part, value_part,
        before.T[:, :, None], after.T[:, :, None],
    )
    return (grad_query, grad_key, grad_value)


def solution(mesh):
    placed = tuple(P(SEQ_EXP, None) for _ in range(5))
    return jax.shard_map(
        body,
        mesh=mesh,
        in_specs=placed,
        out_specs=(P(SEQ_EXP, None), P(SEQ_EXP, None), P(SEQ_EXP, None)),
        check_vma=False,
    )
```

```python
import jax
import jax.numpy as jnp
from jax import lax
from jax.sharding import PartitionSpec as P
from jax.experimental import pallas as pl

BLOCK = 128
SEQ_EXP = ("seq", "exp")


def widen(array):
    return array.astype(jnp.float32)


def halves(array):
    rounded = lax.reduce_precision(array, exponent_bits=8, mantissa_bits=7)
    low = (array - rounded).astype(jnp.bfloat16)
    return (rounded.astype(jnp.bfloat16), low)


def product(form, first_op, second_op):
    return jnp.einsum(form, first_op, second_op, preferred_element_type=jnp.float32)


def split_left(form, wide_op, narrow_op):
    high, low = halves(wide_op)
    return product(form, high, narrow_op) + product(form, low, narrow_op)


def split_right(form, narrow_op, wide_op):
    high, low = halves(wide_op)
    return product(form, narrow_op, high) + product(form, narrow_op, low)


def link(earlier, later):
    return (earlier[0] + later[0], jnp.exp(later[0])[:, None, None] * earlier[1] + later[1])


def pieces_of(array):
    high = array.astype(jnp.bfloat16)
    rest = array - widen(high)
    mid = rest.astype(jnp.bfloat16)
    low = (rest - widen(mid)).astype(jnp.bfloat16)
    return high, mid, low


def carried_both(dev_log, dev_state, dev_adjoint, axis, riders):
    peers = lax.axis_size(axis)
    here = lax.axis_index(axis)
    heads, width = dev_state.shape[0], dev_state.shape[2]
    share = heads * width // peers
    spare = 16
    logs = jnp.zeros((spare, width), jnp.bfloat16)
    for i, part in enumerate(pieces_of(dev_log)):
        logs = logs.at[i * heads : (i + 1) * heads, :].set(
            jnp.broadcast_to(part[:, None], (heads, width))
        )
    payload = jnp.concatenate(
        [
            dev_state.astype(jnp.bfloat16).reshape(peers, share, width),
            dev_adjoint.astype(jnp.bfloat16).reshape(peers, share, width),
            jnp.broadcast_to(logs[None], (peers, spare, width)),
        ],
        axis=1,
    )
    got = lax.all_to_all(payload, axis, 0, 0, tiled=True)
    got, riders = lax.optimization_barrier((got, riders))
    head = (here * share) // width
    pick = (lax.broadcasted_iota(jnp.int32, (heads,), 0) == head).astype(jnp.float32)
    log_rows = widen(got[:, 2 * share : 2 * share + 3 * heads, 0]).reshape(peers, 3, heads)
    totals = jnp.sum(log_rows[:, 0] * pick[None, :], axis=1)
    totals = totals + jnp.sum(log_rows[:, 1] * pick[None, :], axis=1)
    totals = totals + jnp.sum(log_rows[:, 2] * pick[None, :], axis=1)
    dst = lax.broadcasted_iota(jnp.int32, (peers, peers, peers), 0)
    src = lax.broadcasted_iota(jnp.int32, (peers, peers, peers), 1)
    mid = lax.broadcasted_iota(jnp.int32, (peers, peers, peers), 2)
    between_fwd = (src < mid) & (mid < dst)
    between_bwd = (dst < mid) & (mid < src)
    log_fwd = jnp.sum(jnp.where(between_fwd, totals[None, None, :], 0.0), axis=2)
    log_bwd = jnp.sum(jnp.where(between_bwd, totals[None, None, :], 0.0), axis=2)
    dst2 = lax.broadcasted_iota(jnp.int32, (peers, peers), 0)
    src2 = lax.broadcasted_iota(jnp.int32, (peers, peers), 1)
    w_fwd = jnp.where(src2 < dst2, jnp.exp(jnp.where(src2 < dst2, log_fwd, 0.0)), 0.0)
    w_bwd = jnp.where(src2 > dst2, jnp.exp(jnp.where(src2 > dst2, log_bwd, 0.0)), 0.0)
    state_rows = split_left("di,irc->drc", w_fwd, got[:, :share])
    adjoint_rows = split_left("di,irc->drc", w_bwd, got[:, share : 2 * share])
    back = lax.all_to_all(
        jnp.concatenate([state_rows, adjoint_rows], axis=1).astype(jnp.bfloat16),
        axis,
        0,
        0,
        tiled=True,
    )
    start_state = widen(back[:, :share]).reshape(heads, width, width)
    start_adjoint = widen(back[:, share:]).reshape(heads, width, width)
    return start_state, start_adjoint, riders


def running_sum(decay_blk):
    length = decay_blk.shape[1]
    lower = (
        lax.broadcasted_iota(jnp.int32, (length, length), 1)
        <= lax.broadcasted_iota(jnp.int32, (length, length), 0)
    ).astype(decay_blk.dtype)
    return jnp.einsum("ts,nsh->nth", lower, decay_blk, preferred_element_type=jnp.float32)


def within_group(totals, pieces, reverse):
    blocks = totals.shape[0]
    at = lax.broadcasted_iota(jnp.int32, (blocks, blocks, blocks), 0)
    src = lax.broadcasted_iota(jnp.int32, (blocks, blocks, blocks), 1)
    mid = lax.broadcasted_iota(jnp.int32, (blocks, blocks, blocks), 2)
    between = ((at < mid) & (mid < src)) if reverse else ((src < mid) & (mid < at))
    logs = jnp.sum(jnp.where(between[..., None], totals[None, None], 0.0), axis=2)
    pos = lax.broadcasted_iota(jnp.int32, (blocks, blocks), 0)
    other = lax.broadcasted_iota(jnp.int32, (blocks, blocks), 1)
    earlier = (other > pos) if reverse else (other < pos)
    later = (other < pos) if reverse else (other > pos)
    weights = jnp.where(earlier[..., None], jnp.exp(jnp.where(earlier[..., None], logs, 0.0)), 0.0)
    seen_log = jnp.sum(jnp.where(earlier[..., None], totals[None], 0.0), axis=1)
    tail_log = jnp.sum(jnp.where(later[..., None], totals[None], 0.0), axis=1)
    seen = split_left("ijh,jhab->ihab", weights, pieces)
    whole = split_left("jh,jhab->hab", jnp.exp(tail_log), pieces)
    return seen, seen_log, whole, jnp.sum(totals, axis=0)


def local_block(queries, keys, values, out_grad, log_decay):
    length = queries.shape[0]
    heads = log_decay.shape[1]
    width = queries.shape[1] // heads
    query_blk = queries.reshape(length, heads, width)
    key_blk = keys.reshape(length, heads, width)
    value_blk = values.reshape(length, heads, width)
    grad_blk = out_grad.reshape(length, heads, width)
    cumul = running_sum(log_decay[None])[0]
    total = cumul[-1]
    after = jnp.exp(total[None, :] - cumul)
    before = jnp.exp(cumul)
    contrib = split_left("sha,shb->hab", after[..., None] * widen(key_blk), value_blk)
    update = split_left("tha,thb->hab", before[..., None] * widen(query_blk), grad_blk)
    return (query_blk, key_blk, value_blk, grad_blk, cumul, after, before, contrib, update)


def intra(query_blk, key_blk, value_blk, grad_blk, cumul):
    length = cumul.shape[0]
    heads_first = cumul.T
    spread = heads_first[:, :, None] - heads_first[:, None, :]
    causal = lax.broadcasted_iota(jnp.int32, (length, length), 1) <= lax.broadcasted_iota(
        jnp.int32, (length, length), 0
    )
    weights = jnp.where(causal[None], jnp.exp(jnp.where(causal[None], spread, 0.0)), 0.0)
    grad_scores = product("thd,shd->hts", grad_blk, value_blk)
    key_scores = product("thd,shd->hts", query_blk, key_blk)
    first = (weights * grad_scores).astype(jnp.bfloat16)
    second = (weights * key_scores).astype(jnp.bfloat16)
    query_part = product("hts,shd->htd", first, key_blk)
    key_part = product("hts,thd->hsd", first, query_blk)
    value_part = product("hts,thd->hsd", second, grad_blk)
    return query_part, key_part, value_part


def finish_kernel(
    grad_ref, value_ref, key_ref, state_ref, adjoint_ref, qp_ref, kp_ref, vp_ref, before_ref,
    after_ref, gq_ref, gk_ref, gv_ref,
):
    group, width = state_ref.shape[0], state_ref.shape[2]
    back = (((1,), (1,)), ((), ()))
    for i in range(group):
        cols = slice(i * width, (i + 1) * width)
        grad = grad_ref[:, cols]
        value = value_ref[:, cols]
        key = key_ref[:, cols]
        state = state_ref[i]
        adjoint = adjoint_ref[i]
        with_state = lax.dot_general(grad, state, back, preferred_element_type=jnp.float32)
        with_adjoint_v = lax.dot_general(value, adjoint, back, preferred_element_type=jnp.float32)
        with_adjoint_k = jnp.dot(key, adjoint, preferred_element_type=jnp.float32)
        gq_ref[:, cols] = (qp_ref[i] + before_ref[i] * with_state).astype(gq_ref.dtype)
        gk_ref[:, cols] = (kp_ref[i] + after_ref[i] * with_adjoint_v).astype(gk_ref.dtype)
        gv_ref[:, cols] = (vp_ref[i] + after_ref[i] * with_adjoint_k).astype(gv_ref.dtype)


def finish_call(out_grad, values, keys, state_in, adjoint_in, qp, kp, vp, before_t, after_t):
    length, columns = out_grad.shape
    heads, width = state_in.shape[0], state_in.shape[2]
    group = 4
    steps = heads // group
    flat_spec = pl.BlockSpec((length, group * width), lambda h: (0, h))
    head_spec = pl.BlockSpec((group, width, width), lambda h: (h, 0, 0))
    part_spec = pl.BlockSpec((group, length, width), lambda h: (h, 0, 0))
    scale_spec = pl.BlockSpec((group, length, 1), lambda h: (h, 0, 0))
    out = jax.ShapeDtypeStruct((length, columns), jnp.bfloat16)
    return pl.pallas_call(
        finish_kernel,
        grid=(steps,),
        in_specs=[flat_spec, flat_spec, flat_spec, head_spec, head_spec, part_spec, part_spec,
                  part_spec, scale_spec, scale_spec],
        out_specs=[flat_spec, flat_spec, flat_spec],
        out_shape=[out, out, out],
    )(out_grad, values, keys, state_in, adjoint_in, qp, kp, vp, before_t, after_t)


def body(queries, keys, values, out_grad, log_decay):
    peers = lax.axis_size("exp")
    length = queries.shape[0]
    heads = log_decay.shape[1]
    width = queries.shape[1] // heads
    group = heads // peers
    (query_blk, key_blk, value_blk, grad_blk, cumul, after, before, contrib, update) = local_block(
        queries, keys, values, out_grad, log_decay
    )
    share = group * width
    decay_rows = jnp.transpose(log_decay.reshape(length, peers, group), (1, 2, 0))
    pad_rows = 16
    decay_rows = jnp.pad(decay_rows, ((0, 0), (0, pad_rows - group), (0, 0)))
    packed = jnp.concatenate(
        [
            contrib.astype(jnp.bfloat16).reshape(peers, share, width),
            update.astype(jnp.bfloat16).reshape(peers, share, width),
            decay_rows.astype(jnp.bfloat16),
        ],
        axis=1,
    )
    got = lax.all_to_all(packed, "exp", 0, 0, tiled=True)
    contrib_g = got[:, :share].reshape(peers, group, width, width)
    update_g = got[:, share : 2 * share].reshape(peers, group, width, width)
    totals = jnp.sum(widen(got[:, 2 * share : 2 * share + group]), axis=2)
    query_part, key_part, value_part = intra(query_blk, key_blk, value_blk, grad_blk, cumul)
    totals, contrib_g, update_g, query_part, key_part, value_part = lax.optimization_barrier(
        (totals, contrib_g, update_g, query_part, key_part, value_part)
    )
    prefix, prefix_log, dev_state, dev_log = within_group(totals, contrib_g, False)
    suffix, suffix_log, dev_adjoint, unused = within_group(totals, update_g, True)
    start_state, start_adjoint, (prefix, suffix) = carried_both(
        dev_log, dev_state, dev_adjoint, "seq", (prefix, suffix)
    )
    state_prev = jnp.exp(prefix_log)[:, :, None, None] * start_state[None] + prefix
    adjoint = jnp.exp(suffix_log)[:, :, None, None] * start_adjoint[None] + suffix
    returned = jnp.concatenate(
        [
            state_prev.astype(jnp.bfloat16).reshape(peers, share, width),
            adjoint.astype(jnp.bfloat16).reshape(peers, share, width),
        ],
        axis=1,
    )
    back = lax.all_to_all(returned, "exp", 0, 0, tiled=True)
    state_in = back[:, :share].reshape(heads, width, width)
    adjoint_in = back[:, share:].reshape(heads, width, width)
    grad_query, grad_key, grad_value = finish_call(
        out_grad, values, keys, state_in, adjoint_in, query_part, key_part, value_part,
        before.T[:, :, None], after.T[:, :, None],
    )
    return (grad_query, grad_key, grad_value)


def solution(mesh):
    placed = tuple(P(SEQ_EXP, None) for _ in range(5))
    return jax.shard_map(
        body,
        mesh=mesh,
        in_specs=placed,
        out_specs=(P(SEQ_EXP, None), P(SEQ_EXP, None), P(SEQ_EXP, None)),
        check_vma=False,
    )
```

```python
import jax
import jax.numpy as jnp
from jax import lax
from jax.sharding import PartitionSpec as P
from jax.experimental import pallas as pl

BLOCK = 128
SEQ_EXP = ("seq", "exp")


def widen(array):
    return array.astype(jnp.float32)


def halves(array):
    rounded = lax.reduce_precision(array, exponent_bits=8, mantissa_bits=7)
    low = (array - rounded).astype(jnp.bfloat16)
    return (rounded.astype(jnp.bfloat16), low)


def product(form, first_op, second_op):
    return jnp.einsum(form, first_op, second_op, preferred_element_type=jnp.float32)


def split_left(form, wide_op, narrow_op):
    high, low = halves(wide_op)
    return product(form, high, narrow_op) + product(form, low, narrow_op)


def split_right(form, narrow_op, wide_op):
    high, low = halves(wide_op)
    return product(form, narrow_op, high) + product(form, narrow_op, low)


def link(earlier, later):
    return (earlier[0] + later[0], jnp.exp(later[0])[:, None, None] * earlier[1] + later[1])


def pieces_of(array):
    high = array.astype(jnp.bfloat16)
    rest = array - widen(high)
    mid = rest.astype(jnp.bfloat16)
    low = (rest - widen(mid)).astype(jnp.bfloat16)
    return high, mid, low


def carried_both(dev_log, dev_state, dev_adjoint, axis, riders):
    peers = lax.axis_size(axis)
    here = lax.axis_index(axis)
    heads, width = dev_state.shape[0], dev_state.shape[2]
    share = heads * width // peers
    spare = 16
    logs = jnp.zeros((spare, width), jnp.bfloat16)
    for i, part in enumerate(pieces_of(dev_log)):
        logs = logs.at[i * heads : (i + 1) * heads, :].set(
            jnp.broadcast_to(part[:, None], (heads, width))
        )
    payload = jnp.concatenate(
        [
            dev_state.astype(jnp.bfloat16).reshape(peers, share, width),
            dev_adjoint.astype(jnp.bfloat16).reshape(peers, share, width),
            jnp.broadcast_to(logs[None], (peers, spare, width)),
        ],
        axis=1,
    )
    got = lax.all_to_all(payload, axis, 0, 0, tiled=True)
    got, riders = lax.optimization_barrier((got, riders))
    head = (here * share) // width
    pick = (lax.broadcasted_iota(jnp.int32, (heads,), 0) == head).astype(jnp.float32)
    log_rows = widen(got[:, 2 * share : 2 * share + 3 * heads, 0]).reshape(peers, 3, heads)
    totals = jnp.sum(log_rows[:, 0] * pick[None, :], axis=1)
    totals = totals + jnp.sum(log_rows[:, 1] * pick[None, :], axis=1)
    totals = totals + jnp.sum(log_rows[:, 2] * pick[None, :], axis=1)
    dst = lax.broadcasted_iota(jnp.int32, (peers, peers, peers), 0)
    src = lax.broadcasted_iota(jnp.int32, (peers, peers, peers), 1)
    mid = lax.broadcasted_iota(jnp.int32, (peers, peers, peers), 2)
    between_fwd = (src < mid) & (mid < dst)
    between_bwd = (dst < mid) & (mid < src)
    log_fwd = jnp.sum(jnp.where(between_fwd, totals[None, None, :], 0.0), axis=2)
    log_bwd = jnp.sum(jnp.where(between_bwd, totals[None, None, :], 0.0), axis=2)
    dst2 = lax.broadcasted_iota(jnp.int32, (peers, peers), 0)
    src2 = lax.broadcasted_iota(jnp.int32, (peers, peers), 1)
    w_fwd = jnp.where(src2 < dst2, jnp.exp(jnp.where(src2 < dst2, log_fwd, 0.0)), 0.0)
    w_bwd = jnp.where(src2 > dst2, jnp.exp(jnp.where(src2 > dst2, log_bwd, 0.0)), 0.0)
    state_rows = split_left("di,irc->drc", w_fwd, got[:, :share])
    adjoint_rows = split_left("di,irc->drc", w_bwd, got[:, share : 2 * share])
    back = lax.all_to_all(
        jnp.concatenate([state_rows, adjoint_rows], axis=1).astype(jnp.bfloat16),
        axis,
        0,
        0,
        tiled=True,
    )
    start_state = widen(back[:, :share]).reshape(heads, width, width)
    start_adjoint = widen(back[:, share:]).reshape(heads, width, width)
    return start_state, start_adjoint, riders


def running_sum(decay_blk):
    length = decay_blk.shape[1]
    lower = (
        lax.broadcasted_iota(jnp.int32, (length, length), 1)
        <= lax.broadcasted_iota(jnp.int32, (length, length), 0)
    ).astype(decay_blk.dtype)
    return jnp.einsum("ts,nsh->nth", lower, decay_blk, preferred_element_type=jnp.float32)


def within_group(totals, pieces, reverse):
    blocks = totals.shape[0]
    at = lax.broadcasted_iota(jnp.int32, (blocks, blocks, blocks), 0)
    src = lax.broadcasted_iota(jnp.int32, (blocks, blocks, blocks), 1)
    mid = lax.broadcasted_iota(jnp.int32, (blocks, blocks, blocks), 2)
    between = ((at < mid) & (mid < src)) if reverse else ((src < mid) & (mid < at))
    logs = jnp.sum(jnp.where(between[..., None], totals[None, None], 0.0), axis=2)
    pos = lax.broadcasted_iota(jnp.int32, (blocks, blocks), 0)
    other = lax.broadcasted_iota(jnp.int32, (blocks, blocks), 1)
    earlier = (other > pos) if reverse else (other < pos)
    later = (other < pos) if reverse else (other > pos)
    weights = jnp.where(earlier[..., None], jnp.exp(jnp.where(earlier[..., None], logs, 0.0)), 0.0)
    seen_log = jnp.sum(jnp.where(earlier[..., None], totals[None], 0.0), axis=1)
    tail_log = jnp.sum(jnp.where(later[..., None], totals[None], 0.0), axis=1)
    seen = split_left("ijh,jhab->ihab", weights, pieces)
    whole = split_left("jh,jhab->hab", jnp.exp(tail_log), pieces)
    return seen, seen_log, whole, jnp.sum(totals, axis=0)


def local_block(queries, keys, values, out_grad, log_decay):
    length = queries.shape[0]
    heads = log_decay.shape[1]
    width = queries.shape[1] // heads
    query_blk = queries.reshape(length, heads, width)
    key_blk = keys.reshape(length, heads, width)
    value_blk = values.reshape(length, heads, width)
    grad_blk = out_grad.reshape(length, heads, width)
    cumul = running_sum(log_decay[None])[0]
    total = cumul[-1]
    after = jnp.exp(total[None, :] - cumul)
    before = jnp.exp(cumul)
    contrib = split_left("sha,shb->hab", after[..., None] * widen(key_blk), value_blk)
    update = split_left("tha,thb->hab", before[..., None] * widen(query_blk), grad_blk)
    return (query_blk, key_blk, value_blk, grad_blk, cumul, after, before, contrib, update)


def intra(query_blk, key_blk, value_blk, grad_blk, cumul):
    length = cumul.shape[0]
    heads_first = cumul.T
    spread = heads_first[:, :, None] - heads_first[:, None, :]
    causal = lax.broadcasted_iota(jnp.int32, (length, length), 1) <= lax.broadcasted_iota(
        jnp.int32, (length, length), 0
    )
    weights = jnp.where(causal[None], jnp.exp(jnp.where(causal[None], spread, 0.0)), 0.0)
    grad_scores = product("thd,shd->hts", grad_blk, value_blk)
    key_scores = product("thd,shd->hts", query_blk, key_blk)
    first = (weights * grad_scores).astype(jnp.bfloat16)
    second = (weights * key_scores).astype(jnp.bfloat16)
    query_part = product("hts,shd->htd", first, key_blk)
    key_part = product("hts,thd->hsd", first, query_blk)
    value_part = product("hts,thd->hsd", second, grad_blk)
    return query_part, key_part, value_part


def finish_kernel(
    grad_ref, value_ref, key_ref, state_ref, adjoint_ref, qp_ref, kp_ref, vp_ref, before_ref,
    after_ref, gq_ref, gk_ref, gv_ref,
):
    group, width = state_ref.shape[0], state_ref.shape[2]
    back = (((1,), (1,)), ((), ()))
    step = pl.program_id(0)
    lanes = lax.broadcasted_iota(jnp.int32, before_ref.shape, 1)
    before_all = before_ref[...]
    after_all = after_ref[...]
    for i in range(group):
        cols = slice(i * width, (i + 1) * width)
        head = step * group + i
        before = jnp.sum(jnp.where(lanes == head, before_all, 0.0), axis=1, keepdims=True)
        after = jnp.sum(jnp.where(lanes == head, after_all, 0.0), axis=1, keepdims=True)
        grad = grad_ref[:, cols]
        value = value_ref[:, cols]
        key = key_ref[:, cols]
        state = state_ref[i]
        adjoint = adjoint_ref[i]
        with_state = lax.dot_general(grad, state, back, preferred_element_type=jnp.float32)
        with_adjoint_v = lax.dot_general(value, adjoint, back, preferred_element_type=jnp.float32)
        with_adjoint_k = jnp.dot(key, adjoint, preferred_element_type=jnp.float32)
        gq_ref[:, cols] = (qp_ref[i] + before * with_state).astype(gq_ref.dtype)
        gk_ref[:, cols] = (kp_ref[i] + after * with_adjoint_v).astype(gk_ref.dtype)
        gv_ref[:, cols] = (vp_ref[i] + after * with_adjoint_k).astype(gv_ref.dtype)


def finish_call(out_grad, values, keys, state_in, adjoint_in, qp, kp, vp, before, after):
    length, columns = out_grad.shape
    heads, width = state_in.shape[0], state_in.shape[2]
    group = 4
    steps = heads // group
    flat_spec = pl.BlockSpec((length, group * width), lambda h: (0, h))
    head_spec = pl.BlockSpec((group, width, width), lambda h: (h, 0, 0))
    part_spec = pl.BlockSpec((group, length, width), lambda h: (h, 0, 0))
    scale_spec = pl.BlockSpec((length, heads), lambda h: (0, 0))
    out = jax.ShapeDtypeStruct((length, columns), jnp.bfloat16)
    return pl.pallas_call(
        finish_kernel,
        grid=(steps,),
        in_specs=[flat_spec, flat_spec, flat_spec, head_spec, head_spec, part_spec, part_spec,
                  part_spec, scale_spec, scale_spec],
        out_specs=[flat_spec, flat_spec, flat_spec],
        out_shape=[out, out, out],
    )(out_grad, values, keys, state_in, adjoint_in, qp, kp, vp, before, after)


def body(queries, keys, values, out_grad, log_decay):
    peers = lax.axis_size("exp")
    length = queries.shape[0]
    heads = log_decay.shape[1]
    width = queries.shape[1] // heads
    group = heads // peers
    (query_blk, key_blk, value_blk, grad_blk, cumul, after, before, contrib, update) = local_block(
        queries, keys, values, out_grad, log_decay
    )
    share = group * width
    decay_rows = jnp.transpose(log_decay.reshape(length, peers, group), (1, 2, 0))
    pad_rows = 16
    decay_rows = jnp.pad(decay_rows, ((0, 0), (0, pad_rows - group), (0, 0)))
    packed = jnp.concatenate(
        [
            contrib.astype(jnp.bfloat16).reshape(peers, share, width),
            update.astype(jnp.bfloat16).reshape(peers, share, width),
            decay_rows.astype(jnp.bfloat16),
        ],
        axis=1,
    )
    got = lax.all_to_all(packed, "exp", 0, 0, tiled=True)
    contrib_g = got[:, :share].reshape(peers, group, width, width)
    update_g = got[:, share : 2 * share].reshape(peers, group, width, width)
    totals = jnp.sum(widen(got[:, 2 * share : 2 * share + group]), axis=2)
    query_part, key_part, value_part = intra(query_blk, key_blk, value_blk, grad_blk, cumul)
    totals, contrib_g, update_g, query_part, key_part, value_part = lax.optimization_barrier(
        (totals, contrib_g, update_g, query_part, key_part, value_part)
    )
    prefix, prefix_log, dev_state, dev_log = within_group(totals, contrib_g, False)
    suffix, suffix_log, dev_adjoint, unused = within_group(totals, update_g, True)
    start_state, start_adjoint, (prefix, suffix) = carried_both(
        dev_log, dev_state, dev_adjoint, "seq", (prefix, suffix)
    )
    state_prev = jnp.exp(prefix_log)[:, :, None, None] * start_state[None] + prefix
    adjoint = jnp.exp(suffix_log)[:, :, None, None] * start_adjoint[None] + suffix
    returned = jnp.concatenate(
        [
            state_prev.astype(jnp.bfloat16).reshape(peers, share, width),
            adjoint.astype(jnp.bfloat16).reshape(peers, share, width),
        ],
        axis=1,
    )
    back = lax.all_to_all(returned, "exp", 0, 0, tiled=True)
    state_in = back[:, :share].reshape(heads, width, width)
    adjoint_in = back[:, share:].reshape(heads, width, width)
    grad_query, grad_key, grad_value = finish_call(
        out_grad, values, keys, state_in, adjoint_in, query_part, key_part, value_part,
        before, after,
    )
    return (grad_query, grad_key, grad_value)


def solution(mesh):
    placed = tuple(P(SEQ_EXP, None) for _ in range(5))
    return jax.shard_map(
        body,
        mesh=mesh,
        in_specs=placed,
        out_specs=(P(SEQ_EXP, None), P(SEQ_EXP, None), P(SEQ_EXP, None)),
        check_vma=False,
    )
```

```python
import jax
import jax.numpy as jnp
from jax import lax
from jax.sharding import PartitionSpec as P
from jax.experimental import pallas as pl

BLOCK = 128
SEQ_EXP = ("seq", "exp")


def widen(array):
    return array.astype(jnp.float32)


def halves(array):
    rounded = lax.reduce_precision(array, exponent_bits=8, mantissa_bits=7)
    low = (array - rounded).astype(jnp.bfloat16)
    return (rounded.astype(jnp.bfloat16), low)


def product(form, first_op, second_op):
    return jnp.einsum(form, first_op, second_op, preferred_element_type=jnp.float32)


def split_left(form, wide_op, narrow_op):
    high, low = halves(wide_op)
    return product(form, high, narrow_op) + product(form, low, narrow_op)


def split_right(form, narrow_op, wide_op):
    high, low = halves(wide_op)
    return product(form, narrow_op, high) + product(form, narrow_op, low)


def link(earlier, later):
    return (earlier[0] + later[0], jnp.exp(later[0])[:, None, None] * earlier[1] + later[1])


def pieces_of(array):
    high = array.astype(jnp.bfloat16)
    rest = array - widen(high)
    mid = rest.astype(jnp.bfloat16)
    low = (rest - widen(mid)).astype(jnp.bfloat16)
    return high, mid, low


def carried_both(dev_log, dev_state, dev_adjoint, axis, riders):
    peers = lax.axis_size(axis)
    here = lax.axis_index(axis)
    heads, width = dev_state.shape[0], dev_state.shape[2]
    share = heads * width // peers
    spare = 16
    logs = jnp.zeros((spare, width), jnp.bfloat16)
    for i, part in enumerate(pieces_of(dev_log)):
        logs = logs.at[i * heads : (i + 1) * heads, :].set(
            jnp.broadcast_to(part[:, None], (heads, width))
        )
    payload = jnp.concatenate(
        [
            dev_state.astype(jnp.bfloat16).reshape(peers, share, width),
            dev_adjoint.astype(jnp.bfloat16).reshape(peers, share, width),
            jnp.broadcast_to(logs[None], (peers, spare, width)),
        ],
        axis=1,
    )
    got = lax.all_to_all(payload, axis, 0, 0, tiled=True)
    got, riders = lax.optimization_barrier((got, riders))
    head = (here * share) // width
    pick = (lax.broadcasted_iota(jnp.int32, (heads,), 0) == head).astype(jnp.float32)
    log_rows = jnp.max(widen(got[:, 2 * share : 2 * share + 3 * heads, :]), axis=2)
    log_rows = log_rows.reshape(peers, 3, heads)
    totals = jnp.sum(log_rows[:, 0] * pick[None, :], axis=1)
    totals = totals + jnp.sum(log_rows[:, 1] * pick[None, :], axis=1)
    totals = totals + jnp.sum(log_rows[:, 2] * pick[None, :], axis=1)
    dst = lax.broadcasted_iota(jnp.int32, (peers, peers, peers), 0)
    src = lax.broadcasted_iota(jnp.int32, (peers, peers, peers), 1)
    mid = lax.broadcasted_iota(jnp.int32, (peers, peers, peers), 2)
    between_fwd = (src < mid) & (mid < dst)
    between_bwd = (dst < mid) & (mid < src)
    log_fwd = jnp.sum(jnp.where(between_fwd, totals[None, None, :], 0.0), axis=2)
    log_bwd = jnp.sum(jnp.where(between_bwd, totals[None, None, :], 0.0), axis=2)
    dst2 = lax.broadcasted_iota(jnp.int32, (peers, peers), 0)
    src2 = lax.broadcasted_iota(jnp.int32, (peers, peers), 1)
    w_fwd = jnp.where(src2 < dst2, jnp.exp(jnp.where(src2 < dst2, log_fwd, 0.0)), 0.0)
    w_bwd = jnp.where(src2 > dst2, jnp.exp(jnp.where(src2 > dst2, log_bwd, 0.0)), 0.0)
    state_rows = split_left("di,irc->drc", w_fwd, got[:, :share])
    adjoint_rows = split_left("di,irc->drc", w_bwd, got[:, share : 2 * share])
    back = lax.all_to_all(
        jnp.concatenate([state_rows, adjoint_rows], axis=1).astype(jnp.bfloat16),
        axis,
        0,
        0,
        tiled=True,
    )
    start_state = widen(back[:, :share]).reshape(heads, width, width)
    start_adjoint = widen(back[:, share:]).reshape(heads, width, width)
    return start_state, start_adjoint, riders


def running_sum(decay_blk):
    length = decay_blk.shape[1]
    lower = (
        lax.broadcasted_iota(jnp.int32, (length, length), 1)
        <= lax.broadcasted_iota(jnp.int32, (length, length), 0)
    ).astype(decay_blk.dtype)
    return jnp.einsum("ts,nsh->nth", lower, decay_blk, preferred_element_type=jnp.float32)


def within_group(totals, pieces, reverse):
    blocks = totals.shape[0]
    at = lax.broadcasted_iota(jnp.int32, (blocks, blocks, blocks), 0)
    src = lax.broadcasted_iota(jnp.int32, (blocks, blocks, blocks), 1)
    mid = lax.broadcasted_iota(jnp.int32, (blocks, blocks, blocks), 2)
    between = ((at < mid) & (mid < src)) if reverse else ((src < mid) & (mid < at))
    logs = jnp.sum(jnp.where(between[..., None], totals[None, None], 0.0), axis=2)
    pos = lax.broadcasted_iota(jnp.int32, (blocks, blocks), 0)
    other = lax.broadcasted_iota(jnp.int32, (blocks, blocks), 1)
    earlier = (other > pos) if reverse else (other < pos)
    later = (other < pos) if reverse else (other > pos)
    weights = jnp.where(earlier[..., None], jnp.exp(jnp.where(earlier[..., None], logs, 0.0)), 0.0)
    seen_log = jnp.sum(jnp.where(earlier[..., None], totals[None], 0.0), axis=1)
    tail_log = jnp.sum(jnp.where(later[..., None], totals[None], 0.0), axis=1)
    seen = split_left("ijh,jhab->ihab", weights, pieces)
    whole = split_left("jh,jhab->hab", jnp.exp(tail_log), pieces)
    return seen, seen_log, whole, jnp.sum(totals, axis=0)


def local_block(queries, keys, values, out_grad, log_decay):
    length = queries.shape[0]
    heads = log_decay.shape[1]
    width = queries.shape[1] // heads
    query_blk = queries.reshape(length, heads, width)
    key_blk = keys.reshape(length, heads, width)
    value_blk = values.reshape(length, heads, width)
    grad_blk = out_grad.reshape(length, heads, width)
    cumul = running_sum(log_decay[None])[0]
    total = cumul[-1]
    after = jnp.exp(total[None, :] - cumul)
    before = jnp.exp(cumul)
    contrib = split_left("sha,shb->hab", after[..., None] * widen(key_blk), value_blk)
    update = split_left("tha,thb->hab", before[..., None] * widen(query_blk), grad_blk)
    return (query_blk, key_blk, value_blk, grad_blk, cumul, after, before, contrib, update)


def intra(query_blk, key_blk, value_blk, grad_blk, cumul):
    length = cumul.shape[0]
    heads_first = cumul.T
    spread = heads_first[:, :, None] - heads_first[:, None, :]
    causal = lax.broadcasted_iota(jnp.int32, (length, length), 1) <= lax.broadcasted_iota(
        jnp.int32, (length, length), 0
    )
    weights = jnp.where(causal[None], jnp.exp(jnp.where(causal[None], spread, 0.0)), 0.0)
    grad_scores = product("thd,shd->hts", grad_blk, value_blk)
    key_scores = product("thd,shd->hts", query_blk, key_blk)
    first = (weights * grad_scores).astype(jnp.bfloat16)
    second = (weights * key_scores).astype(jnp.bfloat16)
    query_part = product("hts,shd->htd", first, key_blk)
    key_part = product("hts,thd->hsd", first, query_blk)
    value_part = product("hts,thd->hsd", second, grad_blk)
    return query_part, key_part, value_part


def finish_kernel(
    grad_ref, value_ref, key_ref, state_ref, adjoint_ref, qp_ref, kp_ref, vp_ref, before_ref,
    after_ref, gq_ref, gk_ref, gv_ref,
):
    group, width = state_ref.shape[0], state_ref.shape[2]
    back = (((1,), (1,)), ((), ()))
    step = pl.program_id(0)
    lanes = lax.broadcasted_iota(jnp.int32, before_ref.shape, 1)
    before_all = before_ref[...]
    after_all = after_ref[...]
    for i in range(group):
        cols = slice(i * width, (i + 1) * width)
        head = step * group + i
        before = jnp.sum(jnp.where(lanes == head, before_all, 0.0), axis=1, keepdims=True)
        after = jnp.sum(jnp.where(lanes == head, after_all, 0.0), axis=1, keepdims=True)
        grad = grad_ref[:, cols]
        value = value_ref[:, cols]
        key = key_ref[:, cols]
        state = state_ref[i]
        adjoint = adjoint_ref[i]
        with_state = lax.dot_general(grad, state, back, preferred_element_type=jnp.float32)
        with_adjoint_v = lax.dot_general(value, adjoint, back, preferred_element_type=jnp.float32)
        with_adjoint_k = jnp.dot(key, adjoint, preferred_element_type=jnp.float32)
        gq_ref[:, cols] = (qp_ref[i] + before * with_state).astype(gq_ref.dtype)
        gk_ref[:, cols] = (kp_ref[i] + after * with_adjoint_v).astype(gk_ref.dtype)
        gv_ref[:, cols] = (vp_ref[i] + after * with_adjoint_k).astype(gv_ref.dtype)


def finish_call(out_grad, values, keys, state_in, adjoint_in, qp, kp, vp, before, after):
    length, columns = out_grad.shape
    heads, width = state_in.shape[0], state_in.shape[2]
    group = 4
    steps = heads // group
    flat_spec = pl.BlockSpec((length, group * width), lambda h: (0, h))
    head_spec = pl.BlockSpec((group, width, width), lambda h: (h, 0, 0))
    part_spec = pl.BlockSpec((group, length, width), lambda h: (h, 0, 0))
    scale_spec = pl.BlockSpec((length, heads), lambda h: (0, 0))
    out = jax.ShapeDtypeStruct((length, columns), jnp.bfloat16)
    return pl.pallas_call(
        finish_kernel,
        grid=(steps,),
        in_specs=[flat_spec, flat_spec, flat_spec, head_spec, head_spec, part_spec, part_spec,
                  part_spec, scale_spec, scale_spec],
        out_specs=[flat_spec, flat_spec, flat_spec],
        out_shape=[out, out, out],
    )(out_grad, values, keys, state_in, adjoint_in, qp, kp, vp, before, after)


def body(queries, keys, values, out_grad, log_decay):
    peers = lax.axis_size("exp")
    length = queries.shape[0]
    heads = log_decay.shape[1]
    width = queries.shape[1] // heads
    group = heads // peers
    (query_blk, key_blk, value_blk, grad_blk, cumul, after, before, contrib, update) = local_block(
        queries, keys, values, out_grad, log_decay
    )
    share = group * width
    decay_rows = jnp.transpose(log_decay.reshape(length, peers, group), (1, 2, 0))
    pad_rows = 16
    decay_rows = jnp.pad(decay_rows, ((0, 0), (0, pad_rows - group), (0, 0)))
    packed = jnp.concatenate(
        [
            contrib.astype(jnp.bfloat16).reshape(peers, share, width),
            update.astype(jnp.bfloat16).reshape(peers, share, width),
            decay_rows.astype(jnp.bfloat16),
        ],
        axis=1,
    )
    got = lax.all_to_all(packed, "exp", 0, 0, tiled=True)
    contrib_g = got[:, :share].reshape(peers, group, width, width)
    update_g = got[:, share : 2 * share].reshape(peers, group, width, width)
    totals = jnp.sum(widen(got[:, 2 * share : 2 * share + group]), axis=2)
    query_part, key_part, value_part = intra(query_blk, key_blk, value_blk, grad_blk, cumul)
    totals, contrib_g, update_g, query_part, key_part, value_part = lax.optimization_barrier(
        (totals, contrib_g, update_g, query_part, key_part, value_part)
    )
    prefix, prefix_log, dev_state, dev_log = within_group(totals, contrib_g, False)
    suffix, suffix_log, dev_adjoint, unused = within_group(totals, update_g, True)
    start_state, start_adjoint, (prefix, suffix) = carried_both(
        dev_log, dev_state, dev_adjoint, "seq", (prefix, suffix)
    )
    state_prev = jnp.exp(prefix_log)[:, :, None, None] * start_state[None] + prefix
    adjoint = jnp.exp(suffix_log)[:, :, None, None] * start_adjoint[None] + suffix
    returned = jnp.concatenate(
        [
            state_prev.astype(jnp.bfloat16).reshape(peers, share, width),
            adjoint.astype(jnp.bfloat16).reshape(peers, share, width),
        ],
        axis=1,
    )
    back = lax.all_to_all(returned, "exp", 0, 0, tiled=True)
    state_in = back[:, :share].reshape(heads, width, width)
    adjoint_in = back[:, share:].reshape(heads, width, width)
    grad_query, grad_key, grad_value = finish_call(
        out_grad, values, keys, state_in, adjoint_in, query_part, key_part, value_part,
        before, after,
    )
    return (grad_query, grad_key, grad_value)


def solution(mesh):
    placed = tuple(P(SEQ_EXP, None) for _ in range(5))
    return jax.shard_map(
        body,
        mesh=mesh,
        in_specs=placed,
        out_specs=(P(SEQ_EXP, None), P(SEQ_EXP, None), P(SEQ_EXP, None)),
        check_vma=False,
    )
```

```python
import jax
import jax.numpy as jnp
from jax import lax
from jax.sharding import PartitionSpec as P
from jax.experimental import pallas as pl

BLOCK = 128
SEQ_EXP = ("seq", "exp")


def widen(array):
    return array.astype(jnp.float32)


def halves(array):
    rounded = lax.reduce_precision(array, exponent_bits=8, mantissa_bits=7)
    low = (array - rounded).astype(jnp.bfloat16)
    return (rounded.astype(jnp.bfloat16), low)


def product(form, first_op, second_op):
    return jnp.einsum(form, first_op, second_op, preferred_element_type=jnp.float32)


def split_left(form, wide_op, narrow_op):
    high, low = halves(wide_op)
    return product(form, high, narrow_op) + product(form, low, narrow_op)


def split_right(form, narrow_op, wide_op):
    high, low = halves(wide_op)
    return product(form, narrow_op, high) + product(form, narrow_op, low)


def link(earlier, later):
    return (earlier[0] + later[0], jnp.exp(later[0])[:, None, None] * earlier[1] + later[1])


def pieces_of(array):
    high = lax.reduce_precision(array, exponent_bits=8, mantissa_bits=7)
    rest = array - high
    mid = lax.reduce_precision(rest, exponent_bits=8, mantissa_bits=7)
    low = (rest - mid).astype(jnp.bfloat16)
    return high.astype(jnp.bfloat16), mid.astype(jnp.bfloat16), low


def carried_both(dev_log, dev_state, dev_adjoint, axis, riders):
    peers = lax.axis_size(axis)
    here = lax.axis_index(axis)
    heads, width = dev_state.shape[0], dev_state.shape[2]
    share = heads * width // peers
    spare = 16
    logs = jnp.zeros((spare, width), jnp.bfloat16)
    for i, part in enumerate(pieces_of(dev_log)):
        logs = logs.at[i * heads : (i + 1) * heads, :].set(
            jnp.broadcast_to(part[:, None], (heads, width))
        )
    payload = jnp.concatenate(
        [
            dev_state.astype(jnp.bfloat16).reshape(peers, share, width),
            dev_adjoint.astype(jnp.bfloat16).reshape(peers, share, width),
            jnp.broadcast_to(logs[None], (peers, spare, width)),
        ],
        axis=1,
    )
    got = lax.all_to_all(payload, axis, 0, 0, tiled=True)
    got, riders = lax.optimization_barrier((got, riders))
    head = (here * share) // width
    pick = (lax.broadcasted_iota(jnp.int32, (heads,), 0) == head).astype(jnp.float32)
    log_rows = jnp.max(widen(got[:, 2 * share : 2 * share + 3 * heads, :]), axis=2)
    log_rows = log_rows.reshape(peers, 3, heads)
    totals = jnp.sum(log_rows[:, 0] * pick[None, :], axis=1)
    totals = totals + jnp.sum(log_rows[:, 1] * pick[None, :], axis=1)
    totals = totals + jnp.sum(log_rows[:, 2] * pick[None, :], axis=1)
    dst = lax.broadcasted_iota(jnp.int32, (peers, peers, peers), 0)
    src = lax.broadcasted_iota(jnp.int32, (peers, peers, peers), 1)
    mid = lax.broadcasted_iota(jnp.int32, (peers, peers, peers), 2)
    between_fwd = (src < mid) & (mid < dst)
    between_bwd = (dst < mid) & (mid < src)
    log_fwd = jnp.sum(jnp.where(between_fwd, totals[None, None, :], 0.0), axis=2)
    log_bwd = jnp.sum(jnp.where(between_bwd, totals[None, None, :], 0.0), axis=2)
    dst2 = lax.broadcasted_iota(jnp.int32, (peers, peers), 0)
    src2 = lax.broadcasted_iota(jnp.int32, (peers, peers), 1)
    w_fwd = jnp.where(src2 < dst2, jnp.exp(jnp.where(src2 < dst2, log_fwd, 0.0)), 0.0)
    w_bwd = jnp.where(src2 > dst2, jnp.exp(jnp.where(src2 > dst2, log_bwd, 0.0)), 0.0)
    state_rows = split_left("di,irc->drc", w_fwd, got[:, :share])
    adjoint_rows = split_left("di,irc->drc", w_bwd, got[:, share : 2 * share])
    back = lax.all_to_all(
        jnp.concatenate([state_rows, adjoint_rows], axis=1).astype(jnp.bfloat16),
        axis,
        0,
        0,
        tiled=True,
    )
    start_state = widen(back[:, :share]).reshape(heads, width, width)
    start_adjoint = widen(back[:, share:]).reshape(heads, width, width)
    return start_state, start_adjoint, riders


def running_sum(decay_blk):
    length = decay_blk.shape[1]
    lower = (
        lax.broadcasted_iota(jnp.int32, (length, length), 1)
        <= lax.broadcasted_iota(jnp.int32, (length, length), 0)
    ).astype(decay_blk.dtype)
    return jnp.einsum("ts,nsh->nth", lower, decay_blk, preferred_element_type=jnp.float32)


def within_group(totals, pieces, reverse):
    blocks = totals.shape[0]
    at = lax.broadcasted_iota(jnp.int32, (blocks, blocks, blocks), 0)
    src = lax.broadcasted_iota(jnp.int32, (blocks, blocks, blocks), 1)
    mid = lax.broadcasted_iota(jnp.int32, (blocks, blocks, blocks), 2)
    between = ((at < mid) & (mid < src)) if reverse else ((src < mid) & (mid < at))
    logs = jnp.sum(jnp.where(between[..., None], totals[None, None], 0.0), axis=2)
    pos = lax.broadcasted_iota(jnp.int32, (blocks, blocks), 0)
    other = lax.broadcasted_iota(jnp.int32, (blocks, blocks), 1)
    earlier = (other > pos) if reverse else (other < pos)
    later = (other < pos) if reverse else (other > pos)
    weights = jnp.where(earlier[..., None], jnp.exp(jnp.where(earlier[..., None], logs, 0.0)), 0.0)
    seen_log = jnp.sum(jnp.where(earlier[..., None], totals[None], 0.0), axis=1)
    tail_log = jnp.sum(jnp.where(later[..., None], totals[None], 0.0), axis=1)
    seen = split_left("ijh,jhab->ihab", weights, pieces)
    whole = split_left("jh,jhab->hab", jnp.exp(tail_log), pieces)
    return seen, seen_log, whole, jnp.sum(totals, axis=0)


def local_block(queries, keys, values, out_grad, log_decay):
    length = queries.shape[0]
    heads = log_decay.shape[1]
    width = queries.shape[1] // heads
    query_blk = queries.reshape(length, heads, width)
    key_blk = keys.reshape(length, heads, width)
    value_blk = values.reshape(length, heads, width)
    grad_blk = out_grad.reshape(length, heads, width)
    cumul = running_sum(log_decay[None])[0]
    total = cumul[-1]
    after = jnp.exp(total[None, :] - cumul)
    before = jnp.exp(cumul)
    contrib = split_left("sha,shb->hab", after[..., None] * widen(key_blk), value_blk)
    update = split_left("tha,thb->hab", before[..., None] * widen(query_blk), grad_blk)
    return (query_blk, key_blk, value_blk, grad_blk, cumul, after, before, contrib, update)


def intra(query_blk, key_blk, value_blk, grad_blk, cumul):
    length = cumul.shape[0]
    heads_first = cumul.T
    spread = heads_first[:, :, None] - heads_first[:, None, :]
    causal = lax.broadcasted_iota(jnp.int32, (length, length), 1) <= lax.broadcasted_iota(
        jnp.int32, (length, length), 0
    )
    weights = jnp.where(causal[None], jnp.exp(jnp.where(causal[None], spread, 0.0)), 0.0)
    grad_scores = product("thd,shd->hts", grad_blk, value_blk)
    key_scores = product("thd,shd->hts", query_blk, key_blk)
    first = (weights * grad_scores).astype(jnp.bfloat16)
    second = (weights * key_scores).astype(jnp.bfloat16)
    query_part = product("hts,shd->htd", first, key_blk)
    key_part = product("hts,thd->hsd", first, query_blk)
    value_part = product("hts,thd->hsd", second, grad_blk)
    return query_part, key_part, value_part


def finish_kernel(
    grad_ref, value_ref, key_ref, state_ref, adjoint_ref, qp_ref, kp_ref, vp_ref, before_ref,
    after_ref, gq_ref, gk_ref, gv_ref,
):
    group, width = state_ref.shape[0], state_ref.shape[2]
    back = (((1,), (1,)), ((), ()))
    step = pl.program_id(0)
    lanes = lax.broadcasted_iota(jnp.int32, before_ref.shape, 1)
    before_all = before_ref[...]
    after_all = after_ref[...]
    for i in range(group):
        cols = slice(i * width, (i + 1) * width)
        head = step * group + i
        before = jnp.sum(jnp.where(lanes == head, before_all, 0.0), axis=1, keepdims=True)
        after = jnp.sum(jnp.where(lanes == head, after_all, 0.0), axis=1, keepdims=True)
        grad = grad_ref[:, cols]
        value = value_ref[:, cols]
        key = key_ref[:, cols]
        state = state_ref[i]
        adjoint = adjoint_ref[i]
        with_state = lax.dot_general(grad, state, back, preferred_element_type=jnp.float32)
        with_adjoint_v = lax.dot_general(value, adjoint, back, preferred_element_type=jnp.float32)
        with_adjoint_k = jnp.dot(key, adjoint, preferred_element_type=jnp.float32)
        gq_ref[:, cols] = (qp_ref[i] + before * with_state).astype(gq_ref.dtype)
        gk_ref[:, cols] = (kp_ref[i] + after * with_adjoint_v).astype(gk_ref.dtype)
        gv_ref[:, cols] = (vp_ref[i] + after * with_adjoint_k).astype(gv_ref.dtype)


def finish_call(out_grad, values, keys, state_in, adjoint_in, qp, kp, vp, before, after):
    length, columns = out_grad.shape
    heads, width = state_in.shape[0], state_in.shape[2]
    group = 4
    steps = heads // group
    flat_spec = pl.BlockSpec((length, group * width), lambda h: (0, h))
    head_spec = pl.BlockSpec((group, width, width), lambda h: (h, 0, 0))
    part_spec = pl.BlockSpec((group, length, width), lambda h: (h, 0, 0))
    scale_spec = pl.BlockSpec((length, heads), lambda h: (0, 0))
    out = jax.ShapeDtypeStruct((length, columns), jnp.bfloat16)
    return pl.pallas_call(
        finish_kernel,
        grid=(steps,),
        in_specs=[flat_spec, flat_spec, flat_spec, head_spec, head_spec, part_spec, part_spec,
                  part_spec, scale_spec, scale_spec],
        out_specs=[flat_spec, flat_spec, flat_spec],
        out_shape=[out, out, out],
    )(out_grad, values, keys, state_in, adjoint_in, qp, kp, vp, before, after)


def body(queries, keys, values, out_grad, log_decay):
    peers = lax.axis_size("exp")
    length = queries.shape[0]
    heads = log_decay.shape[1]
    width = queries.shape[1] // heads
    group = heads // peers
    (query_blk, key_blk, value_blk, grad_blk, cumul, after, before, contrib, update) = local_block(
        queries, keys, values, out_grad, log_decay
    )
    share = group * width
    decay_rows = jnp.transpose(log_decay.reshape(length, peers, group), (1, 2, 0))
    pad_rows = 16
    decay_rows = jnp.pad(decay_rows, ((0, 0), (0, pad_rows - group), (0, 0)))
    packed = jnp.concatenate(
        [
            contrib.astype(jnp.bfloat16).reshape(peers, share, width),
            update.astype(jnp.bfloat16).reshape(peers, share, width),
            decay_rows.astype(jnp.bfloat16),
        ],
        axis=1,
    )
    got = lax.all_to_all(packed, "exp", 0, 0, tiled=True)
    contrib_g = got[:, :share].reshape(peers, group, width, width)
    update_g = got[:, share : 2 * share].reshape(peers, group, width, width)
    totals = jnp.sum(widen(got[:, 2 * share : 2 * share + group]), axis=2)
    query_part, key_part, value_part = intra(query_blk, key_blk, value_blk, grad_blk, cumul)
    totals, contrib_g, update_g, query_part, key_part, value_part = lax.optimization_barrier(
        (totals, contrib_g, update_g, query_part, key_part, value_part)
    )
    prefix, prefix_log, dev_state, dev_log = within_group(totals, contrib_g, False)
    suffix, suffix_log, dev_adjoint, unused = within_group(totals, update_g, True)
    start_state, start_adjoint, (prefix, suffix) = carried_both(
        dev_log, dev_state, dev_adjoint, "seq", (prefix, suffix)
    )
    state_prev = jnp.exp(prefix_log)[:, :, None, None] * start_state[None] + prefix
    adjoint = jnp.exp(suffix_log)[:, :, None, None] * start_adjoint[None] + suffix
    returned = jnp.concatenate(
        [
            state_prev.astype(jnp.bfloat16).reshape(peers, share, width),
            adjoint.astype(jnp.bfloat16).reshape(peers, share, width),
        ],
        axis=1,
    )
    back = lax.all_to_all(returned, "exp", 0, 0, tiled=True)
    state_in = back[:, :share].reshape(heads, width, width)
    adjoint_in = back[:, share:].reshape(heads, width, width)
    grad_query, grad_key, grad_value = finish_call(
        out_grad, values, keys, state_in, adjoint_in, query_part, key_part, value_part,
        before, after,
    )
    return (grad_query, grad_key, grad_value)


def solution(mesh):
    placed = tuple(P(SEQ_EXP, None) for _ in range(5))
    return jax.shard_map(
        body,
        mesh=mesh,
        in_specs=placed,
        out_specs=(P(SEQ_EXP, None), P(SEQ_EXP, None), P(SEQ_EXP, None)),
        check_vma=False,
    )
```

```python
import jax
import jax.numpy as jnp
from jax import lax
from jax.sharding import PartitionSpec as P
from jax.experimental import pallas as pl

BLOCK = 128
SEQ_EXP = ("seq", "exp")


def widen(array):
    return array.astype(jnp.float32)


def halves(array):
    rounded = lax.reduce_precision(array, exponent_bits=8, mantissa_bits=7)
    low = (array - rounded).astype(jnp.bfloat16)
    return (rounded.astype(jnp.bfloat16), low)


def product(form, first_op, second_op):
    return jnp.einsum(form, first_op, second_op, preferred_element_type=jnp.float32)


def split_left(form, wide_op, narrow_op):
    high, low = halves(wide_op)
    return product(form, high, narrow_op) + product(form, low, narrow_op)


def split_right(form, narrow_op, wide_op):
    high, low = halves(wide_op)
    return product(form, narrow_op, high) + product(form, narrow_op, low)


def link(earlier, later):
    return (earlier[0] + later[0], jnp.exp(later[0])[:, None, None] * earlier[1] + later[1])


def pieces_of(array):
    high = lax.reduce_precision(array, exponent_bits=8, mantissa_bits=7)
    rest = array - high
    mid = lax.reduce_precision(rest, exponent_bits=8, mantissa_bits=7)
    low = (rest - mid).astype(jnp.bfloat16)
    return high.astype(jnp.bfloat16), mid.astype(jnp.bfloat16), low


def carried_both(dev_log, dev_state, dev_adjoint, axis, riders):
    peers = lax.axis_size(axis)
    here = lax.axis_index(axis)
    heads, width = dev_state.shape[0], dev_state.shape[2]
    share = heads * width // peers
    spare = 16
    logs = jnp.zeros((spare, width), jnp.bfloat16)
    for i, part in enumerate(pieces_of(dev_log)):
        logs = logs.at[i * heads : (i + 1) * heads, :].set(
            jnp.broadcast_to(part[:, None], (heads, width))
        )
    payload = jnp.concatenate(
        [
            dev_state.astype(jnp.bfloat16).reshape(peers, share, width),
            dev_adjoint.astype(jnp.bfloat16).reshape(peers, share, width),
            jnp.broadcast_to(logs[None], (peers, spare, width)),
        ],
        axis=1,
    )
    got = lax.all_to_all(payload, axis, 0, 0, tiled=True)
    got, riders = lax.optimization_barrier((got, riders))
    head = (here * share) // width
    pick = (lax.broadcasted_iota(jnp.int32, (heads,), 0) == head).astype(jnp.float32)
    log_rows = jnp.max(widen(got[:, 2 * share : 2 * share + 3 * heads, :]), axis=2)
    log_rows = log_rows.reshape(peers, 3, heads)
    totals = jnp.sum(log_rows[:, 0] * pick[None, :], axis=1)
    totals = totals + jnp.sum(log_rows[:, 1] * pick[None, :], axis=1)
    totals = totals + jnp.sum(log_rows[:, 2] * pick[None, :], axis=1)
    dst = lax.broadcasted_iota(jnp.int32, (peers, peers, peers), 0)
    src = lax.broadcasted_iota(jnp.int32, (peers, peers, peers), 1)
    mid = lax.broadcasted_iota(jnp.int32, (peers, peers, peers), 2)
    between_fwd = (src < mid) & (mid < dst)
    between_bwd = (dst < mid) & (mid < src)
    log_fwd = jnp.sum(jnp.where(between_fwd, totals[None, None, :], 0.0), axis=2)
    log_bwd = jnp.sum(jnp.where(between_bwd, totals[None, None, :], 0.0), axis=2)
    dst2 = lax.broadcasted_iota(jnp.int32, (peers, peers), 0)
    src2 = lax.broadcasted_iota(jnp.int32, (peers, peers), 1)
    w_fwd = jnp.where(src2 < dst2, jnp.exp(jnp.where(src2 < dst2, log_fwd, 0.0)), 0.0)
    w_bwd = jnp.where(src2 > dst2, jnp.exp(jnp.where(src2 > dst2, log_bwd, 0.0)), 0.0)
    state_rows = split_left("di,irc->drc", w_fwd, got[:, :share])
    adjoint_rows = split_left("di,irc->drc", w_bwd, got[:, share : 2 * share])
    back = lax.all_to_all(
        jnp.concatenate([state_rows, adjoint_rows], axis=1).astype(jnp.bfloat16),
        axis,
        0,
        0,
        tiled=True,
    )
    start_state = widen(back[:, :share]).reshape(heads, width, width)
    start_adjoint = widen(back[:, share:]).reshape(heads, width, width)
    return start_state, start_adjoint, riders


def running_sum(decay_blk):
    length = decay_blk.shape[1]
    lower = (
        lax.broadcasted_iota(jnp.int32, (length, length), 1)
        <= lax.broadcasted_iota(jnp.int32, (length, length), 0)
    ).astype(decay_blk.dtype)
    return jnp.einsum("ts,nsh->nth", lower, decay_blk, preferred_element_type=jnp.float32)


def within_group(totals, pieces, reverse):
    blocks = totals.shape[0]
    at = lax.broadcasted_iota(jnp.int32, (blocks, blocks, blocks), 0)
    src = lax.broadcasted_iota(jnp.int32, (blocks, blocks, blocks), 1)
    mid = lax.broadcasted_iota(jnp.int32, (blocks, blocks, blocks), 2)
    between = ((at < mid) & (mid < src)) if reverse else ((src < mid) & (mid < at))
    logs = jnp.sum(jnp.where(between[..., None], totals[None, None], 0.0), axis=2)
    pos = lax.broadcasted_iota(jnp.int32, (blocks, blocks), 0)
    other = lax.broadcasted_iota(jnp.int32, (blocks, blocks), 1)
    earlier = (other > pos) if reverse else (other < pos)
    later = (other < pos) if reverse else (other > pos)
    weights = jnp.where(earlier[..., None], jnp.exp(jnp.where(earlier[..., None], logs, 0.0)), 0.0)
    seen_log = jnp.sum(jnp.where(earlier[..., None], totals[None], 0.0), axis=1)
    tail_log = jnp.sum(jnp.where(later[..., None], totals[None], 0.0), axis=1)
    seen = split_left("ijh,jhab->ihab", weights, pieces)
    whole = split_left("jh,jhab->hab", jnp.exp(tail_log), pieces)
    return seen, seen_log, whole, jnp.sum(totals, axis=0)


def local_block(queries, keys, values, out_grad, log_decay):
    length = queries.shape[0]
    heads = log_decay.shape[1]
    width = queries.shape[1] // heads
    query_blk = queries.reshape(length, heads, width)
    key_blk = keys.reshape(length, heads, width)
    value_blk = values.reshape(length, heads, width)
    grad_blk = out_grad.reshape(length, heads, width)
    cumul = running_sum(log_decay[None])[0]
    total = cumul[-1]
    after = jnp.exp(total[None, :] - cumul)
    before = jnp.exp(cumul)
    contrib = split_left("sha,shb->hab", after[..., None] * widen(key_blk), value_blk)
    update = split_left("tha,thb->hab", before[..., None] * widen(query_blk), grad_blk)
    return (query_blk, key_blk, value_blk, grad_blk, cumul, after, before, contrib, update)


def intra(query_blk, key_blk, value_blk, grad_blk, cumul):
    length = cumul.shape[0]
    heads_first = cumul.T
    spread = heads_first[:, :, None] - heads_first[:, None, :]
    causal = lax.broadcasted_iota(jnp.int32, (length, length), 1) <= lax.broadcasted_iota(
        jnp.int32, (length, length), 0
    )
    weights = jnp.where(causal[None], jnp.exp(jnp.where(causal[None], spread, 0.0)), 0.0)
    grad_scores = product("thd,shd->hts", grad_blk, value_blk)
    key_scores = product("thd,shd->hts", query_blk, key_blk)
    first = (weights * grad_scores).astype(jnp.bfloat16)
    second = (weights * key_scores).astype(jnp.bfloat16)
    query_part = product("hts,shd->htd", first, key_blk)
    key_part = product("hts,thd->hsd", first, query_blk)
    value_part = product("hts,thd->hsd", second, grad_blk)
    return query_part, key_part, value_part


def finish_kernel(
    grad_ref, value_ref, key_ref, state_ref, adjoint_ref, qp_ref, kp_ref, vp_ref, before_ref,
    after_ref, gq_ref, gk_ref, gv_ref,
):
    group, width = state_ref.shape[0], state_ref.shape[2]
    back = (((1,), (1,)), ((), ()))
    step = pl.program_id(0)
    lanes = lax.broadcasted_iota(jnp.int32, before_ref.shape, 1)
    before_all = before_ref[...]
    after_all = after_ref[...]
    for i in range(group):
        cols = slice(i * width, (i + 1) * width)
        head = step * group + i
        before = jnp.sum(jnp.where(lanes == head, before_all, 0.0), axis=1, keepdims=True)
        after = jnp.sum(jnp.where(lanes == head, after_all, 0.0), axis=1, keepdims=True)
        grad = grad_ref[:, cols]
        value = value_ref[:, cols]
        key = key_ref[:, cols]
        state = state_ref[i]
        adjoint = adjoint_ref[i]
        with_state = lax.dot_general(grad, state, back, preferred_element_type=jnp.float32)
        with_adjoint_v = lax.dot_general(value, adjoint, back, preferred_element_type=jnp.float32)
        with_adjoint_k = jnp.dot(key, adjoint, preferred_element_type=jnp.float32)
        gq_ref[:, cols] = (qp_ref[i] + before * with_state).astype(gq_ref.dtype)
        gk_ref[:, cols] = (kp_ref[i] + after * with_adjoint_v).astype(gk_ref.dtype)
        gv_ref[:, cols] = (vp_ref[i] + after * with_adjoint_k).astype(gv_ref.dtype)


def finish_call(out_grad, values, keys, state_in, adjoint_in, qp, kp, vp, before, after):
    length, columns = out_grad.shape
    heads, width = state_in.shape[0], state_in.shape[2]
    group = 8
    steps = heads // group
    flat_spec = pl.BlockSpec((length, group * width), lambda h: (0, h))
    head_spec = pl.BlockSpec((group, width, width), lambda h: (h, 0, 0))
    part_spec = pl.BlockSpec((group, length, width), lambda h: (h, 0, 0))
    scale_spec = pl.BlockSpec((length, heads), lambda h: (0, 0))
    out = jax.ShapeDtypeStruct((length, columns), jnp.bfloat16)
    return pl.pallas_call(
        finish_kernel,
        grid=(steps,),
        in_specs=[flat_spec, flat_spec, flat_spec, head_spec, head_spec, part_spec, part_spec,
                  part_spec, scale_spec, scale_spec],
        out_specs=[flat_spec, flat_spec, flat_spec],
        out_shape=[out, out, out],
    )(out_grad, values, keys, state_in, adjoint_in, qp, kp, vp, before, after)


def body(queries, keys, values, out_grad, log_decay):
    peers = lax.axis_size("exp")
    length = queries.shape[0]
    heads = log_decay.shape[1]
    width = queries.shape[1] // heads
    group = heads // peers
    (query_blk, key_blk, value_blk, grad_blk, cumul, after, before, contrib, update) = local_block(
        queries, keys, values, out_grad, log_decay
    )
    share = group * width
    decay_rows = jnp.transpose(log_decay.reshape(length, peers, group), (1, 2, 0))
    pad_rows = 16
    decay_rows = jnp.pad(decay_rows, ((0, 0), (0, pad_rows - group), (0, 0)))
    packed = jnp.concatenate(
        [
            contrib.astype(jnp.bfloat16).reshape(peers, share, width),
            update.astype(jnp.bfloat16).reshape(peers, share, width),
            decay_rows.astype(jnp.bfloat16),
        ],
        axis=1,
    )
    got = lax.all_to_all(packed, "exp", 0, 0, tiled=True)
    contrib_g = got[:, :share].reshape(peers, group, width, width)
    update_g = got[:, share : 2 * share].reshape(peers, group, width, width)
    totals = jnp.sum(widen(got[:, 2 * share : 2 * share + group]), axis=2)
    query_part, key_part, value_part = intra(query_blk, key_blk, value_blk, grad_blk, cumul)
    totals, contrib_g, update_g, query_part, key_part, value_part = lax.optimization_barrier(
        (totals, contrib_g, update_g, query_part, key_part, value_part)
    )
    prefix, prefix_log, dev_state, dev_log = within_group(totals, contrib_g, False)
    suffix, suffix_log, dev_adjoint, unused = within_group(totals, update_g, True)
    start_state, start_adjoint, (prefix, suffix) = carried_both(
        dev_log, dev_state, dev_adjoint, "seq", (prefix, suffix)
    )
    state_prev = jnp.exp(prefix_log)[:, :, None, None] * start_state[None] + prefix
    adjoint = jnp.exp(suffix_log)[:, :, None, None] * start_adjoint[None] + suffix
    returned = jnp.concatenate(
        [
            state_prev.astype(jnp.bfloat16).reshape(peers, share, width),
            adjoint.astype(jnp.bfloat16).reshape(peers, share, width),
        ],
        axis=1,
    )
    back = lax.all_to_all(returned, "exp", 0, 0, tiled=True)
    state_in = back[:, :share].reshape(heads, width, width)
    adjoint_in = back[:, share:].reshape(heads, width, width)
    grad_query, grad_key, grad_value = finish_call(
        out_grad, values, keys, state_in, adjoint_in, query_part, key_part, value_part,
        before, after,
    )
    return (grad_query, grad_key, grad_value)


def solution(mesh):
    placed = tuple(P(SEQ_EXP, None) for _ in range(5))
    return jax.shard_map(
        body,
        mesh=mesh,
        in_specs=placed,
        out_specs=(P(SEQ_EXP, None), P(SEQ_EXP, None), P(SEQ_EXP, None)),
        check_vma=False,
    )
```

```python
import jax
import jax.numpy as jnp
from jax import lax
from jax.sharding import PartitionSpec as P
from jax.experimental import pallas as pl

BLOCK = 128
SEQ_EXP = ("seq", "exp")


def widen(array):
    return array.astype(jnp.float32)


def halves(array):
    rounded = lax.reduce_precision(array, exponent_bits=8, mantissa_bits=7)
    low = (array - rounded).astype(jnp.bfloat16)
    return (rounded.astype(jnp.bfloat16), low)


def product(form, first_op, second_op):
    return jnp.einsum(form, first_op, second_op, preferred_element_type=jnp.float32)


def split_left(form, wide_op, narrow_op):
    high, low = halves(wide_op)
    return product(form, high, narrow_op) + product(form, low, narrow_op)


def split_right(form, narrow_op, wide_op):
    high, low = halves(wide_op)
    return product(form, narrow_op, high) + product(form, narrow_op, low)


def link(earlier, later):
    return (earlier[0] + later[0], jnp.exp(later[0])[:, None, None] * earlier[1] + later[1])


def pieces_of(array):
    high = lax.reduce_precision(array, exponent_bits=8, mantissa_bits=7)
    rest = array - high
    mid = lax.reduce_precision(rest, exponent_bits=8, mantissa_bits=7)
    low = (rest - mid).astype(jnp.bfloat16)
    return high.astype(jnp.bfloat16), mid.astype(jnp.bfloat16), low


def carried_both(dev_log, dev_state, dev_adjoint, axis, riders):
    peers = lax.axis_size(axis)
    here = lax.axis_index(axis)
    heads, width = dev_state.shape[0], dev_state.shape[2]
    share = heads * width // peers
    spare = 16
    logs = jnp.zeros((spare, width), jnp.bfloat16)
    for i, part in enumerate(pieces_of(dev_log)):
        logs = logs.at[i * heads : (i + 1) * heads, :].set(
            jnp.broadcast_to(part[:, None], (heads, width))
        )
    payload = jnp.concatenate(
        [
            dev_state.astype(jnp.bfloat16).reshape(peers, share, width),
            dev_adjoint.astype(jnp.bfloat16).reshape(peers, share, width),
            jnp.broadcast_to(logs[None], (peers, spare, width)),
        ],
        axis=1,
    )
    got = lax.all_to_all(payload, axis, 0, 0, tiled=True)
    got, riders = lax.optimization_barrier((got, riders))
    head = (here * share) // width
    pick = (lax.broadcasted_iota(jnp.int32, (heads,), 0) == head).astype(jnp.float32)
    log_rows = jnp.max(widen(got[:, 2 * share : 2 * share + 3 * heads, :]), axis=2)
    log_rows = log_rows.reshape(peers, 3, heads)
    totals = jnp.sum(log_rows[:, 0] * pick[None, :], axis=1)
    totals = totals + jnp.sum(log_rows[:, 1] * pick[None, :], axis=1)
    totals = totals + jnp.sum(log_rows[:, 2] * pick[None, :], axis=1)
    dst = lax.broadcasted_iota(jnp.int32, (peers, peers, peers), 0)
    src = lax.broadcasted_iota(jnp.int32, (peers, peers, peers), 1)
    mid = lax.broadcasted_iota(jnp.int32, (peers, peers, peers), 2)
    between_fwd = (src < mid) & (mid < dst)
    between_bwd = (dst < mid) & (mid < src)
    log_fwd = jnp.sum(jnp.where(between_fwd, totals[None, None, :], 0.0), axis=2)
    log_bwd = jnp.sum(jnp.where(between_bwd, totals[None, None, :], 0.0), axis=2)
    dst2 = lax.broadcasted_iota(jnp.int32, (peers, peers), 0)
    src2 = lax.broadcasted_iota(jnp.int32, (peers, peers), 1)
    w_fwd = jnp.where(src2 < dst2, jnp.exp(jnp.where(src2 < dst2, log_fwd, 0.0)), 0.0)
    w_bwd = jnp.where(src2 > dst2, jnp.exp(jnp.where(src2 > dst2, log_bwd, 0.0)), 0.0)
    state_rows = split_left("di,irc->drc", w_fwd, got[:, :share])
    adjoint_rows = split_left("di,irc->drc", w_bwd, got[:, share : 2 * share])
    back = lax.all_to_all(
        jnp.concatenate([state_rows, adjoint_rows], axis=1).astype(jnp.bfloat16),
        axis,
        0,
        0,
        tiled=True,
    )
    start_state = widen(back[:, :share]).reshape(heads, width, width)
    start_adjoint = widen(back[:, share:]).reshape(heads, width, width)
    return start_state, start_adjoint, riders


def running_sum(decay_blk):
    length = decay_blk.shape[1]
    lower = (
        lax.broadcasted_iota(jnp.int32, (length, length), 1)
        <= lax.broadcasted_iota(jnp.int32, (length, length), 0)
    ).astype(decay_blk.dtype)
    return jnp.einsum("ts,nsh->nth", lower, decay_blk, preferred_element_type=jnp.float32)


def within_group(totals, pieces, reverse):
    blocks = totals.shape[0]
    at = lax.broadcasted_iota(jnp.int32, (blocks, blocks, blocks), 0)
    src = lax.broadcasted_iota(jnp.int32, (blocks, blocks, blocks), 1)
    mid = lax.broadcasted_iota(jnp.int32, (blocks, blocks, blocks), 2)
    between = ((at < mid) & (mid < src)) if reverse else ((src < mid) & (mid < at))
    logs = jnp.sum(jnp.where(between[..., None], totals[None, None], 0.0), axis=2)
    pos = lax.broadcasted_iota(jnp.int32, (blocks, blocks), 0)
    other = lax.broadcasted_iota(jnp.int32, (blocks, blocks), 1)
    earlier = (other > pos) if reverse else (other < pos)
    later = (other < pos) if reverse else (other > pos)
    weights = jnp.where(earlier[..., None], jnp.exp(jnp.where(earlier[..., None], logs, 0.0)), 0.0)
    seen_log = jnp.sum(jnp.where(earlier[..., None], totals[None], 0.0), axis=1)
    tail_log = jnp.sum(jnp.where(later[..., None], totals[None], 0.0), axis=1)
    seen = split_left("ijh,jhab->ihab", weights, pieces)
    whole = split_left("jh,jhab->hab", jnp.exp(tail_log), pieces)
    return seen, seen_log, whole, jnp.sum(totals, axis=0)


def local_block(queries, keys, values, out_grad, log_decay):
    length = queries.shape[0]
    heads = log_decay.shape[1]
    width = queries.shape[1] // heads
    query_blk = queries.reshape(length, heads, width)
    key_blk = keys.reshape(length, heads, width)
    value_blk = values.reshape(length, heads, width)
    grad_blk = out_grad.reshape(length, heads, width)
    cumul = running_sum(log_decay[None])[0]
    total = cumul[-1]
    after = jnp.exp(total[None, :] - cumul)
    before = jnp.exp(cumul)
    contrib = split_left("sha,shb->hab", after[..., None] * widen(key_blk), value_blk)
    update = split_left("tha,thb->hab", before[..., None] * widen(query_blk), grad_blk)
    return (query_blk, key_blk, value_blk, grad_blk, cumul, after, before, contrib, update)


def intra(query_blk, key_blk, value_blk, grad_blk, cumul):
    length = cumul.shape[0]
    heads_first = cumul.T
    spread = heads_first[:, :, None] - heads_first[:, None, :]
    causal = lax.broadcasted_iota(jnp.int32, (length, length), 1) <= lax.broadcasted_iota(
        jnp.int32, (length, length), 0
    )
    weights = jnp.where(causal[None], jnp.exp(jnp.where(causal[None], spread, 0.0)), 0.0)
    grad_scores = product("thd,shd->hts", grad_blk, value_blk)
    key_scores = product("thd,shd->hts", query_blk, key_blk)
    first = (weights * grad_scores).astype(jnp.bfloat16)
    second = (weights * key_scores).astype(jnp.bfloat16)
    query_part = product("hts,shd->htd", first, key_blk)
    key_part = product("hts,thd->hsd", first, query_blk)
    value_part = product("hts,thd->hsd", second, grad_blk)
    return query_part, key_part, value_part


def finish_kernel(
    grad_ref, value_ref, key_ref, state_ref, adjoint_ref, qp_ref, kp_ref, vp_ref, before_ref,
    after_ref, gq_ref, gk_ref, gv_ref,
):
    group, width = state_ref.shape[0], state_ref.shape[2]
    back = (((1,), (1,)), ((), ()))
    step = pl.program_id(0)
    lanes = lax.broadcasted_iota(jnp.int32, before_ref.shape, 1)
    before_all = before_ref[...]
    after_all = after_ref[...]
    for i in range(group):
        cols = slice(i * width, (i + 1) * width)
        head = step * group + i
        before = jnp.sum(jnp.where(lanes == head, before_all, 0.0), axis=1, keepdims=True)
        after = jnp.sum(jnp.where(lanes == head, after_all, 0.0), axis=1, keepdims=True)
        grad = grad_ref[:, cols]
        value = value_ref[:, cols]
        key = key_ref[:, cols]
        state = state_ref[i]
        adjoint = adjoint_ref[i]
        with_state = lax.dot_general(grad, state, back, preferred_element_type=jnp.float32)
        with_adjoint_v = lax.dot_general(value, adjoint, back, preferred_element_type=jnp.float32)
        with_adjoint_k = jnp.dot(key, adjoint, preferred_element_type=jnp.float32)
        gq_ref[:, cols] = (qp_ref[i] + before * with_state).astype(gq_ref.dtype)
        gk_ref[:, cols] = (kp_ref[i] + after * with_adjoint_v).astype(gk_ref.dtype)
        gv_ref[:, cols] = (vp_ref[i] + after * with_adjoint_k).astype(gv_ref.dtype)


def finish_call(out_grad, values, keys, state_in, adjoint_in, qp, kp, vp, before, after):
    length, columns = out_grad.shape
    heads, width = state_in.shape[0], state_in.shape[2]
    group = 16
    steps = heads // group
    flat_spec = pl.BlockSpec((length, group * width), lambda h: (0, h))
    head_spec = pl.BlockSpec((group, width, width), lambda h: (h, 0, 0))
    part_spec = pl.BlockSpec((group, length, width), lambda h: (h, 0, 0))
    scale_spec = pl.BlockSpec((length, heads), lambda h: (0, 0))
    out = jax.ShapeDtypeStruct((length, columns), jnp.bfloat16)
    return pl.pallas_call(
        finish_kernel,
        grid=(steps,),
        in_specs=[flat_spec, flat_spec, flat_spec, head_spec, head_spec, part_spec, part_spec,
                  part_spec, scale_spec, scale_spec],
        out_specs=[flat_spec, flat_spec, flat_spec],
        out_shape=[out, out, out],
    )(out_grad, values, keys, state_in, adjoint_in, qp, kp, vp, before, after)


def body(queries, keys, values, out_grad, log_decay):
    peers = lax.axis_size("exp")
    length = queries.shape[0]
    heads = log_decay.shape[1]
    width = queries.shape[1] // heads
    group = heads // peers
    (query_blk, key_blk, value_blk, grad_blk, cumul, after, before, contrib, update) = local_block(
        queries, keys, values, out_grad, log_decay
    )
    share = group * width
    decay_rows = jnp.transpose(log_decay.reshape(length, peers, group), (1, 2, 0))
    pad_rows = 16
    decay_rows = jnp.pad(decay_rows, ((0, 0), (0, pad_rows - group), (0, 0)))
    packed = jnp.concatenate(
        [
            contrib.astype(jnp.bfloat16).reshape(peers, share, width),
            update.astype(jnp.bfloat16).reshape(peers, share, width),
            decay_rows.astype(jnp.bfloat16),
        ],
        axis=1,
    )
    got = lax.all_to_all(packed, "exp", 0, 0, tiled=True)
    contrib_g = got[:, :share].reshape(peers, group, width, width)
    update_g = got[:, share : 2 * share].reshape(peers, group, width, width)
    totals = jnp.sum(widen(got[:, 2 * share : 2 * share + group]), axis=2)
    query_part, key_part, value_part = intra(query_blk, key_blk, value_blk, grad_blk, cumul)
    totals, contrib_g, update_g, query_part, key_part, value_part = lax.optimization_barrier(
        (totals, contrib_g, update_g, query_part, key_part, value_part)
    )
    prefix, prefix_log, dev_state, dev_log = within_group(totals, contrib_g, False)
    suffix, suffix_log, dev_adjoint, unused = within_group(totals, update_g, True)
    start_state, start_adjoint, (prefix, suffix) = carried_both(
        dev_log, dev_state, dev_adjoint, "seq", (prefix, suffix)
    )
    state_prev = jnp.exp(prefix_log)[:, :, None, None] * start_state[None] + prefix
    adjoint = jnp.exp(suffix_log)[:, :, None, None] * start_adjoint[None] + suffix
    returned = jnp.concatenate(
        [
            state_prev.astype(jnp.bfloat16).reshape(peers, share, width),
            adjoint.astype(jnp.bfloat16).reshape(peers, share, width),
        ],
        axis=1,
    )
    back = lax.all_to_all(returned, "exp", 0, 0, tiled=True)
    state_in = back[:, :share].reshape(heads, width, width)
    adjoint_in = back[:, share:].reshape(heads, width, width)
    grad_query, grad_key, grad_value = finish_call(
        out_grad, values, keys, state_in, adjoint_in, query_part, key_part, value_part,
        before, after,
    )
    return (grad_query, grad_key, grad_value)


def solution(mesh):
    placed = tuple(P(SEQ_EXP, None) for _ in range(5))
    return jax.shard_map(
        body,
        mesh=mesh,
        in_specs=placed,
        out_specs=(P(SEQ_EXP, None), P(SEQ_EXP, None), P(SEQ_EXP, None)),
        check_vma=False,
    )
```
